32 devices in a mesh: groups: 2 (over y), tgt: 4 (over z), inner: 2 (over x), sub: 2 (over core).
Axes of the slice: x: 2, y: 2, z: 4, core: 2. Of those that a mesh axis runs over, the one named last changes fastest.
Arguments:
- density: bfloat16 [4096, 1024], P(('tgt', 'inner', 'sub'), 'groups'), parts along dimension 1, may hold values from -6 to 6
- cluster_basis: bfloat16 [32, 32, 256], P(('groups', 'tgt', 'inner', 'sub')), parts along dimension 0, may hold values from -0.375 to 0.375
- near_blocks: bfloat16 [8, 4, 8, 256, 256], P(('groups', 'tgt'), ('inner', 'sub')), parts along dimension 0, may hold values from -0.25 to 0.25
- near_pairs: int32 [8, 4, 8, 2], P(('groups', 'tgt'), ('inner', 'sub')), parts along dimension 0, may hold values from 0 to 3, as said below
- near_count: int32 [8, 4], P(('groups', 'tgt'), ('inner', 'sub')), parts along dimension 0, may hold values from 4 to 8, as said below
- coupling: bfloat16 [8, 4, 128, 128], P(('groups', 'tgt'), ('inner', 'sub')), parts along dimension 0, may hold values from -0.5 to 0.5
Outputs:
- potential: bfloat16 [4096, 1024], P(('tgt', 'inner', 'sub'), 'groups'), parts along dimension 1
The draws below stay inside these ranges and needn't reach their ends.
There are 2 independent parts, one for each index of `groups`. The reference program is written for one: setup_inputs(seed, part) draws one part's arguments, and reference() takes and returns one part's arrays. A program takes and returns all parts, laid end to end along the dimension named above; each array names one. Nothing has to cross between parts.
Inputs may be any that keep to these rules, and one draw needn't show every extreme that they name: `near_pairs`: within one device's slots the pairs are distinct; the first column is below 4, the second below 4. Only the first near_count slots of a device are live; some device is full in every draw.
All inputs are finite; a program needn't handle non-finite values.
Results may differ from the reference program's by a relative error of at most 0.015.
Values may be sent and summed in bfloat16 or wider, within the bound.
No kernel may reach another device: no remote copies, remote signals or barrier semaphores. Data moves between devices by JAX's collectives and lax.ppermute only.
A program may use at most 64 MiB of HBM per device.

```python
import jax
import jax.numpy as jnp
from jax import lax

B = 256
RANK = 32
NRHS = 512
NIS = 4
NCL = 16
NEAR_DEV = 8
PANELS = 4096
N_TGT = 4


def draw_near_pairs(key, part):
    subkeys = jax.random.split(key, N_TGT * NIS)

    def choose(subkey):
        chosen = jax.random.permutation(subkey, NIS * N_TGT)[:NEAR_DEV]
        return jnp.stack([chosen // N_TGT, chosen % N_TGT], axis=1)
    return jax.vmap(choose)(subkeys).reshape(N_TGT, NIS, NEAR_DEV, 2).astype(jnp.int32)


def draw_near_count(key, part):
    key_count, key_full = jax.random.split(key)
    counts = jax.random.randint(key_count, (N_TGT * NIS,), NEAR_DEV // 2, NEAR_DEV + 1)
    full_device = jax.random.randint(key_full, (), 0, N_TGT * NIS)
    counts = jnp.where(jnp.arange(N_TGT * NIS) == full_device, NEAR_DEV, counts)
    return counts.reshape(N_TGT, NIS).astype(jnp.int32)


def block_levels(rng, dims, cuts, smallest, high):
    level = 1.0
    for position, shards_of in cuts:
        draws = jax.random.uniform(jax.random.fold_in(jax.random.fold_in(rng, 6), position), (shards_of,), jnp.float32, smallest / len(cuts), high / len(cuts))
        level = level * jnp.repeat(jnp.exp(draws), dims[position] // shards_of).reshape((-1,) + (1,) * (len(dims) - 1 - position))
    return level


def normal_values(key, dims, deviation, reach, cuts=(), kind=jnp.bfloat16):
    array = jax.random.normal(key, dims, jnp.float32) * deviation
    if len(cuts) > 0:
        array = block_levels(key, dims, cuts, -0.22, 0.18) * array
    return jnp.clip(array, min=-reach, max=reach).astype(kind)


def setup_inputs(seed: int = 0, part: int = 0) -> dict:
    arg_keys = jax.random.split(jax.random.key(seed), 7)
    part_keys = jax.random.split(jax.random.fold_in(arg_keys[6], part), 7)
    density = normal_values(part_keys[0], (PANELS, NRHS), 1.0, 6.0, ((0, 16),))
    cluster_basis = normal_values(part_keys[1], (NCL, RANK, B), B ** -0.5, 0.375, ((0, 16),))
    near_blocks = normal_values(part_keys[2], (N_TGT, NIS, NEAR_DEV, B, B), (2 * B) ** -0.5, 0.25, ((0, 4), (1, 4)))
    near_pairs = draw_near_pairs(jax.random.fold_in(jax.random.fold_in(arg_keys[6], part), 71), part)
    near_count = draw_near_count(jax.random.fold_in(jax.random.fold_in(arg_keys[6], part), 71), part)
    coupling = normal_values(part_keys[5], (N_TGT, NIS, NIS * RANK, N_TGT * RANK), (N_TGT * RANK) ** -0.5, 0.5, ((0, 4), (1, 4)))
    return {"density": density, "cluster_basis": cluster_basis, "near_blocks": near_blocks, "near_pairs": near_pairs, "near_count": near_count, "coupling": coupling}


def reference(density, cluster_basis, near_blocks, near_pairs, near_count, coupling):
    clusters = density.reshape(N_TGT, NIS, B, NRHS)
    basis_rows = cluster_basis.reshape(N_TGT, NIS, RANK, B)
    projected = jnp.einsum("tirb,tibn->tirn", basis_rows.astype(jnp.float32), clusters.astype(jnp.float32)).astype(jnp.bfloat16)

    def one_device(near_total, device_index):
        tgt_index = device_index // NIS
        inner_index = device_index % NIS
        sources = lax.dynamic_index_in_dim(clusters, inner_index, 1, False)
        pair_list = near_pairs[tgt_index, inner_index]
        live_count = near_count[tgt_index, inner_index]
        tiles = near_blocks[tgt_index, inner_index]
        pieces = sources[pair_list[:, 1]]
        terms = jnp.einsum("kab,kbn->kan", tiles.astype(jnp.float32), pieces.astype(jnp.float32))
        weight = (jnp.arange(NEAR_DEV) < live_count).astype(jnp.float32)
        onehot = (pair_list[:, 0][:, None] == jnp.arange(NIS)[None, :]).astype(jnp.float32) * weight[:, None]
        partial_value = jnp.einsum("ka,kbn->abn", onehot, terms).astype(jnp.bfloat16).astype(jnp.float32)
        target_rows = lax.dynamic_index_in_dim(near_total, tgt_index, 0, False)
        return lax.dynamic_update_index_in_dim(near_total, target_rows + partial_value, tgt_index, 0), None

    near_total, _ = lax.scan(one_device, jnp.zeros((N_TGT, NIS, B, NRHS), jnp.float32), jnp.arange(N_TGT * NIS, dtype=jnp.int32))

    flat_pairs = near_pairs[..., 0] * N_TGT + near_pairs[..., 1]
    live = jnp.arange(NEAR_DEV)[None, None, :] < near_count[:, :, None]
    hits = (flat_pairs[..., None] == jnp.arange(NIS * N_TGT)[None, None, None, :]) & live[..., None]
    keep_mask = 1.0 - jnp.any(hits, axis=2).astype(jnp.float32)
    keep_mask = keep_mask.reshape(N_TGT, NIS, NIS, 1, N_TGT, 1).astype(jnp.bfloat16)
    masked = coupling.reshape(N_TGT, NIS, NIS, RANK, N_TGT, RANK) * keep_mask
    coeffs = jnp.einsum("tiaxsr,sirn->taxn", masked.astype(jnp.float32), projected.astype(jnp.float32))
    coeffs = coeffs.reshape(N_TGT, NIS, RANK, NRHS).astype(jnp.bfloat16)
    far_rows = jnp.einsum("tirb,tirn->tibn", basis_rows.astype(jnp.float32), coeffs.astype(jnp.float32))
    return (near_total + far_rows).astype(jnp.bfloat16).reshape(PANELS, NRHS)
```

```python
import jax
import jax.numpy as jnp
from jax import lax
from jax.experimental import pallas as pl
from jax.experimental.pallas import tpu as pltpu
from jax.sharding import PartitionSpec as P


def _near_far_kernel(pairs_ref, count_ref, tiles_ref, gathered_ref, masked_ref, out_ref, acc_ref):
    slot = pl.program_id(0)
    slot_total = pl.num_programs(0)
    inner_count, width, _ = acc_ref.shape
    tgt_count = gathered_ref.shape[0]
    rank_size = gathered_ref.shape[1] - width

    @pl.when(slot == 0)
    def _():
        acc_ref[...] = jnp.zeros_like(acc_ref)

    @pl.when(slot < count_ref[0])
    def _():
        target = jnp.clip(pairs_ref[2 * slot], 0, inner_count - 1)
        source = jnp.clip(pairs_ref[2 * slot + 1], 0, tgt_count - 1)
        term = jnp.dot(
            tiles_ref[...], gathered_ref[source, :width, :], preferred_element_type=jnp.float32
        )
        acc_ref[target] += term

    @pl.when(slot == slot_total - 1)
    def _():
        out_ref[:, :width, :] = acc_ref[...].astype(out_ref.dtype)
        coeffs = jnp.zeros((inner_count * rank_size, out_ref.shape[2]), jnp.float32)
        for source in range(tgt_count):
            coeffs += jnp.dot(
                masked_ref[source],
                gathered_ref[source, width:, :],
                preferred_element_type=jnp.float32,
            )
        out_ref[:, width:, :] = coeffs.reshape(inner_count, rank_size, -1).astype(out_ref.dtype)


def _near_far(pairs_flat, count, tiles, gathered, masked_t, inner_count):
    slot_count, width, _ = tiles.shape
    tgt_count, rows, rhs_count = gathered.shape

    def tile_index(k, pairs, cnt):
        return (jnp.maximum(jnp.minimum(k, cnt[0] - 1), 0), 0, 0)

    grid_spec = pltpu.PrefetchScalarGridSpec(
        num_scalar_prefetch=2,
        grid=(slot_count,),
        in_specs=[
            pl.BlockSpec((None, width, width), tile_index),
            pl.BlockSpec((tgt_count, rows, rhs_count), lambda k, p, c: (0, 0, 0)),
            pl.BlockSpec(masked_t.shape, lambda k, p, c: (0, 0, 0)),
        ],
        out_specs=pl.BlockSpec((inner_count, rows, rhs_count), lambda k, p, c: (0, 0, 0)),
        scratch_shapes=[pltpu.VMEM((inner_count, width, rhs_count), jnp.float32)],
    )
    return pl.pallas_call(
        _near_far_kernel,
        grid_spec=grid_spec,
        out_shape=jax.ShapeDtypeStruct((inner_count, rows, rhs_count), jnp.bfloat16),
        compiler_params=pltpu.CompilerParams(
            dimension_semantics=("arbitrary",), vmem_limit_bytes=100 * 1024 * 1024 // 2
        ),
    )(pairs_flat, count, tiles, gathered, masked_t)


def _epilogue_kernel(reduced_ref, basis_ref, out_ref):
    width = out_ref.shape[0]
    near = reduced_ref[0, :width, :].astype(jnp.float32)
    coeffs = reduced_ref[0, width:, :]
    far = lax.dot_general(
        basis_ref[0], coeffs, (((0,), (0,)), ((), ())), preferred_element_type=jnp.float32
    )
    out_ref[...] = (near + far).astype(out_ref.dtype)


def _epilogue(reduced, basis):
    width = basis.shape[2]
    return pl.pallas_call(
        _epilogue_kernel,
        out_shape=jax.ShapeDtypeStruct((width, reduced.shape[2]), jnp.bfloat16),
    )(reduced, basis)


def on_device(density, cluster_basis, near_blocks, near_pairs, near_count, coupling):
    width = cluster_basis.shape[2]
    rank_size = cluster_basis.shape[1]
    tgt_count = lax.axis_size("tgt")
    inner_count = lax.axis_size(("inner", "sub"))
    own_projected = jnp.dot(
        cluster_basis[0], density, preferred_element_type=jnp.float32
    ).astype(jnp.bfloat16)
    send = jnp.concatenate([density, own_projected], axis=0)
    gathered = lax.all_gather(send, "tgt", axis=0, tiled=False)

    pair_list = near_pairs[0, 0]
    live_count = near_count[0, 0]
    slot_count = pair_list.shape[0]
    flat_pairs = pair_list[:, 0] * tgt_count + pair_list[:, 1]
    live_slots = jnp.arange(slot_count) < live_count
    hit_table = (flat_pairs[:, None] == jnp.arange(inner_count * tgt_count)[None, :]) & live_slots[
        :, None
    ]
    keep_mask = (
        (1.0 - jnp.any(hit_table, axis=0).astype(jnp.float32))
        .reshape(inner_count, 1, tgt_count, 1)
        .astype(jnp.bfloat16)
    )
    masked = coupling[0, 0].reshape(inner_count, rank_size, tgt_count, rank_size) * keep_mask
    masked_t = masked.transpose(2, 0, 1, 3).reshape(tgt_count, inner_count * rank_size, rank_size)

    partial = _near_far(
        pair_list.reshape(-1), live_count.reshape(1), near_blocks[0, 0], gathered, masked_t,
        inner_count,
    )
    reduced = lax.psum_scatter(partial, ("inner", "sub"), scatter_dimension=0, tiled=True)
    return _epilogue(reduced, cluster_basis)


def solution(mesh):
    in_specs = (
        P(("tgt", "inner", "sub"), "groups"),
        P(("groups", "tgt", "inner", "sub"), None, None),
        P(("groups", "tgt"), ("inner", "sub"), None, None, None),
        P(("groups", "tgt"), ("inner", "sub"), None, None),
        P(("groups", "tgt"), ("inner", "sub")),
        P(("groups", "tgt"), ("inner", "sub"), None, None),
    )
    out_specs = P(("tgt", "inner", "sub"), "groups")
    return jax.shard_map(
        on_device, mesh=mesh, in_specs=in_specs, out_specs=out_specs, check_vma=False
    )
```

```python
import jax
import jax.numpy as jnp
from jax import lax
from jax.experimental import pallas as pl
from jax.experimental.pallas import tpu as pltpu
from jax.sharding import PartitionSpec as P


def _near_far_kernel(
    pairs_ref, count_ref, place_ref, tiles_ref, stack_ref, masked_ref, mine_ref, theirs_ref, acc_ref
):
    slot = pl.program_id(0)
    slot_total = pl.num_programs(0)
    inner_count, width, rhs_count = acc_ref.shape
    tgt_count = masked_ref.shape[0]
    rank_size = masked_ref.shape[2]
    half_rank = rank_size // 2
    sub_count = 2
    own_tgt = place_ref[0]
    own_sub = place_ref[1]

    @pl.when(slot == 0)
    def _():
        acc_ref[...] = jnp.zeros_like(acc_ref)

    @pl.when(slot < count_ref[0])
    def _():
        target = jnp.clip(pairs_ref[2 * slot], 0, inner_count - 1)
        source = jnp.clip(pairs_ref[2 * slot + 1], 0, tgt_count - 1)
        term = jnp.dot(
            tiles_ref[...],
            stack_ref[source - own_tgt + tgt_count - 1, :width, :],
            preferred_element_type=jnp.float32,
        )
        acc_ref[target] += term

    @pl.when(slot == slot_total - 1)
    def _():
        coeffs = jnp.zeros((inner_count * rank_size, rhs_count), jnp.float32)
        for source in range(tgt_count):
            block = stack_ref[source - own_tgt + tgt_count - 1]
            dens = block[:width, :]
            packed = block[width:, :]
            top = jnp.dot(packed[:, :width], dens, preferred_element_type=jnp.float32)
            bottom = jnp.dot(packed[:, width:], dens, preferred_element_type=jnp.float32)
            projected = jnp.concatenate([top, bottom], axis=0).astype(jnp.bfloat16)
            coeffs += jnp.dot(masked_ref[source], projected, preferred_element_type=jnp.float32)
        coeffs = coeffs.astype(jnp.bfloat16)

        def write(first_ref, second_ref):
            for target in range(inner_count):
                dest = first_ref if target % sub_count == 0 else second_ref
                row = target // sub_count
                dest[row, :width, :] = acc_ref[target].astype(dest.dtype)
                dest[row, width:, :] = coeffs[target * rank_size : (target + 1) * rank_size]

        @pl.when(own_sub == 0)
        def _():
            write(mine_ref, theirs_ref)

        @pl.when(own_sub != 0)
        def _():
            write(theirs_ref, mine_ref)


def _near_far(pairs_flat, count, place, tiles, stack, masked_t, inner_count, rank_size):
    slot_count, width, _ = tiles.shape
    stack_count, rows, rhs_count = stack.shape
    half_count = inner_count // 2
    out_rows = width + rank_size

    def tile_index(k, pairs, cnt, place):
        return (jnp.maximum(jnp.minimum(k, cnt[0] - 1), 0), 0, 0)

    whole = lambda k, p, c, q: (0, 0, 0)
    grid_spec = pltpu.PrefetchScalarGridSpec(
        num_scalar_prefetch=3,
        grid=(slot_count,),
        in_specs=[
            pl.BlockSpec((None, width, width), tile_index),
            pl.BlockSpec(stack.shape, whole),
            pl.BlockSpec(masked_t.shape, whole),
        ],
        out_specs=[
            pl.BlockSpec((half_count, out_rows, rhs_count), whole),
            pl.BlockSpec((half_count, out_rows, rhs_count), whole),
        ],
        scratch_shapes=[pltpu.VMEM((inner_count, width, rhs_count), jnp.float32)],
    )
    out = jax.ShapeDtypeStruct((half_count, out_rows, rhs_count), jnp.bfloat16)
    return pl.pallas_call(
        _near_far_kernel,
        grid_spec=grid_spec,
        out_shape=[out, out],
        compiler_params=pltpu.CompilerParams(
            dimension_semantics=("arbitrary",), vmem_limit_bytes=56 * 1024 * 1024
        ),
    )(pairs_flat, count, place, tiles, stack, masked_t)


def _epilogue_kernel(total_ref, basis_ref, out_ref):
    width = out_ref.shape[0]
    near = total_ref[:width, :]
    coeffs = total_ref[width:, :].astype(jnp.bfloat16)
    far = lax.dot_general(
        basis_ref[0], coeffs, (((0,), (0,)), ((), ())), preferred_element_type=jnp.float32
    )
    out_ref[...] = (near + far).astype(out_ref.dtype)


def _epilogue(total, basis):
    width = basis.shape[2]
    return pl.pallas_call(
        _epilogue_kernel,
        out_shape=jax.ShapeDtypeStruct((width, total.shape[1]), jnp.bfloat16),
    )(total, basis)


def _line_gather(payload, axis):
    n = lax.axis_size(axis)
    up_pairs = [(i, i + 1) for i in range(n - 1)]
    down_pairs = [(i + 1, i) for i in range(n - 1)]
    ups, downs = [], []
    up, down = payload, payload
    for _ in range(n - 1):
        up = lax.ppermute(up, axis, up_pairs)
        down = lax.ppermute(down, axis, down_pairs)
        ups.append(up)
        downs.append(down)
    return jnp.stack(ups[::-1] + [payload] + downs)


def _ring_reduce_scatter(blocks, axis):
    n = lax.axis_size(axis)
    if n == 1:
        return blocks[0]
    me = lax.axis_index(axis)
    ring = [(i, (i + 1) % n) for i in range(n)]
    carry = lax.dynamic_index_in_dim(blocks, jnp.mod(me - 1, n), 0, False)
    for step in range(n - 1):
        arrived = lax.ppermute(carry.astype(jnp.bfloat16), axis, ring)
        own = lax.dynamic_index_in_dim(blocks, jnp.mod(me - 2 - step, n), 0, False)
        carry = arrived.astype(jnp.float32) + own
    return carry


def on_device(density, cluster_basis, near_blocks, near_pairs, near_count, coupling):
    width = cluster_basis.shape[2]
    rank_size = cluster_basis.shape[1]
    rhs_count = density.shape[1]
    tgt_count = lax.axis_size("tgt")
    inner_count = lax.axis_size(("inner", "sub"))
    assert lax.axis_size("sub") == 2 and 2 * width == rhs_count and rank_size % 2 == 0
    basis = cluster_basis[0]
    half_rank = rank_size // 2
    packed = jnp.concatenate([basis[:half_rank], basis[half_rank:]], axis=1)
    payload = jnp.concatenate([density, packed], axis=0)
    stack = _line_gather(payload, "tgt")

    pair_list = near_pairs[0, 0]
    live_count = near_count[0, 0]
    slot_count = pair_list.shape[0]
    flat_pairs = pair_list[:, 0] * tgt_count + pair_list[:, 1]
    live_slots = jnp.arange(slot_count) < live_count
    hit_table = (flat_pairs[:, None] == jnp.arange(inner_count * tgt_count)[None, :]) & live_slots[
        :, None
    ]
    keep_mask = (
        (1.0 - jnp.any(hit_table, axis=0).astype(jnp.float32))
        .reshape(inner_count, 1, tgt_count, 1)
        .astype(jnp.bfloat16)
    )
    masked = coupling[0, 0].reshape(inner_count, rank_size, tgt_count, rank_size) * keep_mask
    masked_t = masked.transpose(2, 0, 1, 3).reshape(tgt_count, inner_count * rank_size, rank_size)

    place = jnp.stack([lax.axis_index("tgt"), lax.axis_index("sub")]).astype(jnp.int32)
    mine, theirs = _near_far(
        pair_list.reshape(-1), live_count.reshape(1), place, near_blocks[0, 0], stack, masked_t,
        inner_count, rank_size,
    )
    arrived = lax.ppermute(theirs, "sub", [(0, 1), (1, 0)])
    stage = mine.astype(jnp.float32) + arrived.astype(jnp.float32)
    total = _ring_reduce_scatter(stage, "inner")
    return _epilogue(total, cluster_basis)


def solution(mesh):
    in_specs = (
        P(("tgt", "inner", "sub"), "groups"),
        P(("groups", "tgt", "inner", "sub"), None, None),
        P(("groups", "tgt"), ("inner", "sub"), None, None, None),
        P(("groups", "tgt"), ("inner", "sub"), None, None),
        P(("groups", "tgt"), ("inner", "sub")),
        P(("groups", "tgt"), ("inner", "sub"), None, None),
    )
    out_specs = P(("tgt", "inner", "sub"), "groups")
    return jax.shard_map(
        on_device, mesh=mesh, in_specs=in_specs, out_specs=out_specs, check_vma=False
    )
```

```python
import jax
import jax.numpy as jnp
from jax import lax
from jax.experimental import pallas as pl
from jax.experimental.pallas import tpu as pltpu
from jax.sharding import PartitionSpec as P


def _near_far_kernel(
    pairs_ref,
    count_ref,
    place_ref,
    tiles_ref,
    stack_ref,
    basis_ref,
    masked_ref,
    mine_ref,
    theirs_ref,
    acc_ref,
):
    slot = pl.program_id(0)
    slot_total = pl.num_programs(0)
    inner_count, width, rhs_count = acc_ref.shape
    tgt_count = masked_ref.shape[0]
    rank_size = masked_ref.shape[2]
    sub_count = 2
    own_tgt = place_ref[0]
    own_sub = place_ref[1]

    @pl.when(slot == 0)
    def _():
        acc_ref[...] = jnp.zeros_like(acc_ref)

    @pl.when(slot < count_ref[0])
    def _():
        target = jnp.clip(pairs_ref[2 * slot], 0, inner_count - 1)
        source = jnp.clip(pairs_ref[2 * slot + 1], 0, tgt_count - 1)
        term = jnp.dot(
            tiles_ref[...],
            stack_ref[source - own_tgt + tgt_count - 1, :width, :],
            preferred_element_type=jnp.float32,
        )
        acc_ref[target] += term

    @pl.when(slot == slot_total - 1)
    def _():
        coeffs = jnp.zeros((inner_count * rank_size, rhs_count), jnp.float32)
        for source in range(tgt_count):
            offset = source - own_tgt + tgt_count - 1
            projected = jnp.dot(
                basis_ref[offset], stack_ref[offset, :width, :], preferred_element_type=jnp.float32
            ).astype(jnp.bfloat16)
            coeffs += jnp.dot(masked_ref[source], projected, preferred_element_type=jnp.float32)
        coeffs = coeffs.astype(jnp.bfloat16)

        def write(first_ref, second_ref):
            for target in range(inner_count):
                dest = first_ref if target % sub_count == 0 else second_ref
                row = target // sub_count
                dest[row, :width, :] = acc_ref[target].astype(dest.dtype)
                dest[row, width:, :] = coeffs[target * rank_size : (target + 1) * rank_size]

        @pl.when(own_sub == 0)
        def _():
            write(mine_ref, theirs_ref)

        @pl.when(own_sub != 0)
        def _():
            write(theirs_ref, mine_ref)


def _near_far(pairs_flat, count, place, tiles, stack, basis_stack, masked_t, inner_count, rank_size):
    slot_count, width, _ = tiles.shape
    stack_count, rows, rhs_count = stack.shape
    half_count = inner_count // 2
    out_rows = width + rank_size

    def tile_index(k, pairs, cnt, place):
        return (jnp.maximum(jnp.minimum(k, cnt[0] - 1), 0), 0, 0)

    whole = lambda k, p, c, q: (0, 0, 0)
    grid_spec = pltpu.PrefetchScalarGridSpec(
        num_scalar_prefetch=3,
        grid=(slot_count,),
        in_specs=[
            pl.BlockSpec((None, width, width), tile_index),
            pl.BlockSpec(stack.shape, whole),
            pl.BlockSpec(basis_stack.shape, whole),
            pl.BlockSpec(masked_t.shape, whole),
        ],
        out_specs=[
            pl.BlockSpec((half_count, out_rows, rhs_count), whole),
            pl.BlockSpec((half_count, out_rows, rhs_count), whole),
        ],
        scratch_shapes=[pltpu.VMEM((inner_count, width, rhs_count), jnp.float32)],
    )
    out = jax.ShapeDtypeStruct((half_count, out_rows, rhs_count), jnp.bfloat16)
    return pl.pallas_call(
        _near_far_kernel,
        grid_spec=grid_spec,
        out_shape=[out, out],
        compiler_params=pltpu.CompilerParams(
            dimension_semantics=("arbitrary",), vmem_limit_bytes=56 * 1024 * 1024
        ),
    )(pairs_flat, count, place, tiles, stack, basis_stack, masked_t)


def _epilogue_kernel(*refs):
    basis_ref, total_refs, out_ref = refs[0], refs[1:-1], refs[-1]
    width = out_ref.shape[0]
    for index, total_ref in enumerate(total_refs):
        cols = total_ref.shape[1]
        near = total_ref[:width, :]
        coeffs = total_ref[width:, :].astype(jnp.bfloat16)
        far = lax.dot_general(
            basis_ref[0], coeffs, (((0,), (0,)), ((), ())), preferred_element_type=jnp.float32
        )
        out_ref[:, index * cols : (index + 1) * cols] = (near + far).astype(out_ref.dtype)


def _epilogue(totals, basis):
    width = basis.shape[2]
    cols = sum(total.shape[1] for total in totals)
    return pl.pallas_call(
        _epilogue_kernel,
        out_shape=jax.ShapeDtypeStruct((width, cols), jnp.bfloat16),
    )(basis, *totals)


def _line_gather(payload, axis, ties=()):
    n = lax.axis_size(axis)
    up_pairs = [(i, i + 1) for i in range(n - 1)]
    down_pairs = [(i + 1, i) for i in range(n - 1)]
    ups, downs = [], []
    up, down = payload, payload
    for step in range(n - 1):
        if step < len(ties) and ties[step]:
            up, down = lax.optimization_barrier((up, down) + tuple(ties[step]))[:2]
        up = lax.ppermute(up, axis, up_pairs)
        down = lax.ppermute(down, axis, down_pairs)
        ups.append(up)
        downs.append(down)
    return jnp.stack(ups[::-1] + [payload] + downs), (up, down)


def _ring_reduce_scatter(blocks, axis):
    n = lax.axis_size(axis)
    if n == 1:
        return blocks[0]
    me = lax.axis_index(axis)
    ring = [(i, (i + 1) % n) for i in range(n)]
    carry = lax.dynamic_index_in_dim(blocks, jnp.mod(me - 1, n), 0, False)
    for step in range(n - 1):
        arrived = lax.ppermute(carry.astype(jnp.bfloat16), axis, ring)
        own = lax.dynamic_index_in_dim(blocks, jnp.mod(me - 2 - step, n), 0, False)
        carry = arrived.astype(jnp.float32) + own
    return carry


def on_device(density, cluster_basis, near_blocks, near_pairs, near_count, coupling):
    width = cluster_basis.shape[2]
    rank_size = cluster_basis.shape[1]
    rhs_count = density.shape[1]
    tgt_count = lax.axis_size("tgt")
    inner_count = lax.axis_size(("inner", "sub"))
    assert lax.axis_size("sub") == 2 and 2 * width == rhs_count
    basis = cluster_basis[0]
    chunk_count = 2
    cols = rhs_count // chunk_count

    pair_list = near_pairs[0, 0]
    live_count = near_count[0, 0]
    slot_count = pair_list.shape[0]
    flat_pairs = pair_list[:, 0] * tgt_count + pair_list[:, 1]
    live_slots = jnp.arange(slot_count) < live_count
    hit_table = (flat_pairs[:, None] == jnp.arange(inner_count * tgt_count)[None, :]) & live_slots[
        :, None
    ]
    keep_mask = (
        (1.0 - jnp.any(hit_table, axis=0).astype(jnp.float32))
        .reshape(inner_count, 1, tgt_count, 1)
        .astype(jnp.bfloat16)
    )
    masked = coupling[0, 0].reshape(inner_count, rank_size, tgt_count, rank_size) * keep_mask
    masked_t = masked.transpose(2, 0, 1, 3).reshape(tgt_count, inner_count * rank_size, rank_size)
    place = jnp.stack([lax.axis_index("tgt"), lax.axis_index("sub")]).astype(jnp.int32)

    totals = []
    basis_stack = None
    previous = None
    for chunk in range(chunk_count):
        piece = density[:, chunk * cols : (chunk + 1) * cols]
        if chunk == 0:
            stack, last_round = _line_gather(jnp.concatenate([piece, basis], axis=0), "tgt")
            basis_stack = stack[:, width:, :]
        else:
            ties = (previous[0], previous[1], previous[2])
            stack, last_round = _line_gather(piece, "tgt", ties)
            stack = lax.optimization_barrier((stack, previous[3]))[0]
        mine, theirs = _near_far(
            pair_list.reshape(-1), live_count.reshape(1), place, near_blocks[0, 0], stack,
            basis_stack, masked_t, inner_count, rank_size,
        )
        arrived = lax.ppermute(theirs, "sub", [(0, 1), (1, 0)])
        stage = mine.astype(jnp.float32) + arrived.astype(jnp.float32)
        totals.append(_ring_reduce_scatter(stage, "inner"))
        previous = (tuple(last_round), (mine, theirs), (stage,), totals[-1])
    return _epilogue(totals, cluster_basis)


def solution(mesh):
    in_specs = (
        P(("tgt", "inner", "sub"), "groups"),
        P(("groups", "tgt", "inner", "sub"), None, None),
        P(("groups", "tgt"), ("inner", "sub"), None, None, None),
        P(("groups", "tgt"), ("inner", "sub"), None, None),
        P(("groups", "tgt"), ("inner", "sub")),
        P(("groups", "tgt"), ("inner", "sub"), None, None),
    )
    out_specs = P(("tgt", "inner", "sub"), "groups")
    return jax.shard_map(
        on_device, mesh=mesh, in_specs=in_specs, out_specs=out_specs, check_vma=False
    )
```

```python
import jax
import jax.numpy as jnp
from jax import lax
from jax.experimental import pallas as pl
from jax.experimental.pallas import tpu as pltpu
from jax.sharding import PartitionSpec as P


def _near_far_kernel(
    pairs_ref, count_ref, place_ref, tiles_ref, stack_ref, masked_ref, mine_ref, theirs_ref, acc_ref
):
    slot = pl.program_id(0)
    slot_total = pl.num_programs(0)
    inner_count, width, rhs_count = acc_ref.shape
    tgt_count = masked_ref.shape[0]
    rank_size = masked_ref.shape[2]
    half_rank = rank_size // 2
    sub_count = 2
    own_tgt = place_ref[0]
    own_sub = place_ref[1]

    @pl.when(slot == 0)
    def _():
        acc_ref[...] = jnp.zeros_like(acc_ref)

    @pl.when(slot < count_ref[0])
    def _():
        target = jnp.clip(pairs_ref[2 * slot], 0, inner_count - 1)
        source = jnp.clip(pairs_ref[2 * slot + 1], 0, tgt_count - 1)
        term = jnp.dot(
            tiles_ref[...],
            stack_ref[source - own_tgt + tgt_count - 1, :width, :],
            preferred_element_type=jnp.float32,
        )
        acc_ref[target] += term

    @pl.when(slot == slot_total - 1)
    def _():
        coeffs = jnp.zeros((inner_count * rank_size, rhs_count), jnp.float32)
        for source in range(tgt_count):
            block = stack_ref[source - own_tgt + tgt_count - 1]
            dens = block[:width, :]
            packed = block[width:, :]
            top = jnp.dot(packed[:, :width], dens, preferred_element_type=jnp.float32)
            bottom = jnp.dot(packed[:, width:], dens, preferred_element_type=jnp.float32)
            projected = jnp.concatenate([top, bottom], axis=0).astype(jnp.bfloat16)
            coeffs += jnp.dot(masked_ref[source], projected, preferred_element_type=jnp.float32)
        coeffs = coeffs.astype(jnp.bfloat16)

        def write(first_ref, second_ref):
            for target in range(inner_count):
                dest = first_ref if target % sub_count == 0 else second_ref
                row = target // sub_count
                dest[row, :width, :] = acc_ref[target].astype(dest.dtype)
                dest[row, width:, :] = coeffs[target * rank_size : (target + 1) * rank_size]

        @pl.when(own_sub == 0)
        def _():
            write(mine_ref, theirs_ref)

        @pl.when(own_sub != 0)
        def _():
            write(theirs_ref, mine_ref)


def _near_far(pairs_flat, count, place, tiles, stack, masked_t, inner_count, rank_size):
    slot_count, width, _ = tiles.shape
    stack_count, rows, rhs_count = stack.shape
    half_count = inner_count // 2
    out_rows = width + rank_size

    def tile_index(k, pairs, cnt, place):
        return (jnp.maximum(jnp.minimum(k, cnt[0] - 1), 0), 0, 0)

    whole = lambda k, p, c, q: (0, 0, 0)
    grid_spec = pltpu.PrefetchScalarGridSpec(
        num_scalar_prefetch=3,
        grid=(slot_count,),
        in_specs=[
            pl.BlockSpec((None, width, width), tile_index),
            pl.BlockSpec(stack.shape, whole),
            pl.BlockSpec(masked_t.shape, whole),
        ],
        out_specs=[
            pl.BlockSpec((half_count, out_rows, rhs_count), whole),
            pl.BlockSpec((half_count, out_rows, rhs_count), whole),
        ],
        scratch_shapes=[pltpu.VMEM((inner_count, width, rhs_count), jnp.float32)],
    )
    out = jax.ShapeDtypeStruct((half_count, out_rows, rhs_count), jnp.bfloat16)
    return pl.pallas_call(
        _near_far_kernel,
        grid_spec=grid_spec,
        out_shape=[out, out],
        compiler_params=pltpu.CompilerParams(
            dimension_semantics=("arbitrary",), vmem_limit_bytes=56 * 1024 * 1024
        ),
    )(pairs_flat, count, place, tiles, stack, masked_t)


def _epilogue_kernel(total_ref, basis_ref, out_ref):
    width = out_ref.shape[0]
    near = total_ref[:width, :]
    coeffs = total_ref[width:, :].astype(jnp.bfloat16)
    far = lax.dot_general(
        basis_ref[0], coeffs, (((0,), (0,)), ((), ())), preferred_element_type=jnp.float32
    )
    out_ref[...] = (near + far).astype(out_ref.dtype)


def _epilogue(total, basis):
    width = basis.shape[2]
    return pl.pallas_call(
        _epilogue_kernel,
        out_shape=jax.ShapeDtypeStruct((width, total.shape[1]), jnp.bfloat16),
    )(total, basis)


def _line_gather(payload, axis):
    n = lax.axis_size(axis)
    ups, downs = [], []
    up, down = payload, payload
    for step in range(n - 1):
        up_pairs = [(i, i + 1) for i in range(step, n - 1)]
        down_pairs = [(i + 1, i) for i in range(n - 1 - step)]
        up = lax.ppermute(up, axis, up_pairs)
        down = lax.ppermute(down, axis, down_pairs)
        ups.append(up)
        downs.append(down)
    return jnp.stack(ups[::-1] + [payload] + downs)


def _ring_reduce_scatter(blocks, axis):
    n = lax.axis_size(axis)
    if n == 1:
        return blocks[0]
    me = lax.axis_index(axis)
    ring = [(i, (i + 1) % n) for i in range(n)]
    carry = lax.dynamic_index_in_dim(blocks, jnp.mod(me - 1, n), 0, False)
    for step in range(n - 1):
        arrived = lax.ppermute(carry.astype(jnp.bfloat16), axis, ring)
        own = lax.dynamic_index_in_dim(blocks, jnp.mod(me - 2 - step, n), 0, False)
        carry = arrived.astype(jnp.float32) + own
    return carry


def on_device(density, cluster_basis, near_blocks, near_pairs, near_count, coupling):
    width = cluster_basis.shape[2]
    rank_size = cluster_basis.shape[1]
    rhs_count = density.shape[1]
    tgt_count = lax.axis_size("tgt")
    inner_count = lax.axis_size(("inner", "sub"))
    assert lax.axis_size("sub") == 2 and 2 * width == rhs_count and rank_size % 2 == 0
    basis = cluster_basis[0]
    half_rank = rank_size // 2
    packed = jnp.concatenate([basis[:half_rank], basis[half_rank:]], axis=1)
    payload = jnp.concatenate([density, packed], axis=0)
    stack = _line_gather(payload, "tgt")

    pair_list = near_pairs[0, 0]
    live_count = near_count[0, 0]
    slot_count = pair_list.shape[0]
    flat_pairs = pair_list[:, 0] * tgt_count + pair_list[:, 1]
    live_slots = jnp.arange(slot_count) < live_count
    hit_table = (flat_pairs[:, None] == jnp.arange(inner_count * tgt_count)[None, :]) & live_slots[
        :, None
    ]
    keep_mask = (
        (1.0 - jnp.any(hit_table, axis=0).astype(jnp.float32))
        .reshape(inner_count, 1, tgt_count, 1)
        .astype(jnp.bfloat16)
    )
    masked = coupling[0, 0].reshape(inner_count, rank_size, tgt_count, rank_size) * keep_mask
    masked_t = masked.transpose(2, 0, 1, 3).reshape(tgt_count, inner_count * rank_size, rank_size)

    place = jnp.stack([lax.axis_index("tgt"), lax.axis_index("sub")]).astype(jnp.int32)
    mine, theirs = _near_far(
        pair_list.reshape(-1), live_count.reshape(1), place, near_blocks[0, 0], stack, masked_t,
        inner_count, rank_size,
    )
    arrived = lax.ppermute(theirs, "sub", [(0, 1), (1, 0)])
    stage = mine.astype(jnp.float32) + arrived.astype(jnp.float32)
    total = _ring_reduce_scatter(stage, "inner")
    return _epilogue(total, cluster_basis)


def solution(mesh):
    in_specs = (
        P(("tgt", "inner", "sub"), "groups"),
        P(("groups", "tgt", "inner", "sub"), None, None),
        P(("groups", "tgt"), ("inner", "sub"), None, None, None),
        P(("groups", "tgt"), ("inner", "sub"), None, None),
        P(("groups", "tgt"), ("inner", "sub")),
        P(("groups", "tgt"), ("inner", "sub"), None, None),
    )
    out_specs = P(("tgt", "inner", "sub"), "groups")
    return jax.shard_map(
        on_device, mesh=mesh, in_specs=in_specs, out_specs=out_specs, check_vma=False
    )
```

```python
import jax
import jax.numpy as jnp
from jax import lax
from jax.experimental import pallas as pl
from jax.experimental.pallas import tpu as pltpu
from jax.sharding import PartitionSpec as P


def _near_far_kernel(
    pairs_ref, count_ref, place_ref, tiles_ref, source_ref, packed_ref, masked_ref,
    mine_ref, theirs_ref, acc_ref, coeff_ref,
):
    step = pl.program_id(0)
    step_total = pl.num_programs(0)
    inner_count, width, rhs_count = acc_ref.shape
    tgt_count = masked_ref.shape[0]
    rank_size = masked_ref.shape[2]
    slot_count = step_total - tgt_count
    half_rank = rank_size // 2
    sub_count = 2
    own_tgt = place_ref[0]
    own_sub = place_ref[1]

    @pl.when(step == 0)
    def _():
        acc_ref[...] = jnp.zeros_like(acc_ref)
        coeff_ref[...] = jnp.zeros_like(coeff_ref)

    @pl.when(step < jnp.minimum(count_ref[0], slot_count))
    def _():
        target = jnp.clip(pairs_ref[2 * step], 0, inner_count - 1)
        term = jnp.dot(tiles_ref[...], source_ref[...], preferred_element_type=jnp.float32)
        acc_ref[target] += term

    @pl.when(step >= slot_count)
    def _():
        source = step - slot_count
        packed = packed_ref[source - own_tgt + tgt_count - 1]
        dens = source_ref[...]
        top = jnp.dot(packed[:, :width], dens, preferred_element_type=jnp.float32)
        bottom = jnp.dot(packed[:, width:], dens, preferred_element_type=jnp.float32)
        projected = jnp.concatenate([top, bottom], axis=0).astype(jnp.bfloat16)
        coeff_ref[...] += jnp.dot(masked_ref[source], projected, preferred_element_type=jnp.float32)

    @pl.when(step == step_total - 1)
    def _():
        def write(first_ref, second_ref):
            for target in range(inner_count):
                dest = first_ref if target % sub_count == 0 else second_ref
                row = target // sub_count
                dest[row, :width, :] = acc_ref[target].astype(dest.dtype)
                dest[row, width:, :] = coeff_ref[
                    target * rank_size : (target + 1) * rank_size
                ].astype(dest.dtype)

        @pl.when(own_sub == 0)
        def _():
            write(mine_ref, theirs_ref)

        @pl.when(own_sub != 0)
        def _():
            write(theirs_ref, mine_ref)


def _near_far(pairs_flat, count, place, tiles, stack, masked_t, inner_count, rank_size):
    slot_count, width, _ = tiles.shape
    stack_count, rows, rhs_count = stack.shape
    tgt_count = masked_t.shape[0]
    half_rank = rank_size // 2
    half_count = inner_count // 2
    out_rows = width + rank_size

    def last_slot(k, cnt):
        return jnp.maximum(jnp.minimum(jnp.minimum(k, cnt[0] - 1), slot_count - 1), 0)

    def tile_index(k, pairs, cnt, place):
        return (last_slot(k, cnt), 0, 0)

    def source_index(k, pairs, cnt, place):
        near_source = jnp.clip(pairs[2 * last_slot(k, cnt) + 1], 0, tgt_count - 1)
        source = jnp.where(k < slot_count, near_source, k - slot_count)
        return (source - place[0] + tgt_count - 1, 0, 0)

    whole = lambda k, p, c, q: (0, 0, 0)
    grid_spec = pltpu.PrefetchScalarGridSpec(
        num_scalar_prefetch=3,
        grid=(slot_count + tgt_count,),
        in_specs=[
            pl.BlockSpec((None, width, width), tile_index),
            pl.BlockSpec((None, width, rhs_count), source_index),
            pl.BlockSpec(
                (stack_count, half_rank, rhs_count), lambda k, p, c, q: (0, width // half_rank, 0)
            ),
            pl.BlockSpec(masked_t.shape, whole),
        ],
        out_specs=[
            pl.BlockSpec((half_count, out_rows, rhs_count), whole),
            pl.BlockSpec((half_count, out_rows, rhs_count), whole),
        ],
        scratch_shapes=[
            pltpu.VMEM((inner_count, width, rhs_count), jnp.float32),
            pltpu.VMEM((inner_count * rank_size, rhs_count), jnp.float32),
        ],
    )
    out = jax.ShapeDtypeStruct((half_count, out_rows, rhs_count), jnp.bfloat16)
    return pl.pallas_call(
        _near_far_kernel,
        grid_spec=grid_spec,
        out_shape=[out, out],
        compiler_params=pltpu.CompilerParams(
            dimension_semantics=("arbitrary",), vmem_limit_bytes=56 * 1024 * 1024
        ),
    )(pairs_flat, count, place, tiles, stack, stack, masked_t)


def _epilogue_kernel(basis_ref, *refs):
    piece_refs, out_ref = refs[:-1], refs[-1]
    width = out_ref.shape[0]
    total = piece_refs[0][...].astype(jnp.float32)
    for piece_ref in piece_refs[1:]:
        total += piece_ref[...].astype(jnp.float32)
    coeffs = total[width:, :].astype(jnp.bfloat16)
    far = lax.dot_general(
        basis_ref[0], coeffs, (((0,), (0,)), ((), ())), preferred_element_type=jnp.float32
    )
    out_ref[...] = (total[:width, :] + far).astype(out_ref.dtype)


def _epilogue(pieces, basis):
    width = basis.shape[2]
    return pl.pallas_call(
        _epilogue_kernel,
        out_shape=jax.ShapeDtypeStruct((width, pieces[0].shape[1]), jnp.bfloat16),
    )(basis, *pieces)


def _line_gather(payload, axis):
    n = lax.axis_size(axis)
    ups, downs = [], []
    up, down = payload, payload
    for step in range(n - 1):
        up_pairs = [(i, i + 1) for i in range(step, n - 1)]
        down_pairs = [(i + 1, i) for i in range(n - 1 - step)]
        up = lax.ppermute(up, axis, up_pairs)
        down = lax.ppermute(down, axis, down_pairs)
        ups.append(up)
        downs.append(down)
    return jnp.stack(ups[::-1] + [payload] + downs)


def _ring_reduce_scatter(blocks, axis):
    n = lax.axis_size(axis)
    if n == 1:
        return blocks[0]
    me = lax.axis_index(axis)
    ring = [(i, (i + 1) % n) for i in range(n)]
    carry = lax.dynamic_index_in_dim(blocks, jnp.mod(me - 1, n), 0, False)
    for step in range(n - 1):
        arrived = lax.ppermute(carry.astype(jnp.bfloat16), axis, ring)
        own = lax.dynamic_index_in_dim(blocks, jnp.mod(me - 2 - step, n), 0, False)
        carry = arrived.astype(jnp.float32) + own
    return carry


def on_device(density, cluster_basis, near_blocks, near_pairs, near_count, coupling):
    width = cluster_basis.shape[2]
    rank_size = cluster_basis.shape[1]
    rhs_count = density.shape[1]
    tgt_count = lax.axis_size("tgt")
    inner_count = lax.axis_size(("inner", "sub"))
    assert lax.axis_size("sub") == 2 and 2 * width == rhs_count and rank_size % 2 == 0
    basis = cluster_basis[0]
    half_rank = rank_size // 2
    packed = jnp.concatenate([basis[:half_rank], basis[half_rank:]], axis=1)
    payload = jnp.concatenate([density, packed], axis=0)
    stack = _line_gather(payload, "tgt")

    pair_list = near_pairs[0, 0]
    live_count = near_count[0, 0]
    slot_count = pair_list.shape[0]
    flat_pairs = pair_list[:, 0] * tgt_count + pair_list[:, 1]
    live_slots = jnp.arange(slot_count) < live_count
    hit_table = (flat_pairs[:, None] == jnp.arange(inner_count * tgt_count)[None, :]) & live_slots[
        :, None
    ]
    keep_mask = (
        (1.0 - jnp.any(hit_table, axis=0).astype(jnp.float32))
        .reshape(inner_count, 1, tgt_count, 1)
        .astype(jnp.bfloat16)
    )
    masked = coupling[0, 0].reshape(inner_count, rank_size, tgt_count, rank_size) * keep_mask
    masked_t = masked.transpose(2, 0, 1, 3).reshape(tgt_count, inner_count * rank_size, rank_size)

    place = jnp.stack([lax.axis_index("tgt"), lax.axis_index("sub")]).astype(jnp.int32)
    mine, theirs = _near_far(
        pair_list.reshape(-1), live_count.reshape(1), place, near_blocks[0, 0], stack, masked_t,
        inner_count, rank_size,
    )
    arrived = lax.ppermute(theirs, "sub", [(0, 1), (1, 0)])
    if lax.axis_size("inner") == 2:
        me = lax.axis_index("inner")
        send = (
            lax.dynamic_index_in_dim(mine, 1 - me, 0, False).astype(jnp.float32)
            + lax.dynamic_index_in_dim(arrived, 1 - me, 0, False).astype(jnp.float32)
        ).astype(jnp.bfloat16)
        back = lax.ppermute(send, "inner", [(0, 1), (1, 0)])
        pieces = (
            lax.dynamic_index_in_dim(mine, me, 0, False),
            lax.dynamic_index_in_dim(arrived, me, 0, False),
            back,
        )
    else:
        stage = mine.astype(jnp.float32) + arrived.astype(jnp.float32)
        pieces = (_ring_reduce_scatter(stage, "inner"),)
    return _epilogue(pieces, cluster_basis)


def solution(mesh):
    in_specs = (
        P(("tgt", "inner", "sub"), "groups"),
        P(("groups", "tgt", "inner", "sub"), None, None),
        P(("groups", "tgt"), ("inner", "sub"), None, None, None),
        P(("groups", "tgt"), ("inner", "sub"), None, None),
        P(("groups", "tgt"), ("inner", "sub")),
        P(("groups", "tgt"), ("inner", "sub"), None, None),
    )
    out_specs = P(("tgt", "inner", "sub"), "groups")
    return jax.shard_map(
        on_device, mesh=mesh, in_specs=in_specs, out_specs=out_specs, check_vma=False
    )
```

```python
import jax
import jax.numpy as jnp
from jax import lax
from jax.experimental import pallas as pl
from jax.experimental.pallas import tpu as pltpu
from jax.sharding import PartitionSpec as P


def _near_far_kernel(
    pairs_ref, count_ref, place_ref, tiles_ref, stack_ref, masked_ref, mine_ref, theirs_ref, acc_ref
):
    slot = pl.program_id(0)
    slot_total = pl.num_programs(0)
    inner_count, width, rhs_count = acc_ref.shape
    tgt_count = masked_ref.shape[0]
    rank_size = masked_ref.shape[2]
    half_rank = rank_size // 2
    sub_count = 2
    own_tgt = place_ref[0]
    own_sub = place_ref[1]

    @pl.when(slot == 0)
    def _():
        acc_ref[...] = jnp.zeros_like(acc_ref)

    @pl.when(slot < count_ref[0])
    def _():
        target = jnp.clip(pairs_ref[2 * slot], 0, inner_count - 1)
        source = jnp.clip(pairs_ref[2 * slot + 1], 0, tgt_count - 1)
        term = jnp.dot(
            tiles_ref[...],
            stack_ref[source - own_tgt + tgt_count - 1, :width, :],
            preferred_element_type=jnp.float32,
        )
        acc_ref[target] += term

    @pl.when(slot == slot_total - 1)
    def _():
        coeffs = jnp.zeros((inner_count * rank_size, rhs_count), jnp.float32)
        for source in range(tgt_count):
            block = stack_ref[source - own_tgt + tgt_count - 1]
            dens = block[:width, :]
            packed = block[width:, :]
            top = jnp.dot(packed[:, :width], dens, preferred_element_type=jnp.float32)
            bottom = jnp.dot(packed[:, width:], dens, preferred_element_type=jnp.float32)
            projected = jnp.concatenate([top, bottom], axis=0).astype(jnp.bfloat16)
            coeffs += jnp.dot(masked_ref[source], projected, preferred_element_type=jnp.float32)
        coeffs = coeffs.astype(jnp.bfloat16)

        def write(first_ref, second_ref):
            for target in range(inner_count):
                dest = first_ref if target % sub_count == 0 else second_ref
                row = target // sub_count
                dest[row, :width, :] = acc_ref[target].astype(dest.dtype)
                dest[row, width:, :] = coeffs[target * rank_size : (target + 1) * rank_size]

        @pl.when(own_sub == 0)
        def _():
            write(mine_ref, theirs_ref)

        @pl.when(own_sub != 0)
        def _():
            write(theirs_ref, mine_ref)


def _near_far(pairs_flat, count, place, tiles, stack, masked_t, inner_count, rank_size):
    slot_count, width, _ = tiles.shape
    stack_count, rows, rhs_count = stack.shape
    half_count = inner_count // 2
    out_rows = width + rank_size

    def tile_index(k, pairs, cnt, place):
        return (jnp.maximum(jnp.minimum(k, cnt[0] - 1), 0), 0, 0)

    whole = lambda k, p, c, q: (0, 0, 0)
    grid_spec = pltpu.PrefetchScalarGridSpec(
        num_scalar_prefetch=3,
        grid=(slot_count,),
        in_specs=[
            pl.BlockSpec((None, width, width), tile_index),
            pl.BlockSpec(stack.shape, whole),
            pl.BlockSpec(masked_t.shape, whole),
        ],
        out_specs=[
            pl.BlockSpec((half_count, out_rows, rhs_count), whole),
            pl.BlockSpec((half_count, out_rows, rhs_count), whole),
        ],
        scratch_shapes=[pltpu.VMEM((inner_count, width, rhs_count), jnp.float32)],
    )
    out = jax.ShapeDtypeStruct((half_count, out_rows, rhs_count), jnp.bfloat16)
    block_bytes = 2 * (
        width * width * tiles.dtype.itemsize
        + stack.size * stack.dtype.itemsize
        + masked_t.size * masked_t.dtype.itemsize
        + 2 * half_count * out_rows * rhs_count * 2
    )
    vmem_bytes = block_bytes + inner_count * width * rhs_count * 4 + (4 << 20)
    return pl.pallas_call(
        _near_far_kernel,
        grid_spec=grid_spec,
        out_shape=[out, out],
        compiler_params=pltpu.CompilerParams(
            dimension_semantics=("arbitrary",), vmem_limit_bytes=int(vmem_bytes)
        ),
    )(pairs_flat, count, place, tiles, stack, masked_t)


def _epilogue_kernel(total_ref, basis_ref, out_ref):
    width = out_ref.shape[0]
    near = total_ref[:width, :]
    coeffs = total_ref[width:, :].astype(jnp.bfloat16)
    far = lax.dot_general(
        basis_ref[0], coeffs, (((0,), (0,)), ((), ())), preferred_element_type=jnp.float32
    )
    out_ref[...] = (near + far).astype(out_ref.dtype)


def _epilogue(total, basis):
    width = basis.shape[2]
    return pl.pallas_call(
        _epilogue_kernel,
        out_shape=jax.ShapeDtypeStruct((width, total.shape[1]), jnp.bfloat16),
    )(total, basis)


def _line_gather(payload, axis):
    n = lax.axis_size(axis)
    ups, downs = [], []
    up, down = payload, payload
    for step in range(n - 1):
        up_pairs = [(i, i + 1) for i in range(step, n - 1)]
        down_pairs = [(i + 1, i) for i in range(n - 1 - step)]
        up = lax.ppermute(up, axis, up_pairs)
        down = lax.ppermute(down, axis, down_pairs)
        ups.append(up)
        downs.append(down)
    return jnp.stack(ups[::-1] + [payload] + downs)


def _ring_reduce_scatter(blocks, axis):
    n = lax.axis_size(axis)
    if n == 1:
        return blocks[0]
    me = lax.axis_index(axis)
    ring = [(i, (i + 1) % n) for i in range(n)]
    carry = lax.dynamic_index_in_dim(blocks, jnp.mod(me - 1, n), 0, False)
    for step in range(n - 1):
        arrived = lax.ppermute(carry.astype(jnp.bfloat16), axis, ring)
        own = lax.dynamic_index_in_dim(blocks, jnp.mod(me - 2 - step, n), 0, False)
        carry = arrived.astype(jnp.float32) + own
    return carry


def on_device(density, cluster_basis, near_blocks, near_pairs, near_count, coupling):
    width = cluster_basis.shape[2]
    rank_size = cluster_basis.shape[1]
    rhs_count = density.shape[1]
    tgt_count = lax.axis_size("tgt")
    inner_count = lax.axis_size(("inner", "sub"))
    assert lax.axis_size("sub") == 2 and 2 * width == rhs_count and rank_size % 2 == 0
    basis = cluster_basis[0]
    half_rank = rank_size // 2
    packed = jnp.concatenate([basis[:half_rank], basis[half_rank:]], axis=1)
    payload = jnp.concatenate([density, packed], axis=0)
    stack = _line_gather(payload, "tgt")

    pair_list = near_pairs[0, 0]
    live_count = near_count[0, 0]
    slot_count = pair_list.shape[0]
    flat_pairs = pair_list[:, 0] * tgt_count + pair_list[:, 1]
    live_slots = jnp.arange(slot_count) < live_count
    hit_table = (flat_pairs[:, None] == jnp.arange(inner_count * tgt_count)[None, :]) & live_slots[
        :, None
    ]
    keep_mask = (
        (1.0 - jnp.any(hit_table, axis=0).astype(jnp.float32))
        .reshape(inner_count, 1, tgt_count, 1)
        .astype(jnp.bfloat16)
    )
    masked = coupling[0, 0].reshape(inner_count, rank_size, tgt_count, rank_size) * keep_mask
    masked_t = masked.transpose(2, 0, 1, 3).reshape(tgt_count, inner_count * rank_size, rank_size)

    place = jnp.stack([lax.axis_index("tgt"), lax.axis_index("sub")]).astype(jnp.int32)
    mine, theirs = _near_far(
        pair_list.reshape(-1), live_count.reshape(1), place, near_blocks[0, 0], stack, masked_t,
        inner_count, rank_size,
    )
    arrived = lax.ppermute(theirs, "sub", [(0, 1), (1, 0)])
    stage = mine.astype(jnp.float32) + arrived.astype(jnp.float32)
    total = _ring_reduce_scatter(stage, "inner")
    return _epilogue(total, cluster_basis)


def solution(mesh):
    in_specs = (
        P(("tgt", "inner", "sub"), "groups"),
        P(("groups", "tgt", "inner", "sub"), None, None),
        P(("groups", "tgt"), ("inner", "sub"), None, None, None),
        P(("groups", "tgt"), ("inner", "sub"), None, None),
        P(("groups", "tgt"), ("inner", "sub")),
        P(("groups", "tgt"), ("inner", "sub"), None, None),
    )
    out_specs = P(("tgt", "inner", "sub"), "groups")
    return jax.shard_map(
        on_device, mesh=mesh, in_specs=in_specs, out_specs=out_specs, check_vma=False
    )
```

```python
import jax
import jax.numpy as jnp
from jax import lax
from jax.experimental import pallas as pl
from jax.experimental.pallas import tpu as pltpu
from jax.sharding import PartitionSpec as P


def _near_far_kernel(
    pairs_ref, count_ref, place_ref, tiles_ref, stack_ref, masked_ref, mine_ref, theirs_ref, acc_ref
):
    slot = pl.program_id(0)
    slot_total = pl.num_programs(0)
    inner_count, width, rhs_count = acc_ref.shape
    tgt_count = masked_ref.shape[0]
    rank_size = masked_ref.shape[2]
    half_rank = rank_size // 2
    sub_count = 2
    own_tgt = place_ref[0]
    own_sub = place_ref[1]

    @pl.when(slot == 0)
    def _():
        acc_ref[...] = jnp.zeros_like(acc_ref)

    @pl.when(slot < count_ref[0])
    def _():
        target = jnp.clip(pairs_ref[2 * slot], 0, inner_count - 1)
        source = jnp.clip(pairs_ref[2 * slot + 1], 0, tgt_count - 1)
        term = jnp.dot(
            tiles_ref[...],
            stack_ref[source - own_tgt + tgt_count - 1, :width, :],
            preferred_element_type=jnp.float32,
        )
        acc_ref[target] += term

    @pl.when(slot == slot_total - 1)
    def _():
        coeffs = jnp.zeros((inner_count * rank_size, rhs_count), jnp.float32)
        for source in range(tgt_count):
            block = stack_ref[source - own_tgt + tgt_count - 1]
            dens = block[:width, :]
            packed = block[width:, :]
            top = jnp.dot(packed[:, :width], dens, preferred_element_type=jnp.float32)
            bottom = jnp.dot(packed[:, width:], dens, preferred_element_type=jnp.float32)
            projected = jnp.concatenate([top, bottom], axis=0).astype(jnp.bfloat16)
            coeffs += jnp.dot(masked_ref[source], projected, preferred_element_type=jnp.float32)
        coeffs = coeffs.astype(jnp.bfloat16)

        def write(first_ref, second_ref):
            for target in range(inner_count):
                dest = first_ref if target % sub_count == 0 else second_ref
                row = target // sub_count
                dest[row, :width, :] = acc_ref[target].astype(dest.dtype)
                dest[row, width:, :] = coeffs[target * rank_size : (target + 1) * rank_size]

        @pl.when(own_sub == 0)
        def _():
            write(mine_ref, theirs_ref)

        @pl.when(own_sub != 0)
        def _():
            write(theirs_ref, mine_ref)


def _near_far(pairs_flat, count, place, tiles, stack, masked_t, inner_count, rank_size):
    slot_count, width, _ = tiles.shape
    stack_count, rows, rhs_count = stack.shape
    half_count = inner_count // 2
    out_rows = width + rank_size

    def tile_index(k, pairs, cnt, place):
        return (jnp.maximum(jnp.minimum(k, cnt[0] - 1), 0), 0, 0)

    whole = lambda k, p, c, q: (0, 0, 0)
    grid_spec = pltpu.PrefetchScalarGridSpec(
        num_scalar_prefetch=3,
        grid=(slot_count,),
        in_specs=[
            pl.BlockSpec((None, width, width), tile_index),
            pl.BlockSpec(stack.shape, whole),
            pl.BlockSpec(masked_t.shape, whole),
        ],
        out_specs=[
            pl.BlockSpec((half_count, out_rows, rhs_count), whole),
            pl.BlockSpec((half_count, out_rows, rhs_count), whole),
        ],
        scratch_shapes=[pltpu.VMEM((inner_count, width, rhs_count), jnp.float32)],
    )
    out = jax.ShapeDtypeStruct((half_count, out_rows, rhs_count), jnp.bfloat16)
    block_bytes = 2 * (
        width * width * tiles.dtype.itemsize
        + stack.size * stack.dtype.itemsize
        + masked_t.size * masked_t.dtype.itemsize
        + 2 * half_count * out_rows * rhs_count * 2
    )
    vmem_bytes = block_bytes + inner_count * width * rhs_count * 4 + (4 << 20)
    return pl.pallas_call(
        _near_far_kernel,
        grid_spec=grid_spec,
        out_shape=[out, out],
        compiler_params=pltpu.CompilerParams(
            dimension_semantics=("arbitrary",), vmem_limit_bytes=int(vmem_bytes)
        ),
    )(pairs_flat, count, place, tiles, stack, masked_t)


def _epilogue_kernel(total_ref, basis_ref, out_ref):
    width = out_ref.shape[0]
    near = total_ref[:width, :]
    coeffs = total_ref[width:, :].astype(jnp.bfloat16)
    far = lax.dot_general(
        basis_ref[0], coeffs, (((0,), (0,)), ((), ())), preferred_element_type=jnp.float32
    )
    out_ref[...] = (near + far).astype(out_ref.dtype)


def _epilogue(total, basis):
    width = basis.shape[2]
    return pl.pallas_call(
        _epilogue_kernel,
        out_shape=jax.ShapeDtypeStruct((width, total.shape[1]), jnp.bfloat16),
    )(total, basis)


def _line_gather(payload, axis):
    n = lax.axis_size(axis)
    if n <= 2:
        far_up = far_down = None
    else:
        far_up = lax.ppermute(payload, axis, [(0, n - 1)])
        far_down = lax.ppermute(payload, axis, [(n - 1, 0)])
    ups, downs = [], []
    up, down = payload, payload
    for step in range(n - 1 if far_up is None else n - 2):
        up_pairs = [(i, i + 1) for i in range(step, n - 1)]
        down_pairs = [(i + 1, i) for i in range(n - 1 - step)]
        up = lax.ppermute(up, axis, up_pairs)
        down = lax.ppermute(down, axis, down_pairs)
        ups.append(up)
        downs.append(down)
    if far_up is not None:
        ups.append(far_up)
        downs.append(far_down)
    return jnp.stack(ups[::-1] + [payload] + downs)


def _ring_reduce_scatter(blocks, axis):
    n = lax.axis_size(axis)
    if n == 1:
        return blocks[0]
    me = lax.axis_index(axis)
    ring = [(i, (i + 1) % n) for i in range(n)]
    carry = lax.dynamic_index_in_dim(blocks, jnp.mod(me - 1, n), 0, False)
    for step in range(n - 1):
        arrived = lax.ppermute(carry.astype(jnp.bfloat16), axis, ring)
        own = lax.dynamic_index_in_dim(blocks, jnp.mod(me - 2 - step, n), 0, False)
        carry = arrived.astype(jnp.float32) + own
    return carry


def on_device(density, cluster_basis, near_blocks, near_pairs, near_count, coupling):
    width = cluster_basis.shape[2]
    rank_size = cluster_basis.shape[1]
    rhs_count = density.shape[1]
    tgt_count = lax.axis_size("tgt")
    inner_count = lax.axis_size(("inner", "sub"))
    assert lax.axis_size("sub") == 2 and 2 * width == rhs_count and rank_size % 2 == 0
    basis = cluster_basis[0]
    half_rank = rank_size // 2
    packed = jnp.concatenate([basis[:half_rank], basis[half_rank:]], axis=1)
    payload = jnp.concatenate([density, packed], axis=0)
    stack = _line_gather(payload, "tgt")

    pair_list = near_pairs[0, 0]
    live_count = near_count[0, 0]
    slot_count = pair_list.shape[0]
    flat_pairs = pair_list[:, 0] * tgt_count + pair_list[:, 1]
    live_slots = jnp.arange(slot_count) < live_count
    hit_table = (flat_pairs[:, None] == jnp.arange(inner_count * tgt_count)[None, :]) & live_slots[
        :, None
    ]
    keep_mask = (
        (1.0 - jnp.any(hit_table, axis=0).astype(jnp.float32))
        .reshape(inner_count, 1, tgt_count, 1)
        .astype(jnp.bfloat16)
    )
    masked = coupling[0, 0].reshape(inner_count, rank_size, tgt_count, rank_size) * keep_mask
    masked_t = masked.transpose(2, 0, 1, 3).reshape(tgt_count, inner_count * rank_size, rank_size)

    place = jnp.stack([lax.axis_index("tgt"), lax.axis_index("sub")]).astype(jnp.int32)
    mine, theirs = _near_far(
        pair_list.reshape(-1), live_count.reshape(1), place, near_blocks[0, 0], stack, masked_t,
        inner_count, rank_size,
    )
    arrived = lax.ppermute(theirs, "sub", [(0, 1), (1, 0)])
    stage = mine.astype(jnp.float32) + arrived.astype(jnp.float32)
    total = _ring_reduce_scatter(stage, "inner")
    return _epilogue(total, cluster_basis)


def solution(mesh):
    in_specs = (
        P(("tgt", "inner", "sub"), "groups"),
        P(("groups", "tgt", "inner", "sub"), None, None),
        P(("groups", "tgt"), ("inner", "sub"), None, None, None),
        P(("groups", "tgt"), ("inner", "sub"), None, None),
        P(("groups", "tgt"), ("inner", "sub")),
        P(("groups", "tgt"), ("inner", "sub"), None, None),
    )
    out_specs = P(("tgt", "inner", "sub"), "groups")
    return jax.shard_map(
        on_device, mesh=mesh, in_specs=in_specs, out_specs=out_specs, check_vma=False
    )
```

```python
import jax
import jax.numpy as jnp
from jax import lax
from jax.experimental import pallas as pl
from jax.experimental.pallas import tpu as pltpu
from jax.sharding import PartitionSpec as P


def _near_far_kernel(
    pairs_ref,
    count_ref,
    place_ref,
    tiles_ref,
    stack_ref,
    packed_ref,
    masked_ref,
    mine_ref,
    theirs_ref,
    acc_ref,
):
    slot = pl.program_id(0)
    slot_total = pl.num_programs(0)
    inner_count, width, rhs_count = acc_ref.shape
    tgt_count = masked_ref.shape[0]
    rank_size = masked_ref.shape[2]
    half_rank = rank_size // 2
    sub_count = 2
    own_tgt = place_ref[0]
    own_sub = place_ref[1]

    @pl.when(slot == 0)
    def _():
        acc_ref[...] = jnp.zeros_like(acc_ref)

    @pl.when(slot < count_ref[0])
    def _():
        target = jnp.clip(pairs_ref[2 * slot], 0, inner_count - 1)
        source = jnp.clip(pairs_ref[2 * slot + 1], 0, tgt_count - 1)
        term = jnp.dot(
            tiles_ref[...],
            stack_ref[source - own_tgt + tgt_count - 1, :width, :],
            preferred_element_type=jnp.float32,
        )
        acc_ref[target] += term

    @pl.when(slot == slot_total - 1)
    def _():
        coeffs = jnp.zeros((inner_count * rank_size, rhs_count), jnp.float32)
        for source in range(tgt_count):
            offset = source - own_tgt + tgt_count - 1
            dens = stack_ref[offset, :width, :]
            packed = packed_ref[offset]
            top = jnp.dot(packed[:, :width], dens, preferred_element_type=jnp.float32)
            bottom = jnp.dot(packed[:, width:], dens, preferred_element_type=jnp.float32)
            projected = jnp.concatenate([top, bottom], axis=0).astype(jnp.bfloat16)
            coeffs += jnp.dot(masked_ref[source], projected, preferred_element_type=jnp.float32)
        coeffs = coeffs.astype(jnp.bfloat16)

        def write(first_ref, second_ref):
            for target in range(inner_count):
                dest = first_ref if target % sub_count == 0 else second_ref
                row = target // sub_count
                dest[row, :width, :] = acc_ref[target].astype(dest.dtype)
                dest[row, width:, :] = coeffs[target * rank_size : (target + 1) * rank_size]

        @pl.when(own_sub == 0)
        def _():
            write(mine_ref, theirs_ref)

        @pl.when(own_sub != 0)
        def _():
            write(theirs_ref, mine_ref)


def _near_far(pairs_flat, count, place, tiles, stack, masked_t, inner_count, rank_size, chunk, cols):
    slot_count, width, _ = tiles.shape
    stack_count, rows, full_cols = stack.shape
    half_rank = rank_size // 2
    half_count = inner_count // 2
    out_rows = width + rank_size

    def tile_index(k, pairs, cnt, place):
        return (jnp.maximum(jnp.minimum(k, cnt[0] - 1), 0), 0, 0)

    whole = lambda k, p, c, q: (0, 0, 0)
    grid_spec = pltpu.PrefetchScalarGridSpec(
        num_scalar_prefetch=3,
        grid=(slot_count,),
        in_specs=[
            pl.BlockSpec((None, width, width), tile_index),
            pl.BlockSpec((stack_count, width, cols), lambda k, p, c, q: (0, 0, chunk)),
            pl.BlockSpec(
                (stack_count, half_rank, full_cols), lambda k, p, c, q: (0, width // half_rank, 0)
            ),
            pl.BlockSpec(masked_t.shape, whole),
        ],
        out_specs=[
            pl.BlockSpec((half_count, out_rows, cols), whole),
            pl.BlockSpec((half_count, out_rows, cols), whole),
        ],
        scratch_shapes=[pltpu.VMEM((inner_count, width, cols), jnp.float32)],
    )
    out = jax.ShapeDtypeStruct((half_count, out_rows, cols), jnp.bfloat16)
    block_bytes = 2 * 2 * (
        width * width
        + stack_count * width * cols
        + stack_count * half_rank * full_cols
        + masked_t.size
        + 2 * half_count * out_rows * cols
    )
    vmem_bytes = block_bytes + inner_count * width * cols * 4 + (4 << 20)
    return pl.pallas_call(
        _near_far_kernel,
        grid_spec=grid_spec,
        out_shape=[out, out],
        compiler_params=pltpu.CompilerParams(
            dimension_semantics=("arbitrary",), vmem_limit_bytes=int(vmem_bytes)
        ),
    )(pairs_flat, count, place, tiles, stack, stack, masked_t)


def _epilogue_kernel(me_ref, basis_ref, *refs):
    piece_refs, out_ref = refs[:-1], refs[-1]
    width = out_ref.shape[0]
    total = piece_refs[0][...].astype(jnp.float32)
    for piece_ref in piece_refs[1:]:
        total += piece_ref[...].astype(jnp.float32)
    coeffs = total[width:, :].astype(jnp.bfloat16)
    far = lax.dot_general(
        basis_ref[0], coeffs, (((0,), (0,)), ((), ())), preferred_element_type=jnp.float32
    )
    out_ref[...] = (total[:width, :] + far).astype(out_ref.dtype)


def _epilogue(me, pieces, basis, chunk, rhs_count, previous):
    width = basis.shape[2]
    cols = pieces[0].shape[-1]
    in_specs = [pl.BlockSpec(basis.shape, lambda i, m: (0, 0, 0))]
    for piece in pieces:
        if piece.ndim == 3:
            in_specs.append(pl.BlockSpec((None,) + piece.shape[1:], lambda i, m: (m[0], 0, 0)))
        else:
            in_specs.append(pl.BlockSpec(piece.shape, lambda i, m: (0, 0)))
    args = [me, basis, *pieces]
    aliases = {}
    if previous is not None:
        in_specs.append(pl.BlockSpec(memory_space=pl.ANY))
        args.append(previous)
        aliases = {len(args) - 1: 0}
    grid_spec = pltpu.PrefetchScalarGridSpec(
        num_scalar_prefetch=1,
        grid=(1,),
        in_specs=in_specs,
        out_specs=pl.BlockSpec((width, cols), lambda i, m: (0, chunk)),
    )
    kernel = _epilogue_kernel
    if previous is not None:
        kernel = lambda m, b, *r: _epilogue_kernel(m, b, *r[:-2], r[-1])
    return pl.pallas_call(
        kernel,
        grid_spec=grid_spec,
        out_shape=jax.ShapeDtypeStruct((width, rhs_count), jnp.bfloat16),
        input_output_aliases=aliases,
    )(*args)


def _line_gather(payload, axis):
    n = lax.axis_size(axis)
    if n <= 2:
        far_up = far_down = None
    else:
        far_up = lax.ppermute(payload, axis, [(0, n - 1)])
        far_down = lax.ppermute(payload, axis, [(n - 1, 0)])
    ups, downs = [], []
    up, down = payload, payload
    for step in range(n - 1 if far_up is None else n - 2):
        up_pairs = [(i, i + 1) for i in range(step, n - 1)]
        down_pairs = [(i + 1, i) for i in range(n - 1 - step)]
        up = lax.ppermute(up, axis, up_pairs)
        down = lax.ppermute(down, axis, down_pairs)
        ups.append(up)
        downs.append(down)
    if far_up is not None:
        ups.append(far_up)
        downs.append(far_down)
    return jnp.stack(ups[::-1] + [payload] + downs)


def _ring_reduce_scatter(blocks, axis):
    n = lax.axis_size(axis)
    if n == 1:
        return blocks[0]
    me = lax.axis_index(axis)
    ring = [(i, (i + 1) % n) for i in range(n)]
    carry = lax.dynamic_index_in_dim(blocks, jnp.mod(me - 1, n), 0, False)
    for step in range(n - 1):
        arrived = lax.ppermute(carry.astype(jnp.bfloat16), axis, ring)
        own = lax.dynamic_index_in_dim(blocks, jnp.mod(me - 2 - step, n), 0, False)
        carry = arrived.astype(jnp.float32) + own
    return carry


def on_device(density, cluster_basis, near_blocks, near_pairs, near_count, coupling):
    width = cluster_basis.shape[2]
    rank_size = cluster_basis.shape[1]
    rhs_count = density.shape[1]
    tgt_count = lax.axis_size("tgt")
    inner_count = lax.axis_size(("inner", "sub"))
    assert lax.axis_size("sub") == 2 and 2 * width == rhs_count and rank_size % 2 == 0
    basis = cluster_basis[0]
    half_rank = rank_size // 2
    packed = jnp.concatenate([basis[:half_rank], basis[half_rank:]], axis=1)
    payload = jnp.concatenate([density, packed], axis=0)
    stack = _line_gather(payload, "tgt")

    pair_list = near_pairs[0, 0]
    live_count = near_count[0, 0]
    slot_count = pair_list.shape[0]
    flat_pairs = pair_list[:, 0] * tgt_count + pair_list[:, 1]
    live_slots = jnp.arange(slot_count) < live_count
    hit_table = (flat_pairs[:, None] == jnp.arange(inner_count * tgt_count)[None, :]) & live_slots[
        :, None
    ]
    keep_mask = (
        (1.0 - jnp.any(hit_table, axis=0).astype(jnp.float32))
        .reshape(inner_count, 1, tgt_count, 1)
        .astype(jnp.bfloat16)
    )
    masked = coupling[0, 0].reshape(inner_count, rank_size, tgt_count, rank_size) * keep_mask
    masked_t = masked.transpose(2, 0, 1, 3).reshape(tgt_count, inner_count * rank_size, rank_size)

    place = jnp.stack([lax.axis_index("tgt"), lax.axis_index("sub")]).astype(jnp.int32)
    chunk_count = 2
    cols = rhs_count // chunk_count
    result = None
    for chunk in range(chunk_count):
        mine, theirs = _near_far(
            pair_list.reshape(-1), live_count.reshape(1), place, near_blocks[0, 0], stack,
            masked_t, inner_count, rank_size, chunk, cols,
        )
        arrived = lax.ppermute(theirs, "sub", [(0, 1), (1, 0)])
        if lax.axis_size("inner") == 2:
            me = lax.axis_index("inner")
            send = (
                lax.dynamic_index_in_dim(mine, 1 - me, 0, False).astype(jnp.float32)
                + lax.dynamic_index_in_dim(arrived, 1 - me, 0, False).astype(jnp.float32)
            ).astype(jnp.bfloat16)
            back = lax.ppermute(send, "inner", [(0, 1), (1, 0)])
            pieces = (mine, arrived, back)
        else:
            stage = mine.astype(jnp.float32) + arrived.astype(jnp.float32)
            pieces = (_ring_reduce_scatter(stage, "inner"),)
        me_index = lax.axis_index("inner").astype(jnp.int32).reshape(1)
        result = _epilogue(me_index, pieces, cluster_basis, chunk, rhs_count, result)
    return result


def solution(mesh):
    in_specs = (
        P(("tgt", "inner", "sub"), "groups"),
        P(("groups", "tgt", "inner", "sub"), None, None),
        P(("groups", "tgt"), ("inner", "sub"), None, None, None),
        P(("groups", "tgt"), ("inner", "sub"), None, None),
        P(("groups", "tgt"), ("inner", "sub")),
        P(("groups", "tgt"), ("inner", "sub"), None, None),
    )
    out_specs = P(("tgt", "inner", "sub"), "groups")
    return jax.shard_map(
        on_device, mesh=mesh, in_specs=in_specs, out_specs=out_specs, check_vma=False
    )
```

```python
import jax
import jax.numpy as jnp
from jax import lax
from jax.experimental import pallas as pl
from jax.experimental.pallas import tpu as pltpu
from jax.sharding import PartitionSpec as P


def _near_far_kernel(
    pairs_ref, count_ref, place_ref, tiles_ref, stack_ref, masked_ref, mine_ref, theirs_ref, acc_ref
):
    inner_count, width, rhs_count = acc_ref.shape
    slot_count = tiles_ref.shape[0]
    tgt_count = masked_ref.shape[0]
    rank_size = masked_ref.shape[2]
    sub_count = 2
    own_tgt = place_ref[0]
    own_sub = place_ref[1]
    acc_ref[...] = jnp.zeros_like(acc_ref)

    def add_slot(slot, carry):
        target = jnp.clip(pairs_ref[2 * slot], 0, inner_count - 1)
        source = jnp.clip(pairs_ref[2 * slot + 1], 0, tgt_count - 1)
        term = jnp.dot(
            tiles_ref[slot],
            stack_ref[source - own_tgt + tgt_count - 1, :width, :],
            preferred_element_type=jnp.float32,
        )
        acc_ref[target] += term
        return carry

    lax.fori_loop(0, jnp.clip(count_ref[0], 0, slot_count), add_slot, 0)

    coeffs = jnp.zeros((inner_count * rank_size, rhs_count), jnp.float32)
    for source in range(tgt_count):
        block = stack_ref[source - own_tgt + tgt_count - 1]
        dens = block[:width, :]
        packed = block[width:, :]
        top = jnp.dot(packed[:, :width], dens, preferred_element_type=jnp.float32)
        bottom = jnp.dot(packed[:, width:], dens, preferred_element_type=jnp.float32)
        projected = jnp.concatenate([top, bottom], axis=0).astype(jnp.bfloat16)
        coeffs += jnp.dot(masked_ref[source], projected, preferred_element_type=jnp.float32)
    coeffs = coeffs.astype(jnp.bfloat16)

    def write(first_ref, second_ref):
        for target in range(inner_count):
            dest = first_ref if target % sub_count == 0 else second_ref
            row = target // sub_count
            dest[row, :width, :] = acc_ref[target].astype(dest.dtype)
            dest[row, width:, :] = coeffs[target * rank_size : (target + 1) * rank_size]

    @pl.when(own_sub == 0)
    def _():
        write(mine_ref, theirs_ref)

    @pl.when(own_sub != 0)
    def _():
        write(theirs_ref, mine_ref)


def _near_far(pairs_flat, count, place, tiles, stack, masked_t, inner_count, rank_size):
    slot_count, width, _ = tiles.shape
    stack_count, rows, rhs_count = stack.shape
    half_count = inner_count // 2
    out_rows = width + rank_size
    whole = lambda k, p, c, q: (0, 0, 0)
    grid_spec = pltpu.PrefetchScalarGridSpec(
        num_scalar_prefetch=3,
        grid=(1,),
        in_specs=[
            pl.BlockSpec(tiles.shape, whole),
            pl.BlockSpec(stack.shape, whole),
            pl.BlockSpec(masked_t.shape, whole),
        ],
        out_specs=[
            pl.BlockSpec((half_count, out_rows, rhs_count), whole),
            pl.BlockSpec((half_count, out_rows, rhs_count), whole),
        ],
        scratch_shapes=[pltpu.VMEM((inner_count, width, rhs_count), jnp.float32)],
    )
    out = jax.ShapeDtypeStruct((half_count, out_rows, rhs_count), jnp.bfloat16)
    block_bytes = 2 * (
        tiles.size * tiles.dtype.itemsize
        + stack.size * stack.dtype.itemsize
        + masked_t.size * masked_t.dtype.itemsize
        + 2 * half_count * out_rows * rhs_count * 2
    )
    vmem_bytes = block_bytes + inner_count * width * rhs_count * 4 + (4 << 20)
    return pl.pallas_call(
        _near_far_kernel,
        grid_spec=grid_spec,
        out_shape=[out, out],
        compiler_params=pltpu.CompilerParams(
            dimension_semantics=("arbitrary",), vmem_limit_bytes=int(vmem_bytes)
        ),
    )(pairs_flat, count, place, tiles, stack, masked_t)


def _epilogue_kernel(total_ref, basis_ref, out_ref):
    width = out_ref.shape[0]
    near = total_ref[:width, :]
    coeffs = total_ref[width:, :].astype(jnp.bfloat16)
    far = lax.dot_general(
        basis_ref[0], coeffs, (((0,), (0,)), ((), ())), preferred_element_type=jnp.float32
    )
    out_ref[...] = (near + far).astype(out_ref.dtype)


def _epilogue(total, basis):
    width = basis.shape[2]
    return pl.pallas_call(
        _epilogue_kernel,
        out_shape=jax.ShapeDtypeStruct((width, total.shape[1]), jnp.bfloat16),
    )(total, basis)


def _line_gather(payload, axis):
    n = lax.axis_size(axis)
    if n <= 2:
        far_up = far_down = None
    else:
        far_up = lax.ppermute(payload, axis, [(0, n - 1)])
        far_down = lax.ppermute(payload, axis, [(n - 1, 0)])
    ups, downs = [], []
    up, down = payload, payload
    for step in range(n - 1 if far_up is None else n - 2):
        up_pairs = [(i, i + 1) for i in range(step, n - 1)]
        down_pairs = [(i + 1, i) for i in range(n - 1 - step)]
        up = lax.ppermute(up, axis, up_pairs)
        down = lax.ppermute(down, axis, down_pairs)
        ups.append(up)
        downs.append(down)
    if far_up is not None:
        ups.append(far_up)
        downs.append(far_down)
    return jnp.stack(ups[::-1] + [payload] + downs)


def _ring_reduce_scatter(blocks, axis):
    n = lax.axis_size(axis)
    if n == 1:
        return blocks[0]
    me = lax.axis_index(axis)
    ring = [(i, (i + 1) % n) for i in range(n)]
    carry = lax.dynamic_index_in_dim(blocks, jnp.mod(me - 1, n), 0, False)
    for step in range(n - 1):
        arrived = lax.ppermute(carry.astype(jnp.bfloat16), axis, ring)
        own = lax.dynamic_index_in_dim(blocks, jnp.mod(me - 2 - step, n), 0, False)
        carry = arrived.astype(jnp.float32) + own
    return carry


def on_device(density, cluster_basis, near_blocks, near_pairs, near_count, coupling):
    width = cluster_basis.shape[2]
    rank_size = cluster_basis.shape[1]
    rhs_count = density.shape[1]
    tgt_count = lax.axis_size("tgt")
    inner_count = lax.axis_size(("inner", "sub"))
    assert lax.axis_size("sub") == 2 and 2 * width == rhs_count and rank_size % 2 == 0
    basis = cluster_basis[0]
    half_rank = rank_size // 2
    packed = jnp.concatenate([basis[:half_rank], basis[half_rank:]], axis=1)
    payload = jnp.concatenate([density, packed], axis=0)
    stack = _line_gather(payload, "tgt")

    pair_list = near_pairs[0, 0]
    live_count = near_count[0, 0]
    slot_count = pair_list.shape[0]
    flat_pairs = pair_list[:, 0] * tgt_count + pair_list[:, 1]
    live_slots = jnp.arange(slot_count) < live_count
    hit_table = (flat_pairs[:, None] == jnp.arange(inner_count * tgt_count)[None, :]) & live_slots[
        :, None
    ]
    keep_mask = (
        (1.0 - jnp.any(hit_table, axis=0).astype(jnp.float32))
        .reshape(inner_count, 1, tgt_count, 1)
        .astype(jnp.bfloat16)
    )
    masked = coupling[0, 0].reshape(inner_count, rank_size, tgt_count, rank_size) * keep_mask
    masked_t = masked.transpose(2, 0, 1, 3).reshape(tgt_count, inner_count * rank_size, rank_size)

    place = jnp.stack([lax.axis_index("tgt"), lax.axis_index("sub")]).astype(jnp.int32)
    mine, theirs = _near_far(
        pair_list.reshape(-1), live_count.reshape(1), place, near_blocks[0, 0], stack, masked_t,
        inner_count, rank_size,
    )
    arrived = lax.ppermute(theirs, "sub", [(0, 1), (1, 0)])
    stage = mine.astype(jnp.float32) + arrived.astype(jnp.float32)
    total = _ring_reduce_scatter(stage, "inner")
    return _epilogue(total, cluster_basis)


def solution(mesh):
    in_specs = (
        P(("tgt", "inner", "sub"), "groups"),
        P(("groups", "tgt", "inner", "sub"), None, None),
        P(("groups", "tgt"), ("inner", "sub"), None, None, None),
        P(("groups", "tgt"), ("inner", "sub"), None, None),
        P(("groups", "tgt"), ("inner", "sub")),
        P(("groups", "tgt"), ("inner", "sub"), None, None),
    )
    out_specs = P(("tgt", "inner", "sub"), "groups")
    return jax.shard_map(
        on_device, mesh=mesh, in_specs=in_specs, out_specs=out_specs, check_vma=False
    )
```

```python
import jax
import jax.numpy as jnp
from jax import lax
from jax.experimental import pallas as pl
from jax.experimental.pallas import tpu as pltpu
from jax.sharding import PartitionSpec as P


def _near_far_kernel(
    pairs_ref, count_ref, place_ref, tiles_ref, stack_ref, masked_ref, mine_ref, theirs_ref, acc_ref
):
    inner_count, width, rhs_count = acc_ref.shape
    slot_count = tiles_ref.shape[0]
    tgt_count = masked_ref.shape[0]
    rank_size = masked_ref.shape[2]
    sub_count = 2
    own_tgt = place_ref[0]
    own_sub = place_ref[1]
    acc_ref[...] = jnp.zeros_like(acc_ref)

    def add_slot(slot, carry):
        target = jnp.clip(pairs_ref[2 * slot], 0, inner_count - 1)
        source = jnp.clip(pairs_ref[2 * slot + 1], 0, tgt_count - 1)
        term = jnp.dot(
            tiles_ref[slot],
            stack_ref[source - own_tgt + tgt_count - 1, :width, :],
            preferred_element_type=jnp.float32,
        )
        acc_ref[target] += term
        return carry

    lax.fori_loop(0, jnp.clip(count_ref[0], 0, slot_count), add_slot, 0)

    coeffs = jnp.zeros((inner_count * rank_size, rhs_count), jnp.float32)
    for source in range(tgt_count):
        block = stack_ref[source - own_tgt + tgt_count - 1]
        dens = block[:width, :]
        packed = block[width:, :]
        top = jnp.dot(packed[:, :width], dens, preferred_element_type=jnp.float32)
        bottom = jnp.dot(packed[:, width:], dens, preferred_element_type=jnp.float32)
        projected = jnp.concatenate([top, bottom], axis=0).astype(jnp.bfloat16)
        coeffs += jnp.dot(masked_ref[source], projected, preferred_element_type=jnp.float32)
    coeffs = coeffs.astype(jnp.bfloat16)

    def write(first_ref, second_ref):
        for target in range(inner_count):
            dest = first_ref if target % sub_count == 0 else second_ref
            row = target // sub_count
            dest[row, :width, :] = acc_ref[target].astype(dest.dtype)
            dest[row, width:, :] = coeffs[target * rank_size : (target + 1) * rank_size]

    @pl.when(own_sub == 0)
    def _():
        write(mine_ref, theirs_ref)

    @pl.when(own_sub != 0)
    def _():
        write(theirs_ref, mine_ref)


def _near_far(pairs_flat, count, place, tiles, stack, masked_t, inner_count, rank_size):
    slot_count, width, _ = tiles.shape
    stack_count, rows, rhs_count = stack.shape
    half_count = inner_count // 2
    out_rows = width + rank_size
    whole = lambda k, p, c, q: (0, 0, 0)
    grid_spec = pltpu.PrefetchScalarGridSpec(
        num_scalar_prefetch=3,
        grid=(1,),
        in_specs=[
            pl.BlockSpec(tiles.shape, whole),
            pl.BlockSpec(stack.shape, whole),
            pl.BlockSpec(masked_t.shape, whole),
        ],
        out_specs=[
            pl.BlockSpec((half_count, out_rows, rhs_count), whole),
            pl.BlockSpec((half_count, out_rows, rhs_count), whole),
        ],
        scratch_shapes=[pltpu.VMEM((inner_count, width, rhs_count), jnp.float32)],
    )
    out = jax.ShapeDtypeStruct((half_count, out_rows, rhs_count), jnp.bfloat16)
    block_bytes = 2 * (
        tiles.size * tiles.dtype.itemsize
        + stack.size * stack.dtype.itemsize
        + masked_t.size * masked_t.dtype.itemsize
        + 2 * half_count * out_rows * rhs_count * 2
    )
    vmem_bytes = block_bytes + inner_count * width * rhs_count * 4 + (4 << 20)
    return pl.pallas_call(
        _near_far_kernel,
        grid_spec=grid_spec,
        out_shape=[out, out],
        compiler_params=pltpu.CompilerParams(
            dimension_semantics=("arbitrary",), vmem_limit_bytes=int(vmem_bytes)
        ),
    )(pairs_flat, count, place, tiles, stack, masked_t)


def _epilogue_kernel(me_ref, basis_t_ref, *refs):
    piece_refs, out_ref = refs[:-1], refs[-1]
    width = out_ref.shape[0]
    total = piece_refs[0][...].astype(jnp.float32)
    for piece_ref in piece_refs[1:]:
        total += piece_ref[...].astype(jnp.float32)
    coeffs = total[width:, :].astype(jnp.bfloat16)
    far = jnp.dot(basis_t_ref[...], coeffs, preferred_element_type=jnp.float32)
    out_ref[...] = (total[:width, :] + far).astype(out_ref.dtype)


def _epilogue(me, pieces, basis_t):
    width = basis_t.shape[0]
    cols = pieces[0].shape[-1]
    in_specs = [pl.BlockSpec(basis_t.shape, lambda i, m: (0, 0))]
    for piece in pieces:
        if piece.ndim == 3:
            in_specs.append(pl.BlockSpec((None,) + piece.shape[1:], lambda i, m: (m[0], 0, 0)))
        else:
            in_specs.append(pl.BlockSpec(piece.shape, lambda i, m: (0, 0)))
    grid_spec = pltpu.PrefetchScalarGridSpec(
        num_scalar_prefetch=1,
        grid=(1,),
        in_specs=in_specs,
        out_specs=pl.BlockSpec((width, cols), lambda i, m: (0, 0)),
    )
    return pl.pallas_call(
        _epilogue_kernel,
        grid_spec=grid_spec,
        out_shape=jax.ShapeDtypeStruct((width, cols), jnp.bfloat16),
    )(me, basis_t, *pieces)


def _line_gather(payload, axis):
    n = lax.axis_size(axis)
    if n <= 2:
        far_up = far_down = None
    else:
        far_up = lax.ppermute(payload, axis, [(0, n - 1)])
        far_down = lax.ppermute(payload, axis, [(n - 1, 0)])
    ups, downs = [], []
    up, down = payload, payload
    for step in range(n - 1 if far_up is None else n - 2):
        up_pairs = [(i, i + 1) for i in range(step, n - 1)]
        down_pairs = [(i + 1, i) for i in range(n - 1 - step)]
        up = lax.ppermute(up, axis, up_pairs)
        down = lax.ppermute(down, axis, down_pairs)
        ups.append(up)
        downs.append(down)
    if far_up is not None:
        ups.append(far_up)
        downs.append(far_down)
    return jnp.stack(ups[::-1] + [payload] + downs)


def _ring_reduce_scatter(blocks, axis):
    n = lax.axis_size(axis)
    if n == 1:
        return blocks[0]
    me = lax.axis_index(axis)
    ring = [(i, (i + 1) % n) for i in range(n)]
    carry = lax.dynamic_index_in_dim(blocks, jnp.mod(me - 1, n), 0, False)
    for step in range(n - 1):
        arrived = lax.ppermute(carry.astype(jnp.bfloat16), axis, ring)
        own = lax.dynamic_index_in_dim(blocks, jnp.mod(me - 2 - step, n), 0, False)
        carry = arrived.astype(jnp.float32) + own
    return carry


def on_device(density, cluster_basis, near_blocks, near_pairs, near_count, coupling):
    width = cluster_basis.shape[2]
    rank_size = cluster_basis.shape[1]
    rhs_count = density.shape[1]
    tgt_count = lax.axis_size("tgt")
    inner_count = lax.axis_size(("inner", "sub"))
    assert lax.axis_size("sub") == 2 and 2 * width == rhs_count and rank_size % 2 == 0
    basis = cluster_basis[0]
    half_rank = rank_size // 2
    packed = jnp.concatenate([basis[:half_rank], basis[half_rank:]], axis=1)
    payload = jnp.concatenate([density, packed], axis=0)
    stack = _line_gather(payload, "tgt")

    pair_list = near_pairs[0, 0]
    live_count = near_count[0, 0]
    slot_count = pair_list.shape[0]
    flat_pairs = pair_list[:, 0] * tgt_count + pair_list[:, 1]
    live_slots = jnp.arange(slot_count) < live_count
    hit_table = (flat_pairs[:, None] == jnp.arange(inner_count * tgt_count)[None, :]) & live_slots[
        :, None
    ]
    keep_mask = (
        (1.0 - jnp.any(hit_table, axis=0).astype(jnp.float32))
        .reshape(inner_count, 1, tgt_count, 1)
        .astype(jnp.bfloat16)
    )
    masked = coupling[0, 0].reshape(inner_count, rank_size, tgt_count, rank_size) * keep_mask
    masked_t = masked.transpose(2, 0, 1, 3).reshape(tgt_count, inner_count * rank_size, rank_size)

    place = jnp.stack([lax.axis_index("tgt"), lax.axis_index("sub")]).astype(jnp.int32)
    mine, theirs = _near_far(
        pair_list.reshape(-1), live_count.reshape(1), place, near_blocks[0, 0], stack, masked_t,
        inner_count, rank_size,
    )
    arrived = lax.ppermute(theirs, "sub", [(0, 1), (1, 0)])
    basis_t = cluster_basis[0].T
    me = lax.axis_index("inner")
    if lax.axis_size("inner") == 2:
        send = (
            lax.dynamic_index_in_dim(mine, 1 - me, 0, False).astype(jnp.float32)
            + lax.dynamic_index_in_dim(arrived, 1 - me, 0, False).astype(jnp.float32)
        ).astype(jnp.bfloat16)
        back = lax.ppermute(send, "inner", [(0, 1), (1, 0)])
        pieces = (mine, arrived, back)
    else:
        stage = mine.astype(jnp.float32) + arrived.astype(jnp.float32)
        pieces = (_ring_reduce_scatter(stage, "inner"),)
    return _epilogue(me.astype(jnp.int32).reshape(1), pieces, basis_t)


def solution(mesh):
    in_specs = (
        P(("tgt", "inner", "sub"), "groups"),
        P(("groups", "tgt", "inner", "sub"), None, None),
        P(("groups", "tgt"), ("inner", "sub"), None, None, None),
        P(("groups", "tgt"), ("inner", "sub"), None, None),
        P(("groups", "tgt"), ("inner", "sub")),
        P(("groups", "tgt"), ("inner", "sub"), None, None),
    )
    out_specs = P(("tgt", "inner", "sub"), "groups")
    return jax.shard_map(
        on_device, mesh=mesh, in_specs=in_specs, out_specs=out_specs, check_vma=False
    )
```

```python
import jax
import jax.numpy as jnp
from jax import lax
from jax.experimental import pallas as pl
from jax.experimental.pallas import tpu as pltpu
from jax.sharding import PartitionSpec as P


def _near_far_kernel(
    pairs_ref, count_ref, place_ref, tiles_ref, stack_ref, masked_ref, mine_ref, theirs_ref, acc_ref
):
    inner_count, width, rhs_count = acc_ref.shape
    slot_count = tiles_ref.shape[0]
    tgt_count = masked_ref.shape[0]
    rank_size = masked_ref.shape[2]
    sub_count = 2
    own_tgt = place_ref[0]
    own_sub = place_ref[1]
    acc_ref[...] = jnp.zeros_like(acc_ref)

    def add_slot(slot, carry):
        target = jnp.clip(pairs_ref[2 * slot], 0, inner_count - 1)
        source = jnp.clip(pairs_ref[2 * slot + 1], 0, tgt_count - 1)
        term = jnp.dot(
            tiles_ref[slot],
            stack_ref[source - own_tgt + tgt_count - 1, :width, :],
            preferred_element_type=jnp.float32,
        )
        acc_ref[target] += term
        return carry

    lax.fori_loop(0, jnp.clip(count_ref[0], 0, slot_count), add_slot, 0)

    coeffs = jnp.zeros((inner_count * rank_size, rhs_count), jnp.float32)
    for source in range(tgt_count):
        block = stack_ref[source - own_tgt + tgt_count - 1]
        dens = block[:width, :]
        packed = block[width:, :]
        top = jnp.dot(packed[:, :width], dens, preferred_element_type=jnp.float32)
        bottom = jnp.dot(packed[:, width:], dens, preferred_element_type=jnp.float32)
        projected = jnp.concatenate([top, bottom], axis=0).astype(jnp.bfloat16)
        coeffs += jnp.dot(masked_ref[source], projected, preferred_element_type=jnp.float32)
    coeffs = coeffs.astype(jnp.bfloat16)

    def write(first_ref, second_ref):
        for target in range(inner_count):
            dest = first_ref if target % sub_count == 0 else second_ref
            row = target // sub_count
            dest[row, :width, :] = acc_ref[target].astype(dest.dtype)
            dest[row, width:, :] = coeffs[target * rank_size : (target + 1) * rank_size]

    @pl.when(own_sub == 0)
    def _():
        write(mine_ref, theirs_ref)

    @pl.when(own_sub != 0)
    def _():
        write(theirs_ref, mine_ref)


def _near_far(pairs_flat, count, place, tiles, stack, masked_t, inner_count, rank_size):
    slot_count, width, _ = tiles.shape
    stack_count, rows, rhs_count = stack.shape
    half_count = inner_count // 2
    out_rows = width + rank_size
    whole = lambda k, p, c, q: (0, 0, 0)
    grid_spec = pltpu.PrefetchScalarGridSpec(
        num_scalar_prefetch=3,
        grid=(1,),
        in_specs=[
            pl.BlockSpec(tiles.shape, whole),
            pl.BlockSpec(stack.shape, whole),
            pl.BlockSpec(masked_t.shape, whole),
        ],
        out_specs=[
            pl.BlockSpec((half_count, out_rows, rhs_count), whole),
            pl.BlockSpec((half_count, out_rows, rhs_count), whole),
        ],
        scratch_shapes=[pltpu.VMEM((inner_count, width, rhs_count), jnp.float32)],
    )
    out = jax.ShapeDtypeStruct((half_count, out_rows, rhs_count), jnp.bfloat16)
    block_bytes = 2 * (
        tiles.size * tiles.dtype.itemsize
        + stack.size * stack.dtype.itemsize
        + masked_t.size * masked_t.dtype.itemsize
        + 2 * half_count * out_rows * rhs_count * 2
    )
    vmem_bytes = block_bytes + inner_count * width * rhs_count * 4 + (4 << 20)
    return pl.pallas_call(
        _near_far_kernel,
        grid_spec=grid_spec,
        out_shape=[out, out],
        compiler_params=pltpu.CompilerParams(
            dimension_semantics=("arbitrary",), vmem_limit_bytes=int(vmem_bytes)
        ),
    )(pairs_flat, count, place, tiles, stack, masked_t)


def _epilogue_kernel(me_ref, basis_t_ref, *refs):
    piece_refs, out_ref = refs[:-1], refs[-1]
    width = out_ref.shape[0]
    total = piece_refs[0][...].astype(jnp.float32)
    for piece_ref in piece_refs[1:]:
        total += piece_ref[...].astype(jnp.float32)
    coeffs = total[width:, :].astype(jnp.bfloat16)
    far = jnp.dot(basis_t_ref[...], coeffs, preferred_element_type=jnp.float32)
    out_ref[...] = (total[:width, :] + far).astype(out_ref.dtype)


def _epilogue(me, pieces, basis_t):
    width = basis_t.shape[0]
    cols = pieces[0].shape[-1]
    in_specs = [pl.BlockSpec(basis_t.shape, lambda i, m: (0, 0))]
    for piece in pieces:
        if piece.ndim == 3:
            in_specs.append(pl.BlockSpec((None,) + piece.shape[1:], lambda i, m: (m[0], 0, 0)))
        else:
            in_specs.append(pl.BlockSpec(piece.shape, lambda i, m: (0, 0)))
    grid_spec = pltpu.PrefetchScalarGridSpec(
        num_scalar_prefetch=1,
        grid=(1,),
        in_specs=in_specs,
        out_specs=pl.BlockSpec((width, cols), lambda i, m: (0, 0)),
    )
    return pl.pallas_call(
        _epilogue_kernel,
        grid_spec=grid_spec,
        out_shape=jax.ShapeDtypeStruct((width, cols), jnp.bfloat16),
    )(me, basis_t, *pieces)


def _line_gather(payload, axis):
    n = lax.axis_size(axis)
    if n <= 2:
        far_up = far_down = None
    else:
        far_up = lax.ppermute(payload, axis, [(0, n - 1)])
        far_down = lax.ppermute(payload, axis, [(n - 1, 0)])
    ups, downs = [], []
    up, down = payload, payload
    for step in range(n - 1 if far_up is None else n - 2):
        up_pairs = [(i, i + 1) for i in range(step, n - 1)]
        down_pairs = [(i + 1, i) for i in range(n - 1 - step)]
        up = lax.ppermute(up, axis, up_pairs)
        down = lax.ppermute(down, axis, down_pairs)
        ups.append(up)
        downs.append(down)
    if far_up is not None:
        ups.append(far_up)
        downs.append(far_down)
    return jnp.stack(ups[::-1] + [payload] + downs)


def _ring_reduce_scatter(blocks, axis):
    n = lax.axis_size(axis)
    if n == 1:
        return blocks[0]
    me = lax.axis_index(axis)
    ring = [(i, (i + 1) % n) for i in range(n)]
    carry = lax.dynamic_index_in_dim(blocks, jnp.mod(me - 1, n), 0, False)
    for step in range(n - 1):
        arrived = lax.ppermute(carry.astype(jnp.bfloat16), axis, ring)
        own = lax.dynamic_index_in_dim(blocks, jnp.mod(me - 2 - step, n), 0, False)
        carry = arrived.astype(jnp.float32) + own
    return carry


def on_device(density, cluster_basis, near_blocks, near_pairs, near_count, coupling):
    width = cluster_basis.shape[2]
    rank_size = cluster_basis.shape[1]
    rhs_count = density.shape[1]
    tgt_count = lax.axis_size("tgt")
    inner_count = lax.axis_size(("inner", "sub"))
    assert lax.axis_size("sub") == 2 and 2 * width == rhs_count and rank_size % 2 == 0
    basis = cluster_basis[0]
    half_rank = rank_size // 2
    packed = jnp.concatenate([basis[:half_rank], basis[half_rank:]], axis=1)
    payload = jnp.concatenate([density, packed], axis=0)
    stack = _line_gather(payload, "tgt")

    pair_list = near_pairs[0, 0]
    live_count = near_count[0, 0]
    slot_count = pair_list.shape[0]
    flat_pairs = pair_list[:, 0] * tgt_count + pair_list[:, 1]
    live_slots = jnp.arange(slot_count) < live_count
    hit_table = (flat_pairs[:, None] == jnp.arange(inner_count * tgt_count)[None, :]) & live_slots[
        :, None
    ]
    keep_mask = (
        (1.0 - jnp.any(hit_table, axis=0).astype(jnp.float32))
        .reshape(inner_count, 1, tgt_count, 1)
        .astype(jnp.bfloat16)
    )
    masked = coupling[0, 0].reshape(inner_count, rank_size, tgt_count, rank_size) * keep_mask
    masked_t = masked.transpose(2, 0, 1, 3).reshape(tgt_count, inner_count * rank_size, rank_size)

    place = jnp.stack([lax.axis_index("tgt"), lax.axis_index("sub")]).astype(jnp.int32)
    mine, theirs = _near_far(
        pair_list.reshape(-1), live_count.reshape(1), place, near_blocks[0, 0], stack, masked_t,
        inner_count, rank_size,
    )
    arrived = lax.ppermute(theirs, "sub", [(0, 1), (1, 0)])
    basis_t = cluster_basis[0].T
    me = lax.axis_index("inner")
    if lax.axis_size("inner") == 2:
        send = (
            lax.dynamic_index_in_dim(mine, 1 - me, 0, False).astype(jnp.float32)
            + lax.dynamic_index_in_dim(arrived, 1 - me, 0, False).astype(jnp.float32)
        ).astype(jnp.bfloat16)
        back = lax.ppermute(send, "inner", [(0, 1), (1, 0)])
        pieces = (mine, arrived, back)
    else:
        stage = mine.astype(jnp.float32) + arrived.astype(jnp.float32)
        pieces = (_ring_reduce_scatter(stage, "inner"),)
    width = basis_t.shape[0]
    total = None
    for piece in pieces:
        if piece.ndim == 3:
            piece = lax.dynamic_index_in_dim(piece, me, 0, False)
        piece = piece.astype(jnp.float32)
        total = piece if total is None else total + piece
    far = jnp.dot(basis_t, total[width:].astype(jnp.bfloat16), preferred_element_type=jnp.float32)
    return (total[:width] + far).astype(jnp.bfloat16)


def solution(mesh):
    in_specs = (
        P(("tgt", "inner", "sub"), "groups"),
        P(("groups", "tgt", "inner", "sub"), None, None),
        P(("groups", "tgt"), ("inner", "sub"), None, None, None),
        P(("groups", "tgt"), ("inner", "sub"), None, None),
        P(("groups", "tgt"), ("inner", "sub")),
        P(("groups", "tgt"), ("inner", "sub"), None, None),
    )
    out_specs = P(("tgt", "inner", "sub"), "groups")
    return jax.shard_map(
        on_device, mesh=mesh, in_specs=in_specs, out_specs=out_specs, check_vma=False
    )
```

```python
import jax
import jax.numpy as jnp
from jax import lax
from jax.experimental import pallas as pl
from jax.experimental.pallas import tpu as pltpu
from jax.sharding import PartitionSpec as P


def _near_far_kernel(
    pairs_ref, count_ref, place_ref, tiles_ref, stack_ref, masked_ref, mine_ref, theirs_ref, acc_ref
):
    inner_count, width, rhs_count = acc_ref.shape
    slot_count = tiles_ref.shape[0]
    tgt_count = masked_ref.shape[0]
    rank_size = masked_ref.shape[2]
    sub_count = 2
    own_tgt = place_ref[0]
    own_sub = place_ref[1]
    acc_ref[...] = jnp.zeros_like(acc_ref)

    def add_slot(slot, carry):
        target = jnp.clip(pairs_ref[2 * slot], 0, inner_count - 1)
        source = jnp.clip(pairs_ref[2 * slot + 1], 0, tgt_count - 1)
        term = jnp.dot(
            tiles_ref[slot],
            stack_ref[source - own_tgt + tgt_count - 1, :width, :],
            preferred_element_type=jnp.float32,
        )
        acc_ref[target] += term
        return carry

    lax.fori_loop(0, jnp.clip(count_ref[0], 0, slot_count), add_slot, 0)

    coeffs = jnp.zeros((inner_count * rank_size, rhs_count), jnp.float32)
    for source in range(tgt_count):
        block = stack_ref[source - own_tgt + tgt_count - 1]
        dens = block[:width, :]
        packed = block[width:, :]
        top = jnp.dot(packed[:, :width], dens, preferred_element_type=jnp.float32)
        bottom = jnp.dot(packed[:, width:], dens, preferred_element_type=jnp.float32)
        projected = jnp.concatenate([top, bottom], axis=0).astype(jnp.bfloat16)
        coeffs += jnp.dot(masked_ref[source], projected, preferred_element_type=jnp.float32)
    coeffs = coeffs.astype(jnp.bfloat16)

    def write(first_ref, second_ref):
        for target in range(inner_count):
            dest = first_ref if target % sub_count == 0 else second_ref
            row = target // sub_count
            dest[row, :width, :] = acc_ref[target].astype(dest.dtype)
            dest[row, width:, :] = coeffs[target * rank_size : (target + 1) * rank_size]

    @pl.when(own_sub == 0)
    def _():
        write(mine_ref, theirs_ref)

    @pl.when(own_sub != 0)
    def _():
        write(theirs_ref, mine_ref)


def _near_far(pairs_flat, count, place, tiles, stack, masked_t, inner_count, rank_size):
    slot_count, width, _ = tiles.shape
    stack_count, rows, rhs_count = stack.shape
    half_count = inner_count // 2
    out_rows = width + rank_size
    smem = pl.BlockSpec(memory_space=pltpu.MemorySpace.SMEM)
    vmem = pl.BlockSpec(memory_space=pltpu.MemorySpace.VMEM)
    out = jax.ShapeDtypeStruct((half_count, out_rows, rhs_count), jnp.bfloat16)
    vmem_bytes = (
        tiles.size * tiles.dtype.itemsize
        + stack.size * stack.dtype.itemsize
        + masked_t.size * masked_t.dtype.itemsize
        + 2 * half_count * out_rows * rhs_count * 2
        + inner_count * width * rhs_count * 4
        + (4 << 20)
    )
    return pl.pallas_call(
        _near_far_kernel,
        in_specs=[smem, smem, smem, vmem, vmem, vmem],
        out_specs=[vmem, vmem],
        out_shape=[out, out],
        scratch_shapes=[pltpu.VMEM((inner_count, width, rhs_count), jnp.float32)],
        compiler_params=pltpu.CompilerParams(vmem_limit_bytes=int(vmem_bytes)),
    )(pairs_flat, count, place, tiles, stack, masked_t)


def _epilogue_kernel(me_ref, basis_t_ref, *refs):
    piece_refs, out_ref = refs[:-1], refs[-1]
    width = out_ref.shape[0]
    total = piece_refs[0][...].astype(jnp.float32)
    for piece_ref in piece_refs[1:]:
        total += piece_ref[...].astype(jnp.float32)
    coeffs = total[width:, :].astype(jnp.bfloat16)
    far = jnp.dot(basis_t_ref[...], coeffs, preferred_element_type=jnp.float32)
    out_ref[...] = (total[:width, :] + far).astype(out_ref.dtype)


def _epilogue(me, pieces, basis_t):
    width = basis_t.shape[0]
    cols = pieces[0].shape[-1]
    in_specs = [pl.BlockSpec(basis_t.shape, lambda i, m: (0, 0))]
    for piece in pieces:
        if piece.ndim == 3:
            in_specs.append(pl.BlockSpec((None,) + piece.shape[1:], lambda i, m: (m[0], 0, 0)))
        else:
            in_specs.append(pl.BlockSpec(piece.shape, lambda i, m: (0, 0)))
    grid_spec = pltpu.PrefetchScalarGridSpec(
        num_scalar_prefetch=1,
        grid=(1,),
        in_specs=in_specs,
        out_specs=pl.BlockSpec((width, cols), lambda i, m: (0, 0)),
    )
    return pl.pallas_call(
        _epilogue_kernel,
        grid_spec=grid_spec,
        out_shape=jax.ShapeDtypeStruct((width, cols), jnp.bfloat16),
    )(me, basis_t, *pieces)


def _line_gather(payload, axis):
    n = lax.axis_size(axis)
    if n <= 2:
        far_up = far_down = None
    else:
        far_up = lax.ppermute(payload, axis, [(0, n - 1)])
        far_down = lax.ppermute(payload, axis, [(n - 1, 0)])
    ups, downs = [], []
    up, down = payload, payload
    for step in range(n - 1 if far_up is None else n - 2):
        up_pairs = [(i, i + 1) for i in range(step, n - 1)]
        down_pairs = [(i + 1, i) for i in range(n - 1 - step)]
        up = lax.ppermute(up, axis, up_pairs)
        down = lax.ppermute(down, axis, down_pairs)
        ups.append(up)
        downs.append(down)
    if far_up is not None:
        ups.append(far_up)
        downs.append(far_down)
    return jnp.stack(ups[::-1] + [payload] + downs)


def _ring_reduce_scatter(blocks, axis):
    n = lax.axis_size(axis)
    if n == 1:
        return blocks[0]
    me = lax.axis_index(axis)
    ring = [(i, (i + 1) % n) for i in range(n)]
    carry = lax.dynamic_index_in_dim(blocks, jnp.mod(me - 1, n), 0, False)
    for step in range(n - 1):
        arrived = lax.ppermute(carry.astype(jnp.bfloat16), axis, ring)
        own = lax.dynamic_index_in_dim(blocks, jnp.mod(me - 2 - step, n), 0, False)
        carry = arrived.astype(jnp.float32) + own
    return carry


def on_device(density, cluster_basis, near_blocks, near_pairs, near_count, coupling):
    width = cluster_basis.shape[2]
    rank_size = cluster_basis.shape[1]
    rhs_count = density.shape[1]
    tgt_count = lax.axis_size("tgt")
    inner_count = lax.axis_size(("inner", "sub"))
    assert lax.axis_size("sub") == 2 and 2 * width == rhs_count and rank_size % 2 == 0
    basis = cluster_basis[0]
    half_rank = rank_size // 2
    packed = basis.reshape(half_rank, 2 * width)
    payload = jnp.concatenate([density, packed], axis=0)
    stack = _line_gather(payload, "tgt")

    pair_list = near_pairs[0, 0]
    live_count = near_count[0, 0]
    slot_count = pair_list.shape[0]
    flat_pairs = pair_list[:, 0] * tgt_count + pair_list[:, 1]
    live_slots = jnp.arange(slot_count) < live_count
    hit_table = (flat_pairs[:, None] == jnp.arange(inner_count * tgt_count)[None, :]) & live_slots[
        :, None
    ]
    keep_mask = (
        (1.0 - jnp.any(hit_table, axis=0).astype(jnp.float32))
        .reshape(inner_count, 1, tgt_count, 1)
        .astype(jnp.bfloat16)
    )
    masked = coupling[0, 0].reshape(inner_count, rank_size, tgt_count, rank_size) * keep_mask
    masked_t = masked.transpose(2, 0, 1, 3).reshape(tgt_count, inner_count * rank_size, rank_size)
    rank_order = jnp.concatenate([jnp.arange(0, rank_size, 2), jnp.arange(1, rank_size, 2)])
    masked_t = masked_t[:, :, rank_order]

    place = jnp.stack([lax.axis_index("tgt"), lax.axis_index("sub")]).astype(jnp.int32)
    mine, theirs = _near_far(
        pair_list.reshape(-1), live_count.reshape(1), place, near_blocks[0, 0], stack, masked_t,
        inner_count, rank_size,
    )
    arrived = lax.ppermute(theirs, "sub", [(0, 1), (1, 0)])
    basis_t = cluster_basis[0].T
    me = lax.axis_index("inner")
    if lax.axis_size("inner") == 2:
        send = (
            lax.dynamic_index_in_dim(mine, 1 - me, 0, False).astype(jnp.float32)
            + lax.dynamic_index_in_dim(arrived, 1 - me, 0, False).astype(jnp.float32)
        ).astype(jnp.bfloat16)
        back = lax.ppermute(send, "inner", [(0, 1), (1, 0)])
        pieces = (mine, arrived, back)
    else:
        stage = mine.astype(jnp.float32) + arrived.astype(jnp.float32)
        pieces = (_ring_reduce_scatter(stage, "inner"),)
    width = basis_t.shape[0]
    total = None
    for piece in pieces:
        if piece.ndim == 3:
            piece = lax.dynamic_index_in_dim(piece, me, 0, False)
        piece = piece.astype(jnp.float32)
        total = piece if total is None else total + piece
    far = jnp.dot(basis_t, total[width:].astype(jnp.bfloat16), preferred_element_type=jnp.float32)
    return (total[:width] + far).astype(jnp.bfloat16)


def solution(mesh):
    in_specs = (
        P(("tgt", "inner", "sub"), "groups"),
        P(("groups", "tgt", "inner", "sub"), None, None),
        P(("groups", "tgt"), ("inner", "sub"), None, None, None),
        P(("groups", "tgt"), ("inner", "sub"), None, None),
        P(("groups", "tgt"), ("inner", "sub")),
        P(("groups", "tgt"), ("inner", "sub"), None, None),
    )
    out_specs = P(("tgt", "inner", "sub"), "groups")
    return jax.shard_map(
        on_device, mesh=mesh, in_specs=in_specs, out_specs=out_specs, check_vma=False
    )
```

```python
import jax
import jax.numpy as jnp
from jax import lax
from jax.experimental import pallas as pl
from jax.experimental.pallas import tpu as pltpu
from jax.sharding import PartitionSpec as P


def _near_far_kernel(
    pairs_ref, count_ref, place_ref, tiles_ref, stack_ref, masked_ref, mine_ref, theirs_ref, acc_ref
):
    inner_count, width, rhs_count = acc_ref.shape
    slot_count = tiles_ref.shape[0]
    tgt_count = masked_ref.shape[0]
    rank_size = masked_ref.shape[2]
    sub_count = 2
    own_tgt = place_ref[0]
    own_sub = place_ref[1]
    acc_ref[...] = jnp.zeros_like(acc_ref)

    def add_slot(slot, carry):
        target = jnp.clip(pairs_ref[2 * slot], 0, inner_count - 1)
        source = jnp.clip(pairs_ref[2 * slot + 1], 0, tgt_count - 1)
        term = jnp.dot(
            tiles_ref[slot],
            stack_ref[source - own_tgt + tgt_count - 1, :width, :],
            preferred_element_type=jnp.float32,
        )
        acc_ref[target] += term
        return carry

    lax.fori_loop(0, jnp.clip(count_ref[0], 0, slot_count), add_slot, 0)

    coeffs = jnp.zeros((inner_count * rank_size, rhs_count), jnp.float32)
    for source in range(tgt_count):
        block = stack_ref[source - own_tgt + tgt_count - 1]
        dens = block[:width, :]
        packed = block[width:, :]
        top = jnp.dot(packed[:, :width], dens, preferred_element_type=jnp.float32)
        bottom = jnp.dot(packed[:, width:], dens, preferred_element_type=jnp.float32)
        projected = jnp.concatenate([top, bottom], axis=0).astype(jnp.bfloat16)
        coeffs += jnp.dot(masked_ref[source], projected, preferred_element_type=jnp.float32)
    coeffs = coeffs.astype(jnp.bfloat16)

    def write(first_ref, second_ref):
        for target in range(inner_count):
            dest = first_ref if target % sub_count == 0 else second_ref
            row = target // sub_count
            dest[row, :width, :] = acc_ref[target].astype(dest.dtype)
            dest[row, width:, :] = coeffs[target * rank_size : (target + 1) * rank_size]

    @pl.when(own_sub == 0)
    def _():
        write(mine_ref, theirs_ref)

    @pl.when(own_sub != 0)
    def _():
        write(theirs_ref, mine_ref)


def _near_far(pairs_flat, count, place, tiles, stack, masked_t, inner_count, rank_size):
    slot_count, width, _ = tiles.shape
    stack_count, rows, rhs_count = stack.shape
    half_count = inner_count // 2
    out_rows = width + rank_size
    whole = lambda k, p, c, q: (0, 0, 0)
    grid_spec = pltpu.PrefetchScalarGridSpec(
        num_scalar_prefetch=3,
        grid=(1,),
        in_specs=[
            pl.BlockSpec(tiles.shape, whole),
            pl.BlockSpec(stack.shape, whole),
            pl.BlockSpec(masked_t.shape, whole),
        ],
        out_specs=[
            pl.BlockSpec((half_count, out_rows, rhs_count), whole),
            pl.BlockSpec((half_count, out_rows, rhs_count), whole),
        ],
        scratch_shapes=[pltpu.VMEM((inner_count, width, rhs_count), jnp.float32)],
    )
    out = jax.ShapeDtypeStruct((half_count, out_rows, rhs_count), jnp.bfloat16)
    block_bytes = 2 * (
        tiles.size * tiles.dtype.itemsize
        + stack.size * stack.dtype.itemsize
        + masked_t.size * masked_t.dtype.itemsize
        + 2 * half_count * out_rows * rhs_count * 2
    )
    vmem_bytes = block_bytes + inner_count * width * rhs_count * 4 + (4 << 20)
    return pl.pallas_call(
        _near_far_kernel,
        grid_spec=grid_spec,
        out_shape=[out, out],
        compiler_params=pltpu.CompilerParams(
            dimension_semantics=("arbitrary",), vmem_limit_bytes=int(vmem_bytes)
        ),
    )(pairs_flat, count, place, tiles, stack, masked_t)


def _epilogue_kernel(me_ref, basis_t_ref, *refs):
    piece_refs, out_ref = refs[:-1], refs[-1]
    width = out_ref.shape[0]
    total = piece_refs[0][...].astype(jnp.float32)
    for piece_ref in piece_refs[1:]:
        total += piece_ref[...].astype(jnp.float32)
    coeffs = total[width:, :].astype(jnp.bfloat16)
    far = jnp.dot(basis_t_ref[...], coeffs, preferred_element_type=jnp.float32)
    out_ref[...] = (total[:width, :] + far).astype(out_ref.dtype)


def _epilogue(me, pieces, basis_t):
    width = basis_t.shape[0]
    cols = pieces[0].shape[-1]
    in_specs = [pl.BlockSpec(basis_t.shape, lambda i, m: (0, 0))]
    for piece in pieces:
        if piece.ndim == 3:
            in_specs.append(pl.BlockSpec((None,) + piece.shape[1:], lambda i, m: (m[0], 0, 0)))
        else:
            in_specs.append(pl.BlockSpec(piece.shape, lambda i, m: (0, 0)))
    grid_spec = pltpu.PrefetchScalarGridSpec(
        num_scalar_prefetch=1,
        grid=(1,),
        in_specs=in_specs,
        out_specs=pl.BlockSpec((width, cols), lambda i, m: (0, 0)),
    )
    return pl.pallas_call(
        _epilogue_kernel,
        grid_spec=grid_spec,
        out_shape=jax.ShapeDtypeStruct((width, cols), jnp.bfloat16),
    )(me, basis_t, *pieces)


def _line_gather(payload, axis):
    n = lax.axis_size(axis)
    if n <= 2:
        far_up = far_down = None
    else:
        far_up = lax.ppermute(payload, axis, [(0, n - 1)])
        far_down = lax.ppermute(payload, axis, [(n - 1, 0)])
    ups, downs = [], []
    up, down = payload, payload
    for step in range(n - 1 if far_up is None else n - 2):
        up_pairs = [(i, i + 1) for i in range(step, n - 1)]
        down_pairs = [(i + 1, i) for i in range(n - 1 - step)]
        up = lax.ppermute(up, axis, up_pairs)
        down = lax.ppermute(down, axis, down_pairs)
        ups.append(up)
        downs.append(down)
    if far_up is not None:
        ups.append(far_up)
        downs.append(far_down)
    return jnp.stack(ups[::-1] + [payload] + downs)


def _ring_reduce_scatter(blocks, axis):
    n = lax.axis_size(axis)
    if n == 1:
        return blocks[0]
    me = lax.axis_index(axis)
    ring = [(i, (i + 1) % n) for i in range(n)]
    carry = lax.dynamic_index_in_dim(blocks, jnp.mod(me - 1, n), 0, False)
    for step in range(n - 1):
        arrived = lax.ppermute(carry.astype(jnp.bfloat16), axis, ring)
        own = lax.dynamic_index_in_dim(blocks, jnp.mod(me - 2 - step, n), 0, False)
        carry = arrived.astype(jnp.float32) + own
    return carry


def on_device(density, cluster_basis, near_blocks, near_pairs, near_count, coupling):
    width = cluster_basis.shape[2]
    rank_size = cluster_basis.shape[1]
    rhs_count = density.shape[1]
    tgt_count = lax.axis_size("tgt")
    inner_count = lax.axis_size(("inner", "sub"))
    assert lax.axis_size("sub") == 2 and 2 * width == rhs_count and rank_size % 2 == 0
    basis = cluster_basis[0]
    half_rank = rank_size // 2
    packed = jnp.concatenate([basis[:half_rank], basis[half_rank:]], axis=1)
    payload = jnp.concatenate([density, packed], axis=0)
    stack = _line_gather(payload, "tgt")

    pair_list = near_pairs[0, 0]
    live_count = near_count[0, 0]
    slot_count = pair_list.shape[0]
    flat_pairs = pair_list[:, 0] * tgt_count + pair_list[:, 1]
    live_slots = jnp.arange(slot_count) < live_count
    hit_table = (flat_pairs[:, None] == jnp.arange(inner_count * tgt_count)[None, :]) & live_slots[
        :, None
    ]
    keep_mask = (
        (1.0 - jnp.any(hit_table, axis=0).astype(jnp.float32))
        .reshape(inner_count, 1, tgt_count, 1)
        .astype(jnp.bfloat16)
    )
    masked = coupling[0, 0].reshape(inner_count, rank_size, tgt_count, rank_size) * keep_mask
    masked_t = masked.transpose(2, 0, 1, 3).reshape(tgt_count, inner_count * rank_size, rank_size)

    place = jnp.stack([lax.axis_index("tgt"), lax.axis_index("sub")]).astype(jnp.int32)
    mine, theirs = _near_far(
        pair_list.reshape(-1), live_count.reshape(1), place, near_blocks[0, 0], stack, masked_t,
        inner_count, rank_size,
    )
    basis_t = cluster_basis[0].T
    me = lax.axis_index("inner")
    swap = [(0, 1), (1, 0)]
    if lax.axis_size("inner") == 2:
        onward = lax.ppermute(lax.dynamic_index_in_dim(theirs, 1 - me, 0, False), "sub", swap)
        send = (
            lax.dynamic_index_in_dim(mine, 1 - me, 0, False).astype(jnp.float32)
            + onward.astype(jnp.float32)
        ).astype(jnp.bfloat16)
        back = lax.ppermute(send, "inner", swap)
        keep_src = lax.optimization_barrier((lax.dynamic_index_in_dim(theirs, me, 0, False), send))[0]
        kept = lax.ppermute(keep_src, "sub", swap)
        pieces = (mine, kept, back)
    else:
        arrived = lax.ppermute(theirs, "sub", swap)
        stage = mine.astype(jnp.float32) + arrived.astype(jnp.float32)
        pieces = (_ring_reduce_scatter(stage, "inner"),)
    width = basis_t.shape[0]
    total = None
    for piece in pieces:
        if piece.ndim == 3:
            piece = lax.dynamic_index_in_dim(piece, me, 0, False)
        piece = piece.astype(jnp.float32)
        total = piece if total is None else total + piece
    far = jnp.dot(basis_t, total[width:].astype(jnp.bfloat16), preferred_element_type=jnp.float32)
    return (total[:width] + far).astype(jnp.bfloat16)


def solution(mesh):
    in_specs = (
        P(("tgt", "inner", "sub"), "groups"),
        P(("groups", "tgt", "inner", "sub"), None, None),
        P(("groups", "tgt"), ("inner", "sub"), None, None, None),
        P(("groups", "tgt"), ("inner", "sub"), None, None),
        P(("groups", "tgt"), ("inner", "sub")),
        P(("groups", "tgt"), ("inner", "sub"), None, None),
    )
    out_specs = P(("tgt", "inner", "sub"), "groups")
    return jax.shard_map(
        on_device, mesh=mesh, in_specs=in_specs, out_specs=out_specs, check_vma=False
    )
```

```python
import jax
import jax.numpy as jnp
from jax import lax
from jax.experimental import pallas as pl
from jax.experimental.pallas import tpu as pltpu
from jax.sharding import PartitionSpec as P


def _near_far_kernel(
    pairs_ref,
    count_ref,
    place_ref,
    tiles_ref,
    stack_ref,
    basis_ref,
    masked_ref,
    mine_ref,
    theirs_ref,
    acc_ref,
):
    inner_count, width, rhs_count = acc_ref.shape
    slot_count = tiles_ref.shape[0]
    tgt_count = masked_ref.shape[0]
    rank_size = masked_ref.shape[2]
    sub_count = 2
    own_tgt = place_ref[0]
    own_sub = place_ref[1]
    acc_ref[...] = jnp.zeros_like(acc_ref)

    def add_slot(slot, carry):
        target = jnp.clip(pairs_ref[2 * slot], 0, inner_count - 1)
        source = jnp.clip(pairs_ref[2 * slot + 1], 0, tgt_count - 1)
        term = jnp.dot(
            tiles_ref[slot],
            stack_ref[source - own_tgt + tgt_count - 1, :width, :],
            preferred_element_type=jnp.float32,
        )
        acc_ref[target] += term
        return carry

    lax.fori_loop(0, jnp.clip(count_ref[0], 0, slot_count), add_slot, 0)

    coeffs = jnp.zeros((inner_count * rank_size, rhs_count), jnp.float32)
    for source in range(tgt_count):
        offset = source - own_tgt + tgt_count - 1
        projected = jnp.dot(
            basis_ref[offset], stack_ref[offset, :width, :], preferred_element_type=jnp.float32
        ).astype(jnp.bfloat16)
        coeffs += jnp.dot(masked_ref[source], projected, preferred_element_type=jnp.float32)
    coeffs = coeffs.astype(jnp.bfloat16)

    def write(first_ref, second_ref):
        for target in range(inner_count):
            dest = first_ref if target % sub_count == 0 else second_ref
            row = target // sub_count
            dest[row, :width, :] = acc_ref[target].astype(dest.dtype)
            dest[row, width:, :] = coeffs[target * rank_size : (target + 1) * rank_size]

    @pl.when(own_sub == 0)
    def _():
        write(mine_ref, theirs_ref)

    @pl.when(own_sub != 0)
    def _():
        write(theirs_ref, mine_ref)


def _near_far(pairs_flat, count, place, tiles, stack, basis_src, masked_t, inner_count, rank_size):
    slot_count, width, _ = tiles.shape
    stack_count, rows, rhs_count = stack.shape
    half_count = inner_count // 2
    out_rows = width + rank_size
    whole = lambda k, p, c, q: (0, 0, 0)
    grid_spec = pltpu.PrefetchScalarGridSpec(
        num_scalar_prefetch=3,
        grid=(1,),
        in_specs=[
            pl.BlockSpec(tiles.shape, whole),
            pl.BlockSpec((stack_count, width, rhs_count), whole),
            pl.BlockSpec(
                (stack_count, rank_size, width), lambda k, p, c, q: (0, width // rank_size, 0)
            ),
            pl.BlockSpec(masked_t.shape, whole),
        ],
        out_specs=[
            pl.BlockSpec((half_count, out_rows, rhs_count), whole),
            pl.BlockSpec((half_count, out_rows, rhs_count), whole),
        ],
        scratch_shapes=[pltpu.VMEM((inner_count, width, rhs_count), jnp.float32)],
    )
    out = jax.ShapeDtypeStruct((half_count, out_rows, rhs_count), jnp.bfloat16)
    block_bytes = 2 * 2 * (
        tiles.size
        + stack_count * width * rhs_count
        + stack_count * rank_size * width
        + masked_t.size
        + 2 * half_count * out_rows * rhs_count
    )
    vmem_bytes = block_bytes + inner_count * width * rhs_count * 4 + (4 << 20)
    return pl.pallas_call(
        _near_far_kernel,
        grid_spec=grid_spec,
        out_shape=[out, out],
        compiler_params=pltpu.CompilerParams(
            dimension_semantics=("arbitrary",), vmem_limit_bytes=int(vmem_bytes)
        ),
    )(pairs_flat, count, place, tiles, stack, basis_src, masked_t)


def _epilogue_kernel(me_ref, basis_t_ref, *refs):
    piece_refs, out_ref = refs[:-1], refs[-1]
    width = out_ref.shape[0]
    total = piece_refs[0][...].astype(jnp.float32)
    for piece_ref in piece_refs[1:]:
        total += piece_ref[...].astype(jnp.float32)
    coeffs = total[width:, :].astype(jnp.bfloat16)
    far = jnp.dot(basis_t_ref[...], coeffs, preferred_element_type=jnp.float32)
    out_ref[...] = (total[:width, :] + far).astype(out_ref.dtype)


def _epilogue(me, pieces, basis_t):
    width = basis_t.shape[0]
    cols = pieces[0].shape[-1]
    in_specs = [pl.BlockSpec(basis_t.shape, lambda i, m: (0, 0))]
    for piece in pieces:
        if piece.ndim == 3:
            in_specs.append(pl.BlockSpec((None,) + piece.shape[1:], lambda i, m: (m[0], 0, 0)))
        else:
            in_specs.append(pl.BlockSpec(piece.shape, lambda i, m: (0, 0)))
    grid_spec = pltpu.PrefetchScalarGridSpec(
        num_scalar_prefetch=1,
        grid=(1,),
        in_specs=in_specs,
        out_specs=pl.BlockSpec((width, cols), lambda i, m: (0, 0)),
    )
    return pl.pallas_call(
        _epilogue_kernel,
        grid_spec=grid_spec,
        out_shape=jax.ShapeDtypeStruct((width, cols), jnp.bfloat16),
    )(me, basis_t, *pieces)


def _line_gather(payload, axis, ties=()):
    n = lax.axis_size(axis)
    if ties:
        payload = lax.optimization_barrier((payload,) + tuple(ties[0]))[0]
    if n <= 2:
        far_up = far_down = None
    else:
        far_up = lax.ppermute(payload, axis, [(0, n - 1)])
        far_down = lax.ppermute(payload, axis, [(n - 1, 0)])
    ups, downs = [], []
    up, down = payload, payload
    for step in range(n - 1 if far_up is None else n - 2):
        if 0 < step < len(ties):
            up, down = lax.optimization_barrier((up, down) + tuple(ties[step]))[:2]
        up_pairs = [(i, i + 1) for i in range(step, n - 1)]
        down_pairs = [(i + 1, i) for i in range(n - 1 - step)]
        up = lax.ppermute(up, axis, up_pairs)
        down = lax.ppermute(down, axis, down_pairs)
        ups.append(up)
        downs.append(down)
    if far_up is not None:
        ups.append(far_up)
        downs.append(far_down)
    last = tuple(x for x in (up, down, far_up, far_down) if x is not None)
    return jnp.stack(ups[::-1] + [payload] + downs), last


def _ring_reduce_scatter(blocks, axis):
    n = lax.axis_size(axis)
    if n == 1:
        return blocks[0]
    me = lax.axis_index(axis)
    ring = [(i, (i + 1) % n) for i in range(n)]
    carry = lax.dynamic_index_in_dim(blocks, jnp.mod(me - 1, n), 0, False)
    for step in range(n - 1):
        arrived = lax.ppermute(carry.astype(jnp.bfloat16), axis, ring)
        own = lax.dynamic_index_in_dim(blocks, jnp.mod(me - 2 - step, n), 0, False)
        carry = arrived.astype(jnp.float32) + own
    return carry


def on_device(density, cluster_basis, near_blocks, near_pairs, near_count, coupling):
    width = cluster_basis.shape[2]
    rank_size = cluster_basis.shape[1]
    rhs_count = density.shape[1]
    tgt_count = lax.axis_size("tgt")
    inner_count = lax.axis_size(("inner", "sub"))
    assert lax.axis_size("sub") == 2 and 2 * width == rhs_count and rank_size % 2 == 0
    basis = cluster_basis[0]
    chunk_count = 2
    cols = rhs_count // chunk_count

    pair_list = near_pairs[0, 0]
    live_count = near_count[0, 0]
    slot_count = pair_list.shape[0]
    flat_pairs = pair_list[:, 0] * tgt_count + pair_list[:, 1]
    live_slots = jnp.arange(slot_count) < live_count
    hit_table = (flat_pairs[:, None] == jnp.arange(inner_count * tgt_count)[None, :]) & live_slots[
        :, None
    ]
    keep_mask = (
        (1.0 - jnp.any(hit_table, axis=0).astype(jnp.float32))
        .reshape(inner_count, 1, tgt_count, 1)
        .astype(jnp.bfloat16)
    )
    masked = coupling[0, 0].reshape(inner_count, rank_size, tgt_count, rank_size) * keep_mask
    masked_t = masked.transpose(2, 0, 1, 3).reshape(tgt_count, inner_count * rank_size, rank_size)
    place = jnp.stack([lax.axis_index("tgt"), lax.axis_index("sub")]).astype(jnp.int32)
    basis_t = basis.T
    me = lax.axis_index("inner")
    swap = [(0, 1), (1, 0)]

    outs = []
    basis_src = None
    previous = None
    for chunk in range(chunk_count):
        piece = density[:, chunk * cols : (chunk + 1) * cols]
        if chunk == 0:
            stack, last_round = _line_gather(jnp.concatenate([piece, basis], axis=0), "tgt")
            basis_src = stack
        else:
            stack, last_round = _line_gather(piece, "tgt", (previous[0], previous[1]))
            stack = lax.optimization_barrier((stack, previous[2]))[0]
        mine, theirs = _near_far(
            pair_list.reshape(-1), live_count.reshape(1), place, near_blocks[0, 0], stack,
            basis_src, masked_t, inner_count, rank_size,
        )
        arrived = lax.ppermute(theirs, "sub", swap)
        if lax.axis_size("inner") == 2:
            send = (
                lax.dynamic_index_in_dim(mine, 1 - me, 0, False).astype(jnp.float32)
                + lax.dynamic_index_in_dim(arrived, 1 - me, 0, False).astype(jnp.float32)
            ).astype(jnp.bfloat16)
            back = lax.ppermute(send, "inner", swap)
            pieces = (mine, arrived, back)
            reduced, onward = back, send
        else:
            stage = mine.astype(jnp.float32) + arrived.astype(jnp.float32)
            pieces = (_ring_reduce_scatter(stage, "inner"),)
            reduced, onward = pieces[0], stage
        previous = (tuple(last_round), (onward,), reduced)
        total = None
        for part in pieces:
            if part.ndim == 3:
                part = lax.dynamic_index_in_dim(part, me, 0, False)
            part = part.astype(jnp.float32)
            total = part if total is None else total + part
        far = jnp.dot(
            basis_t, total[width:].astype(jnp.bfloat16), preferred_element_type=jnp.float32
        )
        outs.append((total[:width] + far).astype(jnp.bfloat16))
    return jnp.concatenate(outs, axis=1)


def solution(mesh):
    in_specs = (
        P(("tgt", "inner", "sub"), "groups"),
        P(("groups", "tgt", "inner", "sub"), None, None),
        P(("groups", "tgt"), ("inner", "sub"), None, None, None),
        P(("groups", "tgt"), ("inner", "sub"), None, None),
        P(("groups", "tgt"), ("inner", "sub")),
        P(("groups", "tgt"), ("inner", "sub"), None, None),
    )
    out_specs = P(("tgt", "inner", "sub"), "groups")
    return jax.shard_map(
        on_device, mesh=mesh, in_specs=in_specs, out_specs=out_specs, check_vma=False
    )
```

```python
import jax
import jax.numpy as jnp
from jax import lax
from jax.experimental import pallas as pl
from jax.experimental.pallas import tpu as pltpu
from jax.sharding import PartitionSpec as P


def _near_far_kernel(
    pairs_ref,
    count_ref,
    place_ref,
    tiles_ref,
    stack_ref,
    packed_ref,
    masked_ref,
    mine_ref,
    theirs_ref,
    acc_ref,
):
    inner_count, width, rhs_count = acc_ref.shape
    slot_count = tiles_ref.shape[0]
    tgt_count = masked_ref.shape[0]
    rank_size = masked_ref.shape[2]
    sub_count = 2
    own_tgt = place_ref[0]
    own_sub = place_ref[1]
    acc_ref[...] = jnp.zeros_like(acc_ref)

    def add_slot(slot, carry):
        target = jnp.clip(pairs_ref[2 * slot], 0, inner_count - 1)
        source = jnp.clip(pairs_ref[2 * slot + 1], 0, tgt_count - 1)
        term = jnp.dot(
            tiles_ref[slot],
            stack_ref[source - own_tgt + tgt_count - 1, :width, :],
            preferred_element_type=jnp.float32,
        )
        acc_ref[target] += term
        return carry

    lax.fori_loop(0, jnp.clip(count_ref[0], 0, slot_count), add_slot, 0)

    coeffs = jnp.zeros((inner_count * rank_size, rhs_count), jnp.float32)
    for source in range(tgt_count):
        offset = source - own_tgt + tgt_count - 1
        dens = stack_ref[offset]
        packed = packed_ref[offset]
        top = jnp.dot(packed[:, :width], dens, preferred_element_type=jnp.float32)
        bottom = jnp.dot(packed[:, width:], dens, preferred_element_type=jnp.float32)
        projected = jnp.concatenate([top, bottom], axis=0).astype(jnp.bfloat16)
        coeffs += jnp.dot(masked_ref[source], projected, preferred_element_type=jnp.float32)
    coeffs = coeffs.astype(jnp.bfloat16)

    def write(first_ref, second_ref):
        for target in range(inner_count):
            dest = first_ref if target % sub_count == 0 else second_ref
            row = target // sub_count
            dest[row, :width, :] = acc_ref[target].astype(dest.dtype)
            dest[row, width:, :] = coeffs[target * rank_size : (target + 1) * rank_size]

    @pl.when(own_sub == 0)
    def _():
        write(mine_ref, theirs_ref)

    @pl.when(own_sub != 0)
    def _():
        write(theirs_ref, mine_ref)


def _near_far(pairs_flat, count, place, tiles, stack, packed, masked_t, inner_count, rank_size):
    slot_count, width, _ = tiles.shape
    stack_count, rows, rhs_count = stack.shape
    half_count = inner_count // 2
    out_rows = width + rank_size
    whole = lambda k, p, c, q: (0, 0, 0)
    grid_spec = pltpu.PrefetchScalarGridSpec(
        num_scalar_prefetch=3,
        grid=(1,),
        in_specs=[
            pl.BlockSpec(tiles.shape, whole),
            pl.BlockSpec(stack.shape, whole),
            pl.BlockSpec(packed.shape, whole),
            pl.BlockSpec(masked_t.shape, whole),
        ],
        out_specs=[
            pl.BlockSpec((half_count, out_rows, rhs_count), whole),
            pl.BlockSpec((half_count, out_rows, rhs_count), whole),
        ],
        scratch_shapes=[pltpu.VMEM((inner_count, width, rhs_count), jnp.float32)],
    )
    out = jax.ShapeDtypeStruct((half_count, out_rows, rhs_count), jnp.bfloat16)
    block_bytes = 2 * (
        tiles.size * tiles.dtype.itemsize
        + stack.size * stack.dtype.itemsize
        + packed.size * packed.dtype.itemsize
        + masked_t.size * masked_t.dtype.itemsize
        + 2 * half_count * out_rows * rhs_count * 2
    )
    vmem_bytes = block_bytes + inner_count * width * rhs_count * 4 + (4 << 20)
    return pl.pallas_call(
        _near_far_kernel,
        grid_spec=grid_spec,
        out_shape=[out, out],
        compiler_params=pltpu.CompilerParams(
            dimension_semantics=("arbitrary",), vmem_limit_bytes=int(vmem_bytes)
        ),
    )(pairs_flat, count, place, tiles, stack, packed, masked_t)


def _epilogue_kernel(me_ref, basis_t_ref, *refs):
    piece_refs, out_ref = refs[:-1], refs[-1]
    width = out_ref.shape[0]
    total = piece_refs[0][...].astype(jnp.float32)
    for piece_ref in piece_refs[1:]:
        total += piece_ref[...].astype(jnp.float32)
    coeffs = total[width:, :].astype(jnp.bfloat16)
    far = jnp.dot(basis_t_ref[...], coeffs, preferred_element_type=jnp.float32)
    out_ref[...] = (total[:width, :] + far).astype(out_ref.dtype)


def _epilogue(me, pieces, basis_t):
    width = basis_t.shape[0]
    cols = pieces[0].shape[-1]
    in_specs = [pl.BlockSpec(basis_t.shape, lambda i, m: (0, 0))]
    for piece in pieces:
        if piece.ndim == 3:
            in_specs.append(pl.BlockSpec((None,) + piece.shape[1:], lambda i, m: (m[0], 0, 0)))
        else:
            in_specs.append(pl.BlockSpec(piece.shape, lambda i, m: (0, 0)))
    grid_spec = pltpu.PrefetchScalarGridSpec(
        num_scalar_prefetch=1,
        grid=(1,),
        in_specs=in_specs,
        out_specs=pl.BlockSpec((width, cols), lambda i, m: (0, 0)),
    )
    return pl.pallas_call(
        _epilogue_kernel,
        grid_spec=grid_spec,
        out_shape=jax.ShapeDtypeStruct((width, cols), jnp.bfloat16),
    )(me, basis_t, *pieces)


def _line_gather(payload, axis):
    n = lax.axis_size(axis)
    if n <= 2:
        far_up = far_down = None
    else:
        far_up = lax.ppermute(payload, axis, [(0, n - 1)])
        far_down = lax.ppermute(payload, axis, [(n - 1, 0)])
    ups, downs = [], []
    up, down = payload, payload
    for step in range(n - 1 if far_up is None else n - 2):
        up_pairs = [(i, i + 1) for i in range(step, n - 1)]
        down_pairs = [(i + 1, i) for i in range(n - 1 - step)]
        up = lax.ppermute(up, axis, up_pairs)
        down = lax.ppermute(down, axis, down_pairs)
        ups.append(up)
        downs.append(down)
    if far_up is not None:
        ups.append(far_up)
        downs.append(far_down)
    order = ups[::-1] + [payload] + downs
    return tuple(jnp.stack(parts) for parts in zip(*order))


def _ring_reduce_scatter(blocks, axis):
    n = lax.axis_size(axis)
    if n == 1:
        return blocks[0]
    me = lax.axis_index(axis)
    ring = [(i, (i + 1) % n) for i in range(n)]
    carry = lax.dynamic_index_in_dim(blocks, jnp.mod(me - 1, n), 0, False)
    for step in range(n - 1):
        arrived = lax.ppermute(carry.astype(jnp.bfloat16), axis, ring)
        own = lax.dynamic_index_in_dim(blocks, jnp.mod(me - 2 - step, n), 0, False)
        carry = arrived.astype(jnp.float32) + own
    return carry


def on_device(density, cluster_basis, near_blocks, near_pairs, near_count, coupling):
    width = cluster_basis.shape[2]
    rank_size = cluster_basis.shape[1]
    rhs_count = density.shape[1]
    tgt_count = lax.axis_size("tgt")
    inner_count = lax.axis_size(("inner", "sub"))
    assert lax.axis_size("sub") == 2 and 2 * width == rhs_count and rank_size % 2 == 0
    basis = cluster_basis[0]
    half_rank = rank_size // 2
    packed = jnp.concatenate([basis[:half_rank], basis[half_rank:]], axis=1)
    stack, packed_stack = _line_gather((density, packed), "tgt")

    pair_list = near_pairs[0, 0]
    live_count = near_count[0, 0]
    slot_count = pair_list.shape[0]
    flat_pairs = pair_list[:, 0] * tgt_count + pair_list[:, 1]
    live_slots = jnp.arange(slot_count) < live_count
    hit_table = (flat_pairs[:, None] == jnp.arange(inner_count * tgt_count)[None, :]) & live_slots[
        :, None
    ]
    keep_mask = (
        (1.0 - jnp.any(hit_table, axis=0).astype(jnp.float32))
        .reshape(inner_count, 1, tgt_count, 1)
        .astype(jnp.bfloat16)
    )
    masked = coupling[0, 0].reshape(inner_count, rank_size, tgt_count, rank_size) * keep_mask
    masked_t = masked.transpose(2, 0, 1, 3).reshape(tgt_count, inner_count * rank_size, rank_size)

    place = jnp.stack([lax.axis_index("tgt"), lax.axis_index("sub")]).astype(jnp.int32)
    mine, theirs = _near_far(
        pair_list.reshape(-1), live_count.reshape(1), place, near_blocks[0, 0], stack, packed_stack,
        masked_t,
        inner_count, rank_size,
    )
    arrived = lax.ppermute(theirs, "sub", [(0, 1), (1, 0)])
    basis_t = cluster_basis[0].T
    me = lax.axis_index("inner")
    if lax.axis_size("inner") == 2:
        send = (
            lax.dynamic_index_in_dim(mine, 1 - me, 0, False).astype(jnp.float32)
            + lax.dynamic_index_in_dim(arrived, 1 - me, 0, False).astype(jnp.float32)
        ).astype(jnp.bfloat16)
        back = lax.ppermute(send, "inner", [(0, 1), (1, 0)])
        pieces = (mine, arrived, back)
    else:
        stage = mine.astype(jnp.float32) + arrived.astype(jnp.float32)
        pieces = (_ring_reduce_scatter(stage, "inner"),)
    width = basis_t.shape[0]
    total = None
    for piece in pieces:
        if piece.ndim == 3:
            piece = lax.dynamic_index_in_dim(piece, me, 0, False)
        piece = piece.astype(jnp.float32)
        total = piece if total is None else total + piece
    far = jnp.dot(basis_t, total[width:].astype(jnp.bfloat16), preferred_element_type=jnp.float32)
    return (total[:width] + far).astype(jnp.bfloat16)


def solution(mesh):
    in_specs = (
        P(("tgt", "inner", "sub"), "groups"),
        P(("groups", "tgt", "inner", "sub"), None, None),
        P(("groups", "tgt"), ("inner", "sub"), None, None, None),
        P(("groups", "tgt"), ("inner", "sub"), None, None),
        P(("groups", "tgt"), ("inner", "sub")),
        P(("groups", "tgt"), ("inner", "sub"), None, None),
    )
    out_specs = P(("tgt", "inner", "sub"), "groups")
    return jax.shard_map(
        on_device, mesh=mesh, in_specs=in_specs, out_specs=out_specs, check_vma=False
    )
```

```python
import jax
import jax.numpy as jnp
from jax import lax
from jax.experimental import pallas as pl
from jax.experimental.pallas import tpu as pltpu
from jax.sharding import PartitionSpec as P


def _near_far_kernel(
    pairs_ref, count_ref, place_ref, tiles_ref, stack_ref, masked_ref, mine_ref, theirs_ref, acc_ref
):
    inner_count, width, rhs_count = acc_ref.shape
    slot_count = tiles_ref.shape[0]
    tgt_count = masked_ref.shape[0]
    rank_size = masked_ref.shape[2]
    sub_count = 2
    own_tgt = place_ref[0]
    own_sub = place_ref[1]
    acc_ref[...] = jnp.zeros_like(acc_ref)

    def add_slot(slot, carry):
        target = jnp.clip(pairs_ref[2 * slot], 0, inner_count - 1)
        source = jnp.clip(pairs_ref[2 * slot + 1], 0, tgt_count - 1)
        term = jnp.dot(
            tiles_ref[slot],
            stack_ref[source - own_tgt + tgt_count - 1, :width, :],
            preferred_element_type=jnp.float32,
        )
        acc_ref[target] += term
        return carry

    lax.fori_loop(0, jnp.clip(count_ref[0], 0, slot_count), add_slot, 0)

    coeffs = jnp.zeros((inner_count * rank_size, rhs_count), jnp.float32)
    for source in range(tgt_count):
        block = stack_ref[source - own_tgt + tgt_count - 1]
        dens = block[:width, :]
        packed = block[width:, :]
        top = jnp.dot(packed[:, :width], dens, preferred_element_type=jnp.float32)
        bottom = jnp.dot(packed[:, width:], dens, preferred_element_type=jnp.float32)
        projected = jnp.concatenate([top, bottom], axis=0).astype(jnp.bfloat16)
        coeffs += jnp.dot(masked_ref[source], projected, preferred_element_type=jnp.float32)
    coeffs = coeffs.astype(jnp.bfloat16)

    def write(first_ref, second_ref):
        for target in range(inner_count):
            dest = first_ref if target % sub_count == 0 else second_ref
            row = target // sub_count
            dest[row, :width, :] = acc_ref[target].astype(dest.dtype)
            dest[row, width:, :] = coeffs[target * rank_size : (target + 1) * rank_size]

    @pl.when(own_sub == 0)
    def _():
        write(mine_ref, theirs_ref)

    @pl.when(own_sub != 0)
    def _():
        write(theirs_ref, mine_ref)


def _near_far(pairs_flat, count, place, tiles, stack, masked_t, inner_count, rank_size):
    slot_count, width, _ = tiles.shape
    stack_count, rows, rhs_count = stack.shape
    half_count = inner_count // 2
    out_rows = width + rank_size
    whole = lambda k, p, c, q: (0, 0, 0)
    grid_spec = pltpu.PrefetchScalarGridSpec(
        num_scalar_prefetch=3,
        grid=(1,),
        in_specs=[
            pl.BlockSpec(tiles.shape, whole),
            pl.BlockSpec(stack.shape, whole),
            pl.BlockSpec(masked_t.shape, whole),
        ],
        out_specs=[
            pl.BlockSpec((half_count, out_rows, rhs_count), whole),
            pl.BlockSpec((half_count, out_rows, rhs_count), whole),
        ],
        scratch_shapes=[pltpu.VMEM((inner_count, width, rhs_count), jnp.float32)],
    )
    out = jax.ShapeDtypeStruct((half_count, out_rows, rhs_count), jnp.bfloat16)
    block_bytes = 2 * (
        tiles.size * tiles.dtype.itemsize
        + stack.size * stack.dtype.itemsize
        + masked_t.size * masked_t.dtype.itemsize
        + 2 * half_count * out_rows * rhs_count * 2
    )
    vmem_bytes = block_bytes + inner_count * width * rhs_count * 4 + (4 << 20)
    return pl.pallas_call(
        _near_far_kernel,
        grid_spec=grid_spec,
        out_shape=[out, out],
        compiler_params=pltpu.CompilerParams(
            dimension_semantics=("arbitrary",), vmem_limit_bytes=int(vmem_bytes)
        ),
    )(pairs_flat, count, place, tiles, stack, masked_t)


def _epilogue_kernel(me_ref, basis_t_ref, *refs):
    piece_refs, out_ref = refs[:-1], refs[-1]
    width = out_ref.shape[0]
    total = piece_refs[0][...].astype(jnp.float32)
    for piece_ref in piece_refs[1:]:
        total += piece_ref[...].astype(jnp.float32)
    coeffs = total[width:, :].astype(jnp.bfloat16)
    far = jnp.dot(basis_t_ref[...], coeffs, preferred_element_type=jnp.float32)
    out_ref[...] = (total[:width, :] + far).astype(out_ref.dtype)


def _epilogue(me, pieces, basis_t):
    width = basis_t.shape[0]
    cols = pieces[0].shape[-1]
    in_specs = [pl.BlockSpec(basis_t.shape, lambda i, m: (0, 0))]
    for piece in pieces:
        if piece.ndim == 3:
            in_specs.append(pl.BlockSpec((None,) + piece.shape[1:], lambda i, m: (m[0], 0, 0)))
        else:
            in_specs.append(pl.BlockSpec(piece.shape, lambda i, m: (0, 0)))
    grid_spec = pltpu.PrefetchScalarGridSpec(
        num_scalar_prefetch=1,
        grid=(1,),
        in_specs=in_specs,
        out_specs=pl.BlockSpec((width, cols), lambda i, m: (0, 0)),
    )
    return pl.pallas_call(
        _epilogue_kernel,
        grid_spec=grid_spec,
        out_shape=jax.ShapeDtypeStruct((width, cols), jnp.bfloat16),
    )(me, basis_t, *pieces)


def _line_gather(payload, axis):
    n = lax.axis_size(axis)
    if n == 1:
        return payload[None]
    first_up = lax.ppermute(payload, axis, [(i, (i + 1) % n) for i in range(n)])
    first_down = lax.ppermute(payload, axis, [(i, (i - 1) % n) for i in range(n)])
    ups, downs = [first_up], [first_down]
    up, down = first_up, first_down
    for step in range(1, n - 2):
        up_pairs = [(i, i + 1) for i in range(step, n - 1)]
        down_pairs = [(i + 1, i) for i in range(n - 1 - step)]
        up = lax.ppermute(up, axis, up_pairs)
        down = lax.ppermute(down, axis, down_pairs)
        ups.append(up)
        downs.append(down)
    if n > 2:
        ups.append(first_down)
        downs.append(first_up)
    return jnp.stack(ups[::-1] + [payload] + downs)


def _ring_reduce_scatter(blocks, axis):
    n = lax.axis_size(axis)
    if n == 1:
        return blocks[0]
    me = lax.axis_index(axis)
    ring = [(i, (i + 1) % n) for i in range(n)]
    carry = lax.dynamic_index_in_dim(blocks, jnp.mod(me - 1, n), 0, False)
    for step in range(n - 1):
        arrived = lax.ppermute(carry.astype(jnp.bfloat16), axis, ring)
        own = lax.dynamic_index_in_dim(blocks, jnp.mod(me - 2 - step, n), 0, False)
        carry = arrived.astype(jnp.float32) + own
    return carry


def on_device(density, cluster_basis, near_blocks, near_pairs, near_count, coupling):
    width = cluster_basis.shape[2]
    rank_size = cluster_basis.shape[1]
    rhs_count = density.shape[1]
    tgt_count = lax.axis_size("tgt")
    inner_count = lax.axis_size(("inner", "sub"))
    assert lax.axis_size("sub") == 2 and 2 * width == rhs_count and rank_size % 2 == 0
    basis = cluster_basis[0]
    half_rank = rank_size // 2
    packed = jnp.concatenate([basis[:half_rank], basis[half_rank:]], axis=1)
    payload = jnp.concatenate([density, packed], axis=0)
    stack = _line_gather(payload, "tgt")

    pair_list = near_pairs[0, 0]
    live_count = near_count[0, 0]
    slot_count = pair_list.shape[0]
    flat_pairs = pair_list[:, 0] * tgt_count + pair_list[:, 1]
    live_slots = jnp.arange(slot_count) < live_count
    hit_table = (flat_pairs[:, None] == jnp.arange(inner_count * tgt_count)[None, :]) & live_slots[
        :, None
    ]
    keep_mask = (
        (1.0 - jnp.any(hit_table, axis=0).astype(jnp.float32))
        .reshape(inner_count, 1, tgt_count, 1)
        .astype(jnp.bfloat16)
    )
    masked = coupling[0, 0].reshape(inner_count, rank_size, tgt_count, rank_size) * keep_mask
    masked_t = masked.transpose(2, 0, 1, 3).reshape(tgt_count, inner_count * rank_size, rank_size)

    place = jnp.stack([lax.axis_index("tgt"), lax.axis_index("sub")]).astype(jnp.int32)
    mine, theirs = _near_far(
        pair_list.reshape(-1), live_count.reshape(1), place, near_blocks[0, 0], stack, masked_t,
        inner_count, rank_size,
    )
    arrived = lax.ppermute(theirs, "sub", [(0, 1), (1, 0)])
    basis_t = cluster_basis[0].T
    me = lax.axis_index("inner")
    if lax.axis_size("inner") == 2:
        send = (
            lax.dynamic_index_in_dim(mine, 1 - me, 0, False).astype(jnp.float32)
            + lax.dynamic_index_in_dim(arrived, 1 - me, 0, False).astype(jnp.float32)
        ).astype(jnp.bfloat16)
        back = lax.ppermute(send, "inner", [(0, 1), (1, 0)])
        pieces = (mine, arrived, back)
    else:
        stage = mine.astype(jnp.float32) + arrived.astype(jnp.float32)
        pieces = (_ring_reduce_scatter(stage, "inner"),)
    width = basis_t.shape[0]
    total = None
    for piece in pieces:
        if piece.ndim == 3:
            piece = lax.dynamic_index_in_dim(piece, me, 0, False)
        piece = piece.astype(jnp.float32)
        total = piece if total is None else total + piece
    far = jnp.dot(basis_t, total[width:].astype(jnp.bfloat16), preferred_element_type=jnp.float32)
    return (total[:width] + far).astype(jnp.bfloat16)


def solution(mesh):
    in_specs = (
        P(("tgt", "inner", "sub"), "groups"),
        P(("groups", "tgt", "inner", "sub"), None, None),
        P(("groups", "tgt"), ("inner", "sub"), None, None, None),
        P(("groups", "tgt"), ("inner", "sub"), None, None),
        P(("groups", "tgt"), ("inner", "sub")),
        P(("groups", "tgt"), ("inner", "sub"), None, None),
    )
    out_specs = P(("tgt", "inner", "sub"), "groups")
    return jax.shard_map(
        on_device, mesh=mesh, in_specs=in_specs, out_specs=out_specs, check_vma=False
    )
```

```python
import jax
import jax.numpy as jnp
from jax import lax
from jax.experimental import pallas as pl
from jax.experimental.pallas import tpu as pltpu
from jax.sharding import PartitionSpec as P


def _near_far_kernel(
    pairs_ref, count_ref, place_ref, tiles_ref, stack_ref, masked_ref, mine_ref, theirs_ref, acc_ref
):
    inner_count, width, rhs_count = acc_ref.shape
    slot_count = tiles_ref.shape[0]
    tgt_count = masked_ref.shape[0]
    rank_size = masked_ref.shape[2]
    sub_count = 2
    own_tgt = place_ref[0]
    own_sub = place_ref[1]
    acc_ref[...] = jnp.zeros_like(acc_ref)

    def add_slot(slot, carry):
        target = jnp.clip(pairs_ref[2 * slot], 0, inner_count - 1)
        source = jnp.clip(pairs_ref[2 * slot + 1], 0, tgt_count - 1)
        term = jnp.dot(
            tiles_ref[slot],
            stack_ref[source - own_tgt + tgt_count - 1, :width, :],
            preferred_element_type=jnp.float32,
        )
        acc_ref[target] += term
        return carry

    lax.fori_loop(0, jnp.clip(count_ref[0], 0, slot_count), add_slot, 0)

    coeffs = jnp.zeros((inner_count * rank_size, rhs_count), jnp.float32)
    for source in range(tgt_count):
        block = stack_ref[source - own_tgt + tgt_count - 1]
        dens = block[:width, :]
        packed = block[width:, :]
        top = jnp.dot(packed[:, :width], dens, preferred_element_type=jnp.float32)
        bottom = jnp.dot(packed[:, width:], dens, preferred_element_type=jnp.float32)
        projected = jnp.concatenate([top, bottom], axis=0).astype(jnp.bfloat16)
        coeffs += jnp.dot(masked_ref[source], projected, preferred_element_type=jnp.float32)
    coeffs = coeffs.astype(jnp.bfloat16)

    def write(first_ref, second_ref):
        for target in range(inner_count):
            dest = first_ref if target % sub_count == 0 else second_ref
            row = target // sub_count
            dest[row, :width, :] = acc_ref[target].astype(dest.dtype)
            dest[row, width:, :] = coeffs[target * rank_size : (target + 1) * rank_size]

    @pl.when(own_sub == 0)
    def _():
        write(mine_ref, theirs_ref)

    @pl.when(own_sub != 0)
    def _():
        write(theirs_ref, mine_ref)


def _near_far(pairs_flat, count, place, tiles, stack, masked_t, inner_count, rank_size):
    slot_count, width, _ = tiles.shape
    stack_count, rows, rhs_count = stack.shape
    half_count = inner_count // 2
    out_rows = width + rank_size
    whole = lambda k, p, c, q: (0, 0, 0)
    grid_spec = pltpu.PrefetchScalarGridSpec(
        num_scalar_prefetch=3,
        grid=(1,),
        in_specs=[
            pl.BlockSpec(tiles.shape, whole),
            pl.BlockSpec(stack.shape, whole),
            pl.BlockSpec(masked_t.shape, whole),
        ],
        out_specs=[
            pl.BlockSpec((half_count, out_rows, rhs_count), whole),
            pl.BlockSpec((half_count, out_rows, rhs_count), whole),
        ],
        scratch_shapes=[pltpu.VMEM((inner_count, width, rhs_count), jnp.float32)],
    )
    out = jax.ShapeDtypeStruct((half_count, out_rows, rhs_count), jnp.bfloat16)
    block_bytes = 2 * (
        tiles.size * tiles.dtype.itemsize
        + stack.size * stack.dtype.itemsize
        + masked_t.size * masked_t.dtype.itemsize
        + 2 * half_count * out_rows * rhs_count * 2
    )
    vmem_bytes = block_bytes + inner_count * width * rhs_count * 4 + (4 << 20)
    return pl.pallas_call(
        _near_far_kernel,
        grid_spec=grid_spec,
        out_shape=[out, out],
        compiler_params=pltpu.CompilerParams(
            dimension_semantics=("arbitrary",), vmem_limit_bytes=int(vmem_bytes)
        ),
    )(pairs_flat, count, place, tiles, stack, masked_t)


def _epilogue_kernel(me_ref, basis_t_ref, *refs):
    piece_refs, out_ref = refs[:-1], refs[-1]
    width = out_ref.shape[0]
    total = piece_refs[0][...].astype(jnp.float32)
    for piece_ref in piece_refs[1:]:
        total += piece_ref[...].astype(jnp.float32)
    coeffs = total[width:, :].astype(jnp.bfloat16)
    far = jnp.dot(basis_t_ref[...], coeffs, preferred_element_type=jnp.float32)
    out_ref[...] = (total[:width, :] + far).astype(out_ref.dtype)


def _epilogue(me, pieces, basis_t):
    width = basis_t.shape[0]
    cols = pieces[0].shape[-1]
    in_specs = [pl.BlockSpec(basis_t.shape, lambda i, m: (0, 0))]
    for piece in pieces:
        if piece.ndim == 3:
            in_specs.append(pl.BlockSpec((None,) + piece.shape[1:], lambda i, m: (m[0], 0, 0)))
        else:
            in_specs.append(pl.BlockSpec(piece.shape, lambda i, m: (0, 0)))
    grid_spec = pltpu.PrefetchScalarGridSpec(
        num_scalar_prefetch=1,
        grid=(1,),
        in_specs=in_specs,
        out_specs=pl.BlockSpec((width, cols), lambda i, m: (0, 0)),
    )
    return pl.pallas_call(
        _epilogue_kernel,
        grid_spec=grid_spec,
        out_shape=jax.ShapeDtypeStruct((width, cols), jnp.bfloat16),
    )(me, basis_t, *pieces)


def _line_gather(payload, axis):
    n = lax.axis_size(axis)
    if n == 1:
        return payload[None]
    first_up = lax.ppermute(payload, axis, [(i, (i + 1) % n) for i in range(n)])
    first_down = lax.ppermute(payload, axis, [(i, (i - 1) % n) for i in range(n)])
    ups, downs = [first_up], [first_down]
    up, down = first_up, first_down
    for step in range(1, n - 2):
        up_pairs = [(i, i + 1) for i in range(step, n - 1)]
        down_pairs = [(i + 1, i) for i in range(n - 1 - step)]
        up = lax.ppermute(up, axis, up_pairs)
        down = lax.ppermute(down, axis, down_pairs)
        ups.append(up)
        downs.append(down)
    if n > 2:
        ups.append(first_down)
        downs.append(first_up)
    return jnp.stack(ups[::-1] + [payload] + downs)


def _ring_reduce_scatter(blocks, axis):
    n = lax.axis_size(axis)
    if n == 1:
        return blocks[0]
    me = lax.axis_index(axis)
    ring = [(i, (i + 1) % n) for i in range(n)]
    carry = lax.dynamic_index_in_dim(blocks, jnp.mod(me - 1, n), 0, False)
    for step in range(n - 1):
        arrived = lax.ppermute(carry.astype(jnp.bfloat16), axis, ring)
        own = lax.dynamic_index_in_dim(blocks, jnp.mod(me - 2 - step, n), 0, False)
        carry = arrived.astype(jnp.float32) + own
    return carry


def on_device(density, cluster_basis, near_blocks, near_pairs, near_count, coupling):
    width = cluster_basis.shape[2]
    rank_size = cluster_basis.shape[1]
    rhs_count = density.shape[1]
    tgt_count = lax.axis_size("tgt")
    inner_count = lax.axis_size(("inner", "sub"))
    assert lax.axis_size("sub") == 2 and 2 * width == rhs_count and rank_size % 2 == 0
    basis = cluster_basis[0]
    half_rank = rank_size // 2
    packed = jnp.concatenate([basis[:half_rank], basis[half_rank:]], axis=1)
    payload = jnp.concatenate([density, packed], axis=0)
    stack = _line_gather(payload, "tgt")

    pair_list = near_pairs[0, 0]
    live_count = near_count[0, 0]
    slot_count = pair_list.shape[0]
    flat_pairs = pair_list[:, 0] * tgt_count + pair_list[:, 1]
    live_slots = jnp.arange(slot_count) < live_count
    hit_table = (flat_pairs[:, None] == jnp.arange(inner_count * tgt_count)[None, :]) & live_slots[
        :, None
    ]
    keep_mask = (
        (1.0 - jnp.any(hit_table, axis=0).astype(jnp.float32))
        .reshape(inner_count, 1, tgt_count, 1)
        .astype(jnp.bfloat16)
    )
    masked = coupling[0, 0].reshape(inner_count, rank_size, tgt_count, rank_size) * keep_mask
    masked_t = masked.transpose(2, 0, 1, 3).reshape(tgt_count, inner_count * rank_size, rank_size)

    place = jnp.stack([lax.axis_index("tgt"), lax.axis_index("sub")]).astype(jnp.int32)
    mine, theirs = _near_far(
        pair_list.reshape(-1), live_count.reshape(1), place, near_blocks[0, 0], stack, masked_t,
        inner_count, rank_size,
    )
    basis_t = cluster_basis[0].T
    me = lax.axis_index("inner")
    swap = [(0, 1), (1, 0)]
    if lax.axis_size("inner") == 2:
        onward = lax.ppermute(lax.dynamic_index_in_dim(theirs, 1 - me, 0, False), "sub", swap)
        send = (
            lax.dynamic_index_in_dim(mine, 1 - me, 0, False).astype(jnp.float32)
            + onward.astype(jnp.float32)
        ).astype(jnp.bfloat16)
        back = lax.ppermute(send, "inner", swap)
        keep_src = lax.optimization_barrier((lax.dynamic_index_in_dim(theirs, me, 0, False), send))[0]
        kept = lax.ppermute(keep_src, "sub", swap)
        pieces = (mine, kept, back)
    else:
        arrived = lax.ppermute(theirs, "sub", swap)
        stage = mine.astype(jnp.float32) + arrived.astype(jnp.float32)
        pieces = (_ring_reduce_scatter(stage, "inner"),)
    width = basis_t.shape[0]
    total = None
    for piece in pieces:
        if piece.ndim == 3:
            piece = lax.dynamic_index_in_dim(piece, me, 0, False)
        piece = piece.astype(jnp.float32)
        total = piece if total is None else total + piece
    far = jnp.dot(basis_t, total[width:].astype(jnp.bfloat16), preferred_element_type=jnp.float32)
    return (total[:width] + far).astype(jnp.bfloat16)


def solution(mesh):
    in_specs = (
        P(("tgt", "inner", "sub"), "groups"),
        P(("groups", "tgt", "inner", "sub"), None, None),
        P(("groups", "tgt"), ("inner", "sub"), None, None, None),
        P(("groups", "tgt"), ("inner", "sub"), None, None),
        P(("groups", "tgt"), ("inner", "sub")),
        P(("groups", "tgt"), ("inner", "sub"), None, None),
    )
    out_specs = P(("tgt", "inner", "sub"), "groups")
    return jax.shard_map(
        on_device, mesh=mesh, in_specs=in_specs, out_specs=out_specs, check_vma=False
    )
```

```python
import jax
import jax.numpy as jnp
from jax import lax
from jax.experimental import pallas as pl
from jax.experimental.pallas import tpu as pltpu
from jax.sharding import PartitionSpec as P


def _early(offset, tgt_count):
    return (offset == 0) | (jnp.abs(offset) == 1) | (jnp.abs(offset) == tgt_count - 1)


def _partial_kernel(late, pairs_ref, count_ref, place_ref, tiles_ref, stack_ref, masked_ref, *refs):
    inner_count, width, rhs_count = tiles_ref.shape[1], tiles_ref.shape[1], stack_ref.shape[2]
    slot_count = tiles_ref.shape[0]
    tgt_count = masked_ref.shape[0]
    rank_size = masked_ref.shape[2]
    sub_count = 2
    own_tgt = place_ref[0]
    own_sub = place_ref[1]
    if late:
        acc_in, coeff_in, mine_ref, theirs_ref, acc_ref, coeff_ref = refs
        inner_count = acc_in.shape[0]
        acc_ref[...] = acc_in[...]
        coeff_ref[...] = coeff_in[...]
    else:
        acc_ref, coeff_ref = refs
        inner_count = acc_ref.shape[0]
        acc_ref[...] = jnp.zeros_like(acc_ref)
        coeff_ref[...] = jnp.zeros_like(coeff_ref)

    def add_slot(slot, carry):
        target = jnp.clip(pairs_ref[2 * slot], 0, inner_count - 1)
        source = jnp.clip(pairs_ref[2 * slot + 1], 0, tgt_count - 1)
        offset = source - own_tgt
        wanted = jnp.logical_not(_early(offset, tgt_count)) if late else _early(offset, tgt_count)

        @pl.when(wanted)
        def _():
            term = jnp.dot(
                tiles_ref[slot],
                stack_ref[offset + tgt_count - 1, :width, :],
                preferred_element_type=jnp.float32,
            )
            acc_ref[target] += term

        return carry

    lax.fori_loop(0, jnp.clip(count_ref[0], 0, slot_count), add_slot, 0)

    for source in range(tgt_count):
        offset = source - own_tgt
        wanted = jnp.logical_not(_early(offset, tgt_count)) if late else _early(offset, tgt_count)

        @pl.when(wanted)
        def _():
            block = stack_ref[offset + tgt_count - 1]
            dens = block[:width, :]
            packed = block[width:, :]
            top = jnp.dot(packed[:, :width], dens, preferred_element_type=jnp.float32)
            bottom = jnp.dot(packed[:, width:], dens, preferred_element_type=jnp.float32)
            projected = jnp.concatenate([top, bottom], axis=0).astype(jnp.bfloat16)
            coeff_ref[...] += jnp.dot(
                masked_ref[source], projected, preferred_element_type=jnp.float32
            )

    if late:
        coeffs = coeff_ref[...].astype(jnp.bfloat16)

        def write(first_ref, second_ref):
            for target in range(inner_count):
                dest = first_ref if target % sub_count == 0 else second_ref
                row = target // sub_count
                dest[row, :width, :] = acc_ref[target].astype(dest.dtype)
                dest[row, width:, :] = coeffs[target * rank_size : (target + 1) * rank_size]

        @pl.when(own_sub == 0)
        def _():
            write(mine_ref, theirs_ref)

        @pl.when(own_sub != 0)
        def _():
            write(theirs_ref, mine_ref)


def _near_far(pairs_flat, count, place, tiles, early_stack, stack, masked_t, inner_count, rank_size):
    slot_count, width, _ = tiles.shape
    stack_count, rows, rhs_count = early_stack.shape
    half_count = inner_count // 2
    out_rows = width + rank_size
    whole = lambda k, p, c, q: (0, 0, 0)
    acc_shape = (inner_count, width, rhs_count)
    coeff_shape = (inner_count * rank_size, rhs_count)
    base_specs = [
        pl.BlockSpec(tiles.shape, whole),
        pl.BlockSpec(early_stack.shape, whole),
        pl.BlockSpec(masked_t.shape, whole),
    ]
    acc_spec = pl.BlockSpec(acc_shape, whole)
    coeff_spec = pl.BlockSpec(coeff_shape, lambda k, p, c, q: (0, 0))
    vmem_bytes = (
        2 * (tiles.size * 2 + early_stack.size * 2 + masked_t.size * 2 + 2 * half_count * out_rows * rhs_count * 2)
        + 6 * (inner_count * width * rhs_count * 4 + inner_count * rank_size * rhs_count * 4)
        + (4 << 20)
    )
    params = pltpu.CompilerParams(dimension_semantics=("arbitrary",), vmem_limit_bytes=int(vmem_bytes))
    acc, coeff = pl.pallas_call(
        lambda *r: _partial_kernel(False, *r),
        grid_spec=pltpu.PrefetchScalarGridSpec(
            num_scalar_prefetch=3, grid=(1,), in_specs=base_specs, out_specs=[acc_spec, coeff_spec]
        ),
        out_shape=[
            jax.ShapeDtypeStruct(acc_shape, jnp.float32),
            jax.ShapeDtypeStruct(coeff_shape, jnp.float32),
        ],
        compiler_params=params,
    )(pairs_flat, count, place, tiles, early_stack, masked_t)
    stack = jnp.stack(lax.optimization_barrier((tuple(stack), acc, coeff))[0])
    out = jax.ShapeDtypeStruct((half_count, out_rows, rhs_count), jnp.bfloat16)
    half_spec = pl.BlockSpec((half_count, out_rows, rhs_count), whole)
    return pl.pallas_call(
        lambda *r: _partial_kernel(True, *r),
        grid_spec=pltpu.PrefetchScalarGridSpec(
            num_scalar_prefetch=3,
            grid=(1,),
            in_specs=base_specs + [acc_spec, coeff_spec],
            out_specs=[half_spec, half_spec],
            scratch_shapes=[pltpu.VMEM(acc_shape, jnp.float32), pltpu.VMEM(coeff_shape, jnp.float32)],
        ),
        out_shape=[out, out],
        compiler_params=params,
    )(pairs_flat, count, place, tiles, stack, masked_t, acc, coeff)


def _epilogue_kernel(me_ref, basis_t_ref, *refs):
    piece_refs, out_ref = refs[:-1], refs[-1]
    width = out_ref.shape[0]
    total = piece_refs[0][...].astype(jnp.float32)
    for piece_ref in piece_refs[1:]:
        total += piece_ref[...].astype(jnp.float32)
    coeffs = total[width:, :].astype(jnp.bfloat16)
    far = jnp.dot(basis_t_ref[...], coeffs, preferred_element_type=jnp.float32)
    out_ref[...] = (total[:width, :] + far).astype(out_ref.dtype)


def _epilogue(me, pieces, basis_t):
    width = basis_t.shape[0]
    cols = pieces[0].shape[-1]
    in_specs = [pl.BlockSpec(basis_t.shape, lambda i, m: (0, 0))]
    for piece in pieces:
        if piece.ndim == 3:
            in_specs.append(pl.BlockSpec((None,) + piece.shape[1:], lambda i, m: (m[0], 0, 0)))
        else:
            in_specs.append(pl.BlockSpec(piece.shape, lambda i, m: (0, 0)))
    grid_spec = pltpu.PrefetchScalarGridSpec(
        num_scalar_prefetch=1,
        grid=(1,),
        in_specs=in_specs,
        out_specs=pl.BlockSpec((width, cols), lambda i, m: (0, 0)),
    )
    return pl.pallas_call(
        _epilogue_kernel,
        grid_spec=grid_spec,
        out_shape=jax.ShapeDtypeStruct((width, cols), jnp.bfloat16),
    )(me, basis_t, *pieces)


def _line_gather(payload, axis):
    n = lax.axis_size(axis)
    if n == 1:
        return payload[None], [payload]
    first_up = lax.ppermute(payload, axis, [(i, (i + 1) % n) for i in range(n)])
    first_down = lax.ppermute(payload, axis, [(i, (i - 1) % n) for i in range(n)])
    ups, downs = [first_up], [first_down]
    up, down = first_up, first_down
    for step in range(1, n - 2):
        up_pairs = [(i, i + 1) for i in range(step, n - 1)]
        down_pairs = [(i + 1, i) for i in range(n - 1 - step)]
        up = lax.ppermute(up, axis, up_pairs)
        down = lax.ppermute(down, axis, down_pairs)
        ups.append(up)
        downs.append(down)
    if n > 2:
        ups.append(first_down)
        downs.append(first_up)
    early_ups = [first_up] * (len(ups) - 1) + [first_down]
    early_downs = [first_down] * (len(downs) - 1) + [first_up]
    if n <= 2:
        early_ups, early_downs = [first_up], [first_down]
    return jnp.stack(early_ups[::-1] + [payload] + early_downs), (ups[::-1] + [payload] + downs)


def _ring_reduce_scatter(blocks, axis):
    n = lax.axis_size(axis)
    if n == 1:
        return blocks[0]
    me = lax.axis_index(axis)
    ring = [(i, (i + 1) % n) for i in range(n)]
    carry = lax.dynamic_index_in_dim(blocks, jnp.mod(me - 1, n), 0, False)
    for step in range(n - 1):
        arrived = lax.ppermute(carry.astype(jnp.bfloat16), axis, ring)
        own = lax.dynamic_index_in_dim(blocks, jnp.mod(me - 2 - step, n), 0, False)
        carry = arrived.astype(jnp.float32) + own
    return carry


def on_device(density, cluster_basis, near_blocks, near_pairs, near_count, coupling):
    width = cluster_basis.shape[2]
    rank_size = cluster_basis.shape[1]
    rhs_count = density.shape[1]
    tgt_count = lax.axis_size("tgt")
    inner_count = lax.axis_size(("inner", "sub"))
    assert lax.axis_size("sub") == 2 and 2 * width == rhs_count and rank_size % 2 == 0
    basis = cluster_basis[0]
    half_rank = rank_size // 2
    packed = jnp.concatenate([basis[:half_rank], basis[half_rank:]], axis=1)
    payload = jnp.concatenate([density, packed], axis=0)
    early_stack, stack = _line_gather(payload, "tgt")

    pair_list = near_pairs[0, 0]
    live_count = near_count[0, 0]
    slot_count = pair_list.shape[0]
    flat_pairs = pair_list[:, 0] * tgt_count + pair_list[:, 1]
    live_slots = jnp.arange(slot_count) < live_count
    hit_table = (flat_pairs[:, None] == jnp.arange(inner_count * tgt_count)[None, :]) & live_slots[
        :, None
    ]
    keep_mask = (
        (1.0 - jnp.any(hit_table, axis=0).astype(jnp.float32))
        .reshape(inner_count, 1, tgt_count, 1)
        .astype(jnp.bfloat16)
    )
    masked = coupling[0, 0].reshape(inner_count, rank_size, tgt_count, rank_size) * keep_mask
    masked_t = masked.transpose(2, 0, 1, 3).reshape(tgt_count, inner_count * rank_size, rank_size)

    place = jnp.stack([lax.axis_index("tgt"), lax.axis_index("sub")]).astype(jnp.int32)
    mine, theirs = _near_far(
        pair_list.reshape(-1), live_count.reshape(1), place, near_blocks[0, 0], early_stack, stack, masked_t,
        inner_count, rank_size,
    )
    basis_t = cluster_basis[0].T
    me = lax.axis_index("inner")
    swap = [(0, 1), (1, 0)]
    if lax.axis_size("inner") == 2:
        onward = lax.ppermute(lax.dynamic_index_in_dim(theirs, 1 - me, 0, False), "sub", swap)
        send = (
            lax.dynamic_index_in_dim(mine, 1 - me, 0, False).astype(jnp.float32)
            + onward.astype(jnp.float32)
        ).astype(jnp.bfloat16)
        back = lax.ppermute(send, "inner", swap)
        keep_src = lax.optimization_barrier((lax.dynamic_index_in_dim(theirs, me, 0, False), send))[0]
        kept = lax.ppermute(keep_src, "sub", swap)
        pieces = (mine, kept, back)
    else:
        arrived = lax.ppermute(theirs, "sub", swap)
        stage = mine.astype(jnp.float32) + arrived.astype(jnp.float32)
        pieces = (_ring_reduce_scatter(stage, "inner"),)
    width = basis_t.shape[0]
    total = None
    for piece in pieces:
        if piece.ndim == 3:
            piece = lax.dynamic_index_in_dim(piece, me, 0, False)
        piece = piece.astype(jnp.float32)
        total = piece if total is None else total + piece
    far = jnp.dot(basis_t, total[width:].astype(jnp.bfloat16), preferred_element_type=jnp.float32)
    return (total[:width] + far).astype(jnp.bfloat16)


def solution(mesh):
    in_specs = (
        P(("tgt", "inner", "sub"), "groups"),
        P(("groups", "tgt", "inner", "sub"), None, None),
        P(("groups", "tgt"), ("inner", "sub"), None, None, None),
        P(("groups", "tgt"), ("inner", "sub"), None, None),
        P(("groups", "tgt"), ("inner", "sub")),
        P(("groups", "tgt"), ("inner", "sub"), None, None),
    )
    out_specs = P(("tgt", "inner", "sub"), "groups")
    return jax.shard_map(
        on_device, mesh=mesh, in_specs=in_specs, out_specs=out_specs, check_vma=False
    )
```

```python
import jax
import jax.numpy as jnp
from jax import lax
from jax.experimental import pallas as pl
from jax.experimental.pallas import tpu as pltpu
from jax.sharding import PartitionSpec as P


def _early(offset, tgt_count):
    return (offset == 0) | (jnp.abs(offset) == 1) | (jnp.abs(offset) == tgt_count - 1)


def _partial_kernel(late, pairs_ref, count_ref, place_ref, tiles_ref, stack_ref, masked_ref, *refs):
    inner_count, width, rhs_count = tiles_ref.shape[1], tiles_ref.shape[1], stack_ref.shape[2]
    slot_count = tiles_ref.shape[0]
    tgt_count = masked_ref.shape[0]
    rank_size = masked_ref.shape[2]
    sub_count = 2
    own_tgt = place_ref[0]
    own_sub = place_ref[1]
    stack_count = stack_ref.shape[0]

    def stack_index(offset):
        if not late:
            return offset + tgt_count - 1
        place = jnp.where(offset < 0, tgt_count - 2 + offset, offset + tgt_count - 5)
        return jnp.clip(place, 0, stack_count - 1)

    if late:
        acc_in, coeff_in, mine_ref, theirs_ref, acc_ref, coeff_ref = refs
        inner_count = acc_in.shape[0]
        acc_ref[...] = acc_in[...]
        coeff_ref[...] = coeff_in[...]
    else:
        acc_ref, coeff_ref = refs
        inner_count = acc_ref.shape[0]
        acc_ref[...] = jnp.zeros_like(acc_ref)
        coeff_ref[...] = jnp.zeros_like(coeff_ref)

    def add_slot(slot, carry):
        target = jnp.clip(pairs_ref[2 * slot], 0, inner_count - 1)
        source = jnp.clip(pairs_ref[2 * slot + 1], 0, tgt_count - 1)
        offset = source - own_tgt
        wanted = jnp.logical_not(_early(offset, tgt_count)) if late else _early(offset, tgt_count)

        @pl.when(wanted)
        def _():
            term = jnp.dot(
                tiles_ref[slot],
                stack_ref[stack_index(offset), :width, :],
                preferred_element_type=jnp.float32,
            )
            acc_ref[target] += term

        return carry

    lax.fori_loop(0, jnp.clip(count_ref[0], 0, slot_count), add_slot, 0)

    for source in range(tgt_count):
        offset = source - own_tgt
        wanted = jnp.logical_not(_early(offset, tgt_count)) if late else _early(offset, tgt_count)

        @pl.when(wanted)
        def _():
            block = stack_ref[stack_index(offset)]
            dens = block[:width, :]
            packed = block[width:, :]
            top = jnp.dot(packed[:, :width], dens, preferred_element_type=jnp.float32)
            bottom = jnp.dot(packed[:, width:], dens, preferred_element_type=jnp.float32)
            projected = jnp.concatenate([top, bottom], axis=0).astype(jnp.bfloat16)
            coeff_ref[...] += jnp.dot(
                masked_ref[source], projected, preferred_element_type=jnp.float32
            )

    if late:
        coeffs = coeff_ref[...].astype(jnp.bfloat16)

        def write(first_ref, second_ref):
            for target in range(inner_count):
                dest = first_ref if target % sub_count == 0 else second_ref
                row = target // sub_count
                dest[row, :width, :] = acc_ref[target].astype(dest.dtype)
                dest[row, width:, :] = coeffs[target * rank_size : (target + 1) * rank_size]

        @pl.when(own_sub == 0)
        def _():
            write(mine_ref, theirs_ref)

        @pl.when(own_sub != 0)
        def _():
            write(theirs_ref, mine_ref)


def _near_far(pairs_flat, count, place, tiles, early_stack, stack, masked_t, inner_count, rank_size):
    slot_count, width, _ = tiles.shape
    stack_count, rows, rhs_count = early_stack.shape
    half_count = inner_count // 2
    out_rows = width + rank_size
    whole = lambda k, p, c, q: (0, 0, 0)
    acc_shape = (inner_count, width, rhs_count)
    coeff_shape = (inner_count * rank_size, rhs_count)
    base_specs = [
        pl.BlockSpec(tiles.shape, whole),
        pl.BlockSpec(early_stack.shape, whole),
        pl.BlockSpec(masked_t.shape, whole),
    ]
    acc_spec = pl.BlockSpec(acc_shape, whole)
    coeff_spec = pl.BlockSpec(coeff_shape, lambda k, p, c, q: (0, 0))
    vmem_bytes = (
        2 * (tiles.size * 2 + early_stack.size * 2 + masked_t.size * 2 + 2 * half_count * out_rows * rhs_count * 2)
        + 6 * (inner_count * width * rhs_count * 4 + inner_count * rank_size * rhs_count * 4)
        + (4 << 20)
    )
    params = pltpu.CompilerParams(dimension_semantics=("arbitrary",), vmem_limit_bytes=int(vmem_bytes))
    acc, coeff = pl.pallas_call(
        lambda *r: _partial_kernel(False, *r),
        grid_spec=pltpu.PrefetchScalarGridSpec(
            num_scalar_prefetch=3, grid=(1,), in_specs=base_specs, out_specs=[acc_spec, coeff_spec]
        ),
        out_shape=[
            jax.ShapeDtypeStruct(acc_shape, jnp.float32),
            jax.ShapeDtypeStruct(coeff_shape, jnp.float32),
        ],
        compiler_params=params,
    )(pairs_flat, count, place, tiles, early_stack, masked_t)
    stack = jnp.stack(lax.optimization_barrier((tuple(stack), acc, coeff))[0])
    late_specs = [base_specs[0], pl.BlockSpec(stack.shape, whole), base_specs[2]]
    out = jax.ShapeDtypeStruct((half_count, out_rows, rhs_count), jnp.bfloat16)
    half_spec = pl.BlockSpec((half_count, out_rows, rhs_count), whole)
    return pl.pallas_call(
        lambda *r: _partial_kernel(True, *r),
        grid_spec=pltpu.PrefetchScalarGridSpec(
            num_scalar_prefetch=3,
            grid=(1,),
            in_specs=late_specs + [acc_spec, coeff_spec],
            out_specs=[half_spec, half_spec],
            scratch_shapes=[pltpu.VMEM(acc_shape, jnp.float32), pltpu.VMEM(coeff_shape, jnp.float32)],
        ),
        out_shape=[out, out],
        compiler_params=params,
    )(pairs_flat, count, place, tiles, stack, masked_t, acc, coeff)


def _epilogue_kernel(me_ref, basis_t_ref, *refs):
    piece_refs, out_ref = refs[:-1], refs[-1]
    width = out_ref.shape[0]
    total = piece_refs[0][...].astype(jnp.float32)
    for piece_ref in piece_refs[1:]:
        total += piece_ref[...].astype(jnp.float32)
    coeffs = total[width:, :].astype(jnp.bfloat16)
    far = jnp.dot(basis_t_ref[...], coeffs, preferred_element_type=jnp.float32)
    out_ref[...] = (total[:width, :] + far).astype(out_ref.dtype)


def _epilogue(me, pieces, basis_t):
    width = basis_t.shape[0]
    cols = pieces[0].shape[-1]
    in_specs = [pl.BlockSpec(basis_t.shape, lambda i, m: (0, 0))]
    for piece in pieces:
        if piece.ndim == 3:
            in_specs.append(pl.BlockSpec((None,) + piece.shape[1:], lambda i, m: (m[0], 0, 0)))
        else:
            in_specs.append(pl.BlockSpec(piece.shape, lambda i, m: (0, 0)))
    grid_spec = pltpu.PrefetchScalarGridSpec(
        num_scalar_prefetch=1,
        grid=(1,),
        in_specs=in_specs,
        out_specs=pl.BlockSpec((width, cols), lambda i, m: (0, 0)),
    )
    return pl.pallas_call(
        _epilogue_kernel,
        grid_spec=grid_spec,
        out_shape=jax.ShapeDtypeStruct((width, cols), jnp.bfloat16),
    )(me, basis_t, *pieces)


def _line_gather(payload, axis):
    n = lax.axis_size(axis)
    if n == 1:
        return payload[None], [payload]
    first_up = lax.ppermute(payload, axis, [(i, (i + 1) % n) for i in range(n)])
    first_down = lax.ppermute(payload, axis, [(i, (i - 1) % n) for i in range(n)])
    ups, downs = [first_up], [first_down]
    up, down = first_up, first_down
    for step in range(1, n - 2):
        up_pairs = [(i, i + 1) for i in range(step, n - 1)]
        down_pairs = [(i + 1, i) for i in range(n - 1 - step)]
        up = lax.ppermute(up, axis, up_pairs)
        down = lax.ppermute(down, axis, down_pairs)
        ups.append(up)
        downs.append(down)
    if n > 2:
        ups.append(first_down)
        downs.append(first_up)
    early_ups = [first_up] * (len(ups) - 1) + [first_down]
    early_downs = [first_down] * (len(downs) - 1) + [first_up]
    if n <= 2:
        early_ups, early_downs = [first_up], [first_down]
    late = ups[1:-1][::-1] + downs[1:-1] if n > 3 else [payload]
    return jnp.stack(early_ups[::-1] + [payload] + early_downs), late


def _ring_reduce_scatter(blocks, axis):
    n = lax.axis_size(axis)
    if n == 1:
        return blocks[0]
    me = lax.axis_index(axis)
    ring = [(i, (i + 1) % n) for i in range(n)]
    carry = lax.dynamic_index_in_dim(blocks, jnp.mod(me - 1, n), 0, False)
    for step in range(n - 1):
        arrived = lax.ppermute(carry.astype(jnp.bfloat16), axis, ring)
        own = lax.dynamic_index_in_dim(blocks, jnp.mod(me - 2 - step, n), 0, False)
        carry = arrived.astype(jnp.float32) + own
    return carry


def on_device(density, cluster_basis, near_blocks, near_pairs, near_count, coupling):
    width = cluster_basis.shape[2]
    rank_size = cluster_basis.shape[1]
    rhs_count = density.shape[1]
    tgt_count = lax.axis_size("tgt")
    inner_count = lax.axis_size(("inner", "sub"))
    assert lax.axis_size("sub") == 2 and 2 * width == rhs_count and rank_size % 2 == 0
    basis = cluster_basis[0]
    half_rank = rank_size // 2
    packed = jnp.concatenate([basis[:half_rank], basis[half_rank:]], axis=1)
    payload = jnp.concatenate([density, packed], axis=0)
    early_stack, stack = _line_gather(payload, "tgt")

    pair_list = near_pairs[0, 0]
    live_count = near_count[0, 0]
    slot_count = pair_list.shape[0]
    flat_pairs = pair_list[:, 0] * tgt_count + pair_list[:, 1]
    live_slots = jnp.arange(slot_count) < live_count
    hit_table = (flat_pairs[:, None] == jnp.arange(inner_count * tgt_count)[None, :]) & live_slots[
        :, None
    ]
    keep_mask = (
        (1.0 - jnp.any(hit_table, axis=0).astype(jnp.float32))
        .reshape(inner_count, 1, tgt_count, 1)
        .astype(jnp.bfloat16)
    )
    masked = coupling[0, 0].reshape(inner_count, rank_size, tgt_count, rank_size) * keep_mask
    masked_t = masked.transpose(2, 0, 1, 3).reshape(tgt_count, inner_count * rank_size, rank_size)

    place = jnp.stack([lax.axis_index("tgt"), lax.axis_index("sub")]).astype(jnp.int32)
    mine, theirs = _near_far(
        pair_list.reshape(-1), live_count.reshape(1), place, near_blocks[0, 0], early_stack, stack, masked_t,
        inner_count, rank_size,
    )
    basis_t = cluster_basis[0].T
    me = lax.axis_index("inner")
    swap = [(0, 1), (1, 0)]
    if lax.axis_size("inner") == 2:
        onward = lax.ppermute(lax.dynamic_index_in_dim(theirs, 1 - me, 0, False), "sub", swap)
        send = (
            lax.dynamic_index_in_dim(mine, 1 - me, 0, False).astype(jnp.float32)
            + onward.astype(jnp.float32)
        ).astype(jnp.bfloat16)
        back = lax.ppermute(send, "inner", swap)
        keep_src = lax.optimization_barrier((lax.dynamic_index_in_dim(theirs, me, 0, False), send))[0]
        kept = lax.ppermute(keep_src, "sub", swap)
        pieces = (mine, kept, back)
    else:
        arrived = lax.ppermute(theirs, "sub", swap)
        stage = mine.astype(jnp.float32) + arrived.astype(jnp.float32)
        pieces = (_ring_reduce_scatter(stage, "inner"),)
    width = basis_t.shape[0]
    total = None
    for piece in pieces:
        if piece.ndim == 3:
            piece = lax.dynamic_index_in_dim(piece, me, 0, False)
        piece = piece.astype(jnp.float32)
        total = piece if total is None else total + piece
    far = jnp.dot(basis_t, total[width:].astype(jnp.bfloat16), preferred_element_type=jnp.float32)
    return (total[:width] + far).astype(jnp.bfloat16)


def solution(mesh):
    in_specs = (
        P(("tgt", "inner", "sub"), "groups"),
        P(("groups", "tgt", "inner", "sub"), None, None),
        P(("groups", "tgt"), ("inner", "sub"), None, None, None),
        P(("groups", "tgt"), ("inner", "sub"), None, None),
        P(("groups", "tgt"), ("inner", "sub")),
        P(("groups", "tgt"), ("inner", "sub"), None, None),
    )
    out_specs = P(("tgt", "inner", "sub"), "groups")
    return jax.shard_map(
        on_device, mesh=mesh, in_specs=in_specs, out_specs=out_specs, check_vma=False
    )
```

```python
import jax
import jax.numpy as jnp
from jax import lax
from jax.experimental import pallas as pl
from jax.experimental.pallas import tpu as pltpu
from jax.sharding import PartitionSpec as P


def _early(offset, tgt_count):
    return (offset == 0) | (jnp.abs(offset) == 1) | (jnp.abs(offset) == tgt_count - 1)


def _partial_kernel(late, pairs_ref, count_ref, place_ref, tiles_ref, stack_ref, masked_ref, *refs):
    inner_count, width, rhs_count = tiles_ref.shape[1], tiles_ref.shape[1], stack_ref.shape[2]
    slot_count = tiles_ref.shape[0]
    tgt_count = masked_ref.shape[0]
    rank_size = masked_ref.shape[2]
    sub_count = 2
    own_tgt = place_ref[0]
    own_sub = place_ref[1]
    stack_count = stack_ref.shape[0]

    def stack_index(offset):
        if not late:
            return offset + tgt_count - 1
        place = jnp.where(offset < 0, tgt_count - 2 + offset, offset + tgt_count - 5)
        return jnp.clip(place, 0, stack_count - 1)

    if late:
        acc_ref, coeff_ref, mine_ref, theirs_ref = refs
        inner_count = acc_ref.shape[0]
    else:
        acc_ref, coeff_ref = refs
        inner_count = acc_ref.shape[0]
        acc_ref[...] = jnp.zeros_like(acc_ref)
        coeff_ref[...] = jnp.zeros_like(coeff_ref)

    def add_slot(slot, carry):
        target = jnp.clip(pairs_ref[2 * slot], 0, inner_count - 1)
        source = jnp.clip(pairs_ref[2 * slot + 1], 0, tgt_count - 1)
        offset = source - own_tgt
        wanted = jnp.logical_not(_early(offset, tgt_count)) if late else _early(offset, tgt_count)

        @pl.when(wanted)
        def _():
            term = jnp.dot(
                tiles_ref[slot],
                stack_ref[stack_index(offset), :width, :],
                preferred_element_type=jnp.float32,
            )
            acc_ref[target] += term

        return carry

    lax.fori_loop(0, jnp.clip(count_ref[0], 0, slot_count), add_slot, 0)

    for source in range(tgt_count):
        offset = source - own_tgt
        wanted = jnp.logical_not(_early(offset, tgt_count)) if late else _early(offset, tgt_count)

        @pl.when(wanted)
        def _():
            block = stack_ref[stack_index(offset)]
            dens = block[:width, :]
            packed = block[width:, :]
            top = jnp.dot(packed[:, :width], dens, preferred_element_type=jnp.float32)
            bottom = jnp.dot(packed[:, width:], dens, preferred_element_type=jnp.float32)
            projected = jnp.concatenate([top, bottom], axis=0).astype(jnp.bfloat16)
            coeff_ref[...] += jnp.dot(
                masked_ref[source], projected, preferred_element_type=jnp.float32
            )

    if late:
        coeffs = coeff_ref[...].astype(jnp.bfloat16)

        def write(first_ref, second_ref):
            for target in range(inner_count):
                dest = first_ref if target % sub_count == 0 else second_ref
                row = target // sub_count
                dest[row, :width, :] = acc_ref[target].astype(dest.dtype)
                dest[row, width:, :] = coeffs[target * rank_size : (target + 1) * rank_size]

        @pl.when(own_sub == 0)
        def _():
            write(mine_ref, theirs_ref)

        @pl.when(own_sub != 0)
        def _():
            write(theirs_ref, mine_ref)


def _near_far(pairs_flat, count, place, tiles, early_stack, stack, masked_t, inner_count, rank_size):
    slot_count, width, _ = tiles.shape
    stack_count, rows, rhs_count = early_stack.shape
    half_count = inner_count // 2
    out_rows = width + rank_size
    whole = lambda k, p, c, q: (0, 0, 0)
    acc_shape = (inner_count, width, rhs_count)
    coeff_shape = (inner_count * rank_size, rhs_count)
    base_specs = [
        pl.BlockSpec(tiles.shape, whole),
        pl.BlockSpec(early_stack.shape, whole),
        pl.BlockSpec(masked_t.shape, whole),
    ]
    acc_spec = pl.BlockSpec(acc_shape, whole)
    coeff_spec = pl.BlockSpec(coeff_shape, lambda k, p, c, q: (0, 0))
    vmem_bytes = (
        2 * (tiles.size * 2 + early_stack.size * 2 + masked_t.size * 2 + 2 * half_count * out_rows * rhs_count * 2)
        + 6 * (inner_count * width * rhs_count * 4 + inner_count * rank_size * rhs_count * 4)
        + (4 << 20)
    )
    params = pltpu.CompilerParams(dimension_semantics=("arbitrary",), vmem_limit_bytes=int(vmem_bytes))
    acc, coeff = pl.pallas_call(
        lambda *r: _partial_kernel(False, *r),
        grid_spec=pltpu.PrefetchScalarGridSpec(
            num_scalar_prefetch=3, grid=(1,), in_specs=base_specs, out_specs=[acc_spec, coeff_spec]
        ),
        out_shape=[
            jax.ShapeDtypeStruct(acc_shape, jnp.float32),
            jax.ShapeDtypeStruct(coeff_shape, jnp.float32),
        ],
        compiler_params=params,
    )(pairs_flat, count, place, tiles, early_stack, masked_t)
    stack = jnp.stack(lax.optimization_barrier((tuple(stack), acc, coeff))[0])
    late_specs = [base_specs[0], pl.BlockSpec(stack.shape, whole), base_specs[2]]
    out = jax.ShapeDtypeStruct((half_count, out_rows, rhs_count), jnp.bfloat16)
    half_spec = pl.BlockSpec((half_count, out_rows, rhs_count), whole)
    return pl.pallas_call(
        lambda *r: _partial_kernel(True, *r),
        grid_spec=pltpu.PrefetchScalarGridSpec(
            num_scalar_prefetch=3,
            grid=(1,),
            in_specs=late_specs + [acc_spec, coeff_spec],
            out_specs=[half_spec, half_spec],
        ),
        out_shape=[out, out],
        compiler_params=params,
    )(pairs_flat, count, place, tiles, stack, masked_t, acc, coeff)


def _epilogue_kernel(me_ref, basis_t_ref, *refs):
    piece_refs, out_ref = refs[:-1], refs[-1]
    width = out_ref.shape[0]
    total = piece_refs[0][...].astype(jnp.float32)
    for piece_ref in piece_refs[1:]:
        total += piece_ref[...].astype(jnp.float32)
    coeffs = total[width:, :].astype(jnp.bfloat16)
    far = jnp.dot(basis_t_ref[...], coeffs, preferred_element_type=jnp.float32)
    out_ref[...] = (total[:width, :] + far).astype(out_ref.dtype)


def _epilogue(me, pieces, basis_t):
    width = basis_t.shape[0]
    cols = pieces[0].shape[-1]
    in_specs = [pl.BlockSpec(basis_t.shape, lambda i, m: (0, 0))]
    for piece in pieces:
        if piece.ndim == 3:
            in_specs.append(pl.BlockSpec((None,) + piece.shape[1:], lambda i, m: (m[0], 0, 0)))
        else:
            in_specs.append(pl.BlockSpec(piece.shape, lambda i, m: (0, 0)))
    grid_spec = pltpu.PrefetchScalarGridSpec(
        num_scalar_prefetch=1,
        grid=(1,),
        in_specs=in_specs,
        out_specs=pl.BlockSpec((width, cols), lambda i, m: (0, 0)),
    )
    return pl.pallas_call(
        _epilogue_kernel,
        grid_spec=grid_spec,
        out_shape=jax.ShapeDtypeStruct((width, cols), jnp.bfloat16),
    )(me, basis_t, *pieces)


def _line_gather(payload, axis):
    n = lax.axis_size(axis)
    if n == 1:
        return payload[None], [payload]
    first_up = lax.ppermute(payload, axis, [(i, (i + 1) % n) for i in range(n)])
    first_down = lax.ppermute(payload, axis, [(i, (i - 1) % n) for i in range(n)])
    ups, downs = [first_up], [first_down]
    up, down = first_up, first_down
    for step in range(1, n - 2):
        up_pairs = [(i, i + 1) for i in range(step, n - 1)]
        down_pairs = [(i + 1, i) for i in range(n - 1 - step)]
        up = lax.ppermute(up, axis, up_pairs)
        down = lax.ppermute(down, axis, down_pairs)
        ups.append(up)
        downs.append(down)
    if n > 2:
        ups.append(first_down)
        downs.append(first_up)
    early_ups = [first_up] * (len(ups) - 1) + [first_down]
    early_downs = [first_down] * (len(downs) - 1) + [first_up]
    if n <= 2:
        early_ups, early_downs = [first_up], [first_down]
    late = ups[1:-1][::-1] + downs[1:-1] if n > 3 else [payload]
    return jnp.stack(early_ups[::-1] + [payload] + early_downs), late


def _ring_reduce_scatter(blocks, axis):
    n = lax.axis_size(axis)
    if n == 1:
        return blocks[0]
    me = lax.axis_index(axis)
    ring = [(i, (i + 1) % n) for i in range(n)]
    carry = lax.dynamic_index_in_dim(blocks, jnp.mod(me - 1, n), 0, False)
    for step in range(n - 1):
        arrived = lax.ppermute(carry.astype(jnp.bfloat16), axis, ring)
        own = lax.dynamic_index_in_dim(blocks, jnp.mod(me - 2 - step, n), 0, False)
        carry = arrived.astype(jnp.float32) + own
    return carry


def on_device(density, cluster_basis, near_blocks, near_pairs, near_count, coupling):
    width = cluster_basis.shape[2]
    rank_size = cluster_basis.shape[1]
    rhs_count = density.shape[1]
    tgt_count = lax.axis_size("tgt")
    inner_count = lax.axis_size(("inner", "sub"))
    assert lax.axis_size("sub") == 2 and 2 * width == rhs_count and rank_size % 2 == 0
    basis = cluster_basis[0]
    half_rank = rank_size // 2
    packed = jnp.concatenate([basis[:half_rank], basis[half_rank:]], axis=1)
    payload = jnp.concatenate([density, packed], axis=0)
    early_stack, stack = _line_gather(payload, "tgt")

    pair_list = near_pairs[0, 0]
    live_count = near_count[0, 0]
    slot_count = pair_list.shape[0]
    flat_pairs = pair_list[:, 0] * tgt_count + pair_list[:, 1]
    live_slots = jnp.arange(slot_count) < live_count
    hit_table = (flat_pairs[:, None] == jnp.arange(inner_count * tgt_count)[None, :]) & live_slots[
        :, None
    ]
    keep_mask = (
        (1.0 - jnp.any(hit_table, axis=0).astype(jnp.float32))
        .reshape(inner_count, 1, tgt_count, 1)
        .astype(jnp.bfloat16)
    )
    masked = coupling[0, 0].reshape(inner_count, rank_size, tgt_count, rank_size) * keep_mask
    masked_t = masked.transpose(2, 0, 1, 3).reshape(tgt_count, inner_count * rank_size, rank_size)

    place = jnp.stack([lax.axis_index("tgt"), lax.axis_index("sub")]).astype(jnp.int32)
    mine, theirs = _near_far(
        pair_list.reshape(-1), live_count.reshape(1), place, near_blocks[0, 0], early_stack, stack, masked_t,
        inner_count, rank_size,
    )
    basis_t = cluster_basis[0].T
    me = lax.axis_index("inner")
    swap = [(0, 1), (1, 0)]
    if lax.axis_size("inner") == 2:
        onward = lax.ppermute(lax.dynamic_index_in_dim(theirs, 1 - me, 0, False), "sub", swap)
        send = (
            lax.dynamic_index_in_dim(mine, 1 - me, 0, False).astype(jnp.float32)
            + onward.astype(jnp.float32)
        ).astype(jnp.bfloat16)
        back = lax.ppermute(send, "inner", swap)
        keep_src = lax.optimization_barrier((lax.dynamic_index_in_dim(theirs, me, 0, False), send))[0]
        kept = lax.ppermute(keep_src, "sub", swap)
        pieces = (mine, kept, back)
    else:
        arrived = lax.ppermute(theirs, "sub", swap)
        stage = mine.astype(jnp.float32) + arrived.astype(jnp.float32)
        pieces = (_ring_reduce_scatter(stage, "inner"),)
    width = basis_t.shape[0]
    total = None
    for piece in pieces:
        if piece.ndim == 3:
            piece = lax.dynamic_index_in_dim(piece, me, 0, False)
        piece = piece.astype(jnp.float32)
        total = piece if total is None else total + piece
    far = jnp.dot(basis_t, total[width:].astype(jnp.bfloat16), preferred_element_type=jnp.float32)
    return (total[:width] + far).astype(jnp.bfloat16)


def solution(mesh):
    in_specs = (
        P(("tgt", "inner", "sub"), "groups"),
        P(("groups", "tgt", "inner", "sub"), None, None),
        P(("groups", "tgt"), ("inner", "sub"), None, None, None),
        P(("groups", "tgt"), ("inner", "sub"), None, None),
        P(("groups", "tgt"), ("inner", "sub")),
        P(("groups", "tgt"), ("inner", "sub"), None, None),
    )
    out_specs = P(("tgt", "inner", "sub"), "groups")
    return jax.shard_map(
        on_device, mesh=mesh, in_specs=in_specs, out_specs=out_specs, check_vma=False
    )
```
